32 devices in a mesh: seq: 16 (over z, x, core), head: 2 (over y).
Axes of the slice: x: 2, y: 2, z: 4, core: 2. Of those that a mesh axis runs over, the one named last changes fastest.
Arguments:
- queries: bfloat16 [4096, 4096], P('seq', 'head'), may hold values from -6 to 6
- keys: bfloat16 [4096, 4096], P('seq', 'head'), may hold values from -6 to 6
- values: bfloat16 [4096, 4096], P('seq', 'head'), may hold values from -6 to 6
- out_weight: bfloat16 [4096, 4096], P('head'), may hold values from -0.09375 to 0.09375
- cotangent: bfloat16 [4096, 4096], P(('seq', 'head')), may hold values from -6 to 6
- offsets: int32 [16, 32], P('head'), may hold values from 0 to 127, as said below
Outputs:
- attention: bfloat16 [4096, 4096], P('seq', 'head')
- query_grad: bfloat16 [4096, 4096], P('seq', 'head')
- key_grad: bfloat16 [4096, 4096], P('seq', 'head')
- value_grad: bfloat16 [4096, 4096], P('seq', 'head')
The draws below stay inside these ranges and needn't reach their ends.
Inputs may be any that keep to these rules, and one draw needn't show every extreme that they name: Each row holds 32 distinct offsets in rising order, the last one 128 - 1.
All inputs are finite; a program needn't handle non-finite values.
Results may differ from the reference program's by a relative error of at most 0.011.
Values may be sent and summed in bfloat16 or wider, within the bound.
No kernel may reach another device: no remote copies, remote signals or barrier semaphores. Data moves between devices by JAX's collectives and lax.ppermute only.
A program may use at most 128 MiB of HBM per device.

```python
import math
import jax
import jax.numpy as jnp
from jax import lax

D = 4096
HEADS = 32
HD = 128
WIN = 256
BLOCK = 128
SUMM = 32
SEQ = 4096


def draw_queries(key, part):
    drawn = 1.4 * jax.random.normal(jax.random.fold_in(key, 1), (SEQ, HEADS * HD), jnp.float32)
    return jnp.clip(drawn, -6.0, 6.0).astype(jnp.bfloat16)


def draw_keys(key, part):
    drawn = 1.4 * jax.random.normal(jax.random.fold_in(key, 3), (SEQ, HEADS * HD), jnp.float32)
    return jnp.clip(drawn, -6.0, 6.0).astype(jnp.bfloat16)


def draw_offsets(key, part):
    row_keys = jax.random.split(key, HEADS // 2)

    def one_row(row_key):
        picked = jax.random.permutation(row_key, BLOCK - 1)[:SUMM - 1].astype(jnp.int32)
        joined = jnp.concatenate([picked, jnp.full((1,), BLOCK - 1, jnp.int32)])
        return jnp.sort(joined).astype(jnp.int32)
    return jax.vmap(one_row)(row_keys)


def block_scale(rng, shape, cuts, least, high):
    def one(axis_at, blocks):
        steps = jax.random.uniform(jax.random.fold_in(jax.random.fold_in(rng, 6), axis_at), (blocks,), jnp.float32, least / len(cuts), high / len(cuts))
        return jnp.repeat(jnp.exp(steps), shape[axis_at] // blocks).reshape((-1,) + (1,) * (len(shape) - axis_at - 1))

    level = one(*cuts[0])
    for cut in cuts[1:]:
        level = level * one(*cut)
    return level


def normal_values(key, dims, scale, limit, shards=(), held_as=jnp.bfloat16):
    gain = block_scale(key, dims, shards, -0.22, 0.18) if shards else 1.0
    values = jax.random.normal(key, dims, jnp.float32) * scale * gain
    return jnp.minimum(jnp.maximum(values, -limit), limit).astype(held_as)


def setup_inputs(seed: int = 0) -> dict:
    splits = jax.random.split(jax.random.key(seed), 7)
    return {
        "queries": draw_queries(jax.random.fold_in(splits[6], 71), 0),
        "keys": draw_keys(jax.random.fold_in(splits[6], 71), 0),
        "values": normal_values(splits[2], (SEQ, HEADS * HD), 1.0, 6.0, ((0, 16), (1, 2))),
        "out_weight": normal_values(splits[3], (HEADS * HD, D), (HEADS * HD) ** -0.5, 0.09375, ((0, 2),)),
        "cotangent": normal_values(splits[4], (SEQ, D), 1.0, 6.0, ((0, 32),)),
        "offsets": draw_offsets(jax.random.fold_in(splits[6], 71), 0),
    }


NEG = -1.0e30


def matmul(left, right):
    return jnp.dot(left, right, preferred_element_type=jnp.float32)


def band_head(inputs):
    query_rows, key_rows, value_rows, grad_rows = inputs
    score_scale = HD ** -0.5
    block_rows = math.gcd(512, SEQ)
    padding = jnp.zeros((WIN, HD), key_rows.dtype)
    key_padded = jnp.concatenate([padding, key_rows], 0)
    value_padded = jnp.concatenate([padding, value_rows], 0)

    def advance(carried, number):
        key_acc, value_acc = carried
        row_start = number * block_rows
        query_block = lax.dynamic_slice_in_dim(query_rows, row_start, block_rows, 0)
        grad_block = lax.dynamic_slice_in_dim(grad_rows, row_start, block_rows, 0)
        key_block = lax.dynamic_slice_in_dim(key_padded, row_start, block_rows + WIN, 0)
        value_block = lax.dynamic_slice_in_dim(value_padded, row_start, block_rows + WIN, 0)
        query_pos = row_start + jnp.arange(block_rows, dtype=jnp.int32)
        key_pos = row_start - WIN + jnp.arange(block_rows + WIN, dtype=jnp.int32)
        distance = query_pos[:, None] - key_pos[None, :]
        visible = (distance >= 0) & (distance < WIN) & (key_pos[None, :] >= 0)
        scores = jnp.where(visible, matmul(query_block, key_block.T) * score_scale, NEG)
        row_max = scores.max(-1)
        weights = jnp.exp(scores - row_max[:, None])
        row_sum = weights.sum(-1)
        result = (matmul(weights.astype(jnp.bfloat16), value_block) / row_sum[:, None]).astype(jnp.bfloat16)
        log_total = row_max + jnp.log(row_sum)
        row_delta = jnp.sum(grad_block.astype(jnp.float32) * result.astype(jnp.float32), -1)
        prob_rows = jnp.exp(scores - log_total[:, None])
        grad_prob = matmul(grad_block, value_block.T)
        grad_score = (prob_rows * (grad_prob - row_delta[:, None])).astype(jnp.bfloat16)
        query_change = (matmul(grad_score, key_block) * score_scale).astype(jnp.bfloat16)
        key_part = matmul(grad_score.T, query_block) * score_scale
        value_part = matmul(prob_rows.astype(jnp.bfloat16).T, grad_block)
        key_acc = lax.dynamic_update_slice_in_dim(
            key_acc, lax.dynamic_slice_in_dim(key_acc, row_start, block_rows + WIN, 0) + key_part, row_start, 0)
        value_acc = lax.dynamic_update_slice_in_dim(
            value_acc, lax.dynamic_slice_in_dim(value_acc, row_start, block_rows + WIN, 0) + value_part, row_start, 0)
        return (key_acc, value_acc), (result, query_change)

    zero_grads = jnp.zeros((SEQ + WIN, HD), jnp.float32)
    carried, outputs = lax.scan(advance, (zero_grads, zero_grads), jnp.arange(SEQ // block_rows, dtype=jnp.int32))
    return (outputs[0].reshape(SEQ, HD), outputs[1].reshape(SEQ, HD),
            carried[0][WIN:].astype(jnp.bfloat16), carried[1][WIN:].astype(jnp.bfloat16))


def fixed_head(inputs):
    query_rows, key_rows, value_rows, grad_rows, offset_row = inputs
    score_scale = HD ** -0.5
    block_rows = math.gcd(512, SEQ)
    blocks = SEQ // BLOCK
    summary_rows = ((jnp.arange(blocks, dtype=jnp.int32) * BLOCK)[:, None] + offset_row[None, :]).reshape(-1)
    far_keys = key_rows[summary_rows]
    far_values = value_rows[summary_rows]
    far_block = jnp.arange(blocks * SUMM, dtype=jnp.int32) // SUMM

    def advance(carried, number):
        key_acc, value_acc = carried
        row_start = number * block_rows
        query_block = lax.dynamic_slice_in_dim(query_rows, row_start, block_rows, 0)
        grad_block = lax.dynamic_slice_in_dim(grad_rows, row_start, block_rows, 0)
        key_block = lax.dynamic_slice_in_dim(key_rows, row_start, block_rows, 0)
        value_block = lax.dynamic_slice_in_dim(value_rows, row_start, block_rows, 0)
        query_pos = row_start + jnp.arange(block_rows, dtype=jnp.int32)
        block_ids = query_pos // BLOCK
        own_visible = (block_ids[:, None] == block_ids[None, :]) & (query_pos[None, :] <= query_pos[:, None])
        far_visible = far_block[None, :] < block_ids[:, None]
        own_scores = jnp.where(own_visible, matmul(query_block, key_block.T) * score_scale, NEG)
        far_scores = jnp.where(far_visible, matmul(query_block, far_keys.T) * score_scale, NEG)
        row_max = jnp.maximum(own_scores.max(-1), far_scores.max(-1))
        own_weights = jnp.exp(own_scores - row_max[:, None])
        far_weights = jnp.exp(far_scores - row_max[:, None])
        row_sum = own_weights.sum(-1) + far_weights.sum(-1)
        mixed = matmul(own_weights.astype(jnp.bfloat16), value_block) + matmul(far_weights.astype(jnp.bfloat16), far_values)
        result = (mixed / row_sum[:, None]).astype(jnp.bfloat16)
        log_total = row_max + jnp.log(row_sum)
        row_delta = jnp.sum(grad_block.astype(jnp.float32) * result.astype(jnp.float32), -1)
        own_probs = jnp.exp(own_scores - log_total[:, None])
        far_probs = jnp.exp(far_scores - log_total[:, None])
        own_gscore = (own_probs * (matmul(grad_block, value_block.T) - row_delta[:, None])).astype(jnp.bfloat16)
        far_gscore = (far_probs * (matmul(grad_block, far_values.T) - row_delta[:, None])).astype(jnp.bfloat16)
        query_change = ((matmul(own_gscore, key_block) + matmul(far_gscore, far_keys)) * score_scale).astype(jnp.bfloat16)
        own_kpart = matmul(own_gscore.T, query_block) * score_scale
        own_vpart = matmul(own_probs.astype(jnp.bfloat16).T, grad_block)
        key_acc = key_acc + matmul(far_gscore.T, query_block) * score_scale
        value_acc = value_acc + matmul(far_probs.astype(jnp.bfloat16).T, grad_block)
        return (key_acc, value_acc), (result, query_change, own_kpart, own_vpart)

    zero_grads = jnp.zeros((blocks * SUMM, HD), jnp.float32)
    carried, outputs = lax.scan(advance, (zero_grads, zero_grads), jnp.arange(SEQ // block_rows, dtype=jnp.int32))
    key_total = outputs[2].reshape(SEQ, HD).at[summary_rows].add(carried[0])
    value_total = outputs[3].reshape(SEQ, HD).at[summary_rows].add(carried[1])
    return (outputs[0].reshape(SEQ, HD), outputs[1].reshape(SEQ, HD),
            key_total.astype(jnp.bfloat16), value_total.astype(jnp.bfloat16))


def reference(queries, keys, values, out_weight, cotangent, offsets):
    grad_out = matmul(cotangent, out_weight.T).astype(jnp.bfloat16)
    head_pairs = HEADS // 2

    def split_heads(array):
        return array.reshape(SEQ, head_pairs, 2, HD).transpose(2, 1, 0, 3)

    split_q = split_heads(queries)
    split_k = split_heads(keys)
    split_v = split_heads(values)
    split_g = split_heads(grad_out)
    banded = lax.map(band_head, (split_q[0], split_k[0], split_v[0], split_g[0]))
    fixed = lax.map(fixed_head, (split_q[1], split_k[1], split_v[1], split_g[1], offsets))

    def join_heads(band_part, fixed_part):
        return jnp.stack([band_part, fixed_part], 0).transpose(2, 1, 0, 3).reshape(SEQ, HEADS * HD)

    return (join_heads(banded[0], fixed[0]), join_heads(banded[1], fixed[1]),
            join_heads(banded[2], fixed[2]), join_heads(banded[3], fixed[3]))
```

```python
import jax
import jax.numpy as jnp
from jax import lax
from jax.sharding import PartitionSpec as P

WIN = 256
BLOCK = 128
SUMM = 32


NEG = -1e30


def passed_along(value, axis, steps):
    count = lax.axis_size(axis)
    first, last = (max(0, -steps), min(count, count - steps))
    return lax.ppermute(value, axis, [(source, source + steps) for source in range(first, last)])


def head_scores(left, right, factor):
    return jnp.einsum("qhc,khc->hqk", left, right, preferred_element_type=jnp.float32) * factor


def apply_rows(weights, right):
    return jnp.einsum("hqk,khc->hqc", weights, right, preferred_element_type=jnp.float32)


def apply_cols(weights, left):
    return jnp.einsum("hqk,qhc->khc", weights, left, preferred_element_type=jnp.float32)


def piece_length(total_rows):
    turn_count = max(1, min(8, total_rows // 512))
    while total_rows % turn_count:
        turn_count -= 1
    return total_rows // turn_count


def keep_state(carried):
    return carried


def on_device(queries, keys, values, out_weight, cotangent, offsets):
    seq_rows = queries.shape[0]
    full_width = queries.shape[1]
    head_pairs = offsets.shape[0]
    head_dim = full_width // (2 * head_pairs)
    score_scale = head_dim ** (-0.5)
    block_rows = min(512, seq_rows)
    seq_index = lax.axis_index("seq")
    start_pos = seq_index * seq_rows
    positions = start_pos + jnp.arange(seq_rows, dtype=jnp.int32)
    block_ids = positions // BLOCK
    split_q = queries.reshape(seq_rows, head_pairs, 2, head_dim)
    split_k = keys.reshape(seq_rows, head_pairs, 2, head_dim)
    split_v = values.reshape(seq_rows, head_pairs, 2, head_dim)
    band_q, fixed_q = (split_q[:, :, 0], split_q[:, :, 1])
    band_k, fixed_k = (split_k[:, :, 0], split_k[:, :, 1])
    band_v, fixed_v = (split_v[:, :, 0], split_v[:, :, 1])
    prev_k, prev_v = passed_along((band_k, band_v), "seq", 1)
    ext_k = jnp.concatenate([prev_k, band_k], 0)
    ext_v = jnp.concatenate([prev_v, band_v], 0)
    ext_pos = start_pos - WIN + jnp.arange(seq_rows + WIN, dtype=jnp.int32)

    def band_scores():
        distance = positions[:, None] - ext_pos[None, :]
        visible = (distance >= 0) & (distance < WIN) & (ext_pos[None, :] >= 0)
        scores = head_scores(band_q, ext_k, score_scale)
        return jnp.where(visible[None], scores, NEG)

    def own_scores():
        same_block = positions[:, None] // BLOCK == positions[None, :] // BLOCK
        visible = same_block & (positions[None, :] <= positions[:, None])
        scores = head_scores(fixed_q, fixed_k, score_scale)
        return jnp.where(visible[None], scores, NEG)

    band_out = []
    band_lse = []
    number = 0
    row_start = number * block_rows
    scores = band_scores()
    row_max = scores.max(-1)
    weights = jnp.exp(scores - row_max[..., None])
    row_sum = weights.sum(-1)
    band_out.append(apply_rows(weights.astype(jnp.bfloat16), ext_v) / row_sum[..., None])
    band_lse.append(row_max + jnp.log(row_sum))
    scores = own_scores()
    row_max = scores.max(-1)
    weights = jnp.exp(scores - row_max[..., None])
    fixed_max = row_max
    fixed_sum = weights.sum(-1)
    fixed_acc = apply_rows(weights.astype(jnp.bfloat16), fixed_v)
    band_out = band_out[0]
    band_lse = band_lse[0]
    running = (fixed_max, fixed_sum, fixed_acc)
    digest_count = seq_rows // BLOCK * SUMM
    offset_table = jnp.tile(offsets.T, (seq_rows // BLOCK, 1))
    digest_rows = (jnp.arange(digest_count, dtype=jnp.int32) // SUMM * BLOCK)[
        :, None
    ] + offset_table
    select = (
        digest_rows.T[:, :, None] == jnp.arange(seq_rows, dtype=jnp.int32)[None, None, :]
    ).astype(jnp.bfloat16)
    digest_k = jnp.einsum(
        "hjr,rhc->jhc", select, fixed_k, preferred_element_type=jnp.float32
    ).astype(jnp.bfloat16)
    digest_v = jnp.einsum(
        "hjr,rhc->jhc", select, fixed_v, preferred_element_type=jnp.float32
    ).astype(jnp.bfloat16)
    pair_width = head_pairs * head_dim
    far_kv = lax.all_gather(
        jnp.concatenate(
            [
                digest_k.reshape(digest_count, pair_width),
                digest_v.reshape(digest_count, pair_width),
            ],
            1,
        ),
        "seq",
        axis=0,
        tiled=True,
    )
    far_k, far_v = far_kv[:, :pair_width], far_kv[:, pair_width:]
    far_count = far_k.shape[0]
    piece_rows = piece_length(far_count)
    own_end = (seq_index + 1) * digest_count

    def far_piece(row_start):
        key_piece = far_k[row_start : row_start + piece_rows].reshape(
            piece_rows, head_pairs, head_dim
        )
        value_piece = far_v[row_start : row_start + piece_rows].reshape(
            piece_rows, head_pairs, head_dim
        )
        key_block = (row_start + jnp.arange(piece_rows, dtype=jnp.int32)) // SUMM
        visible = key_block[None, :] < block_ids[:, None]
        scores = jnp.where(visible[None], head_scores(fixed_q, key_piece, score_scale), NEG)
        return (scores, key_piece, value_piece)

    for row_start in range(0, far_count, piece_rows):

        def visit_piece(carried, row_start=row_start):
            row_max, row_sum, weighted = carried
            scores, key_piece, value_piece = far_piece(row_start)
            new_max = jnp.maximum(row_max, scores.max(-1))
            rescale = jnp.exp(row_max - new_max)
            weights = jnp.exp(scores - new_max[..., None])
            return (
                new_max,
                row_sum * rescale + weights.sum(-1),
                weighted * rescale[..., None]
                + apply_rows(weights.astype(jnp.bfloat16), value_piece),
            )

        running = lax.cond(row_start < own_end, visit_piece, keep_state, running)
    fixed_out = running[2] / running[1][..., None]
    fixed_lse = running[0] + jnp.log(running[1])
    attention = jnp.stack([band_out.transpose(1, 0, 2), fixed_out.transpose(1, 0, 2)], 2)
    attention = attention.reshape(seq_rows, full_width).astype(jnp.bfloat16)
    head_count = lax.axis_size("head")
    head_index = lax.axis_index("head")
    pieces = [cotangent] + [
        lax.ppermute(
            cotangent, "head", [(source, (source + shift) % head_count) for source in range(head_count)]
        )
        for shift in range(1, head_count)
    ]
    piece_grads = [
        lax.dot_general(
            piece, out_weight, (((1,), (1,)), ((), ())), preferred_element_type=jnp.float32
        ).astype(jnp.bfloat16)
        for piece in pieces
    ]
    doubled = jnp.stack(piece_grads[::-1] + piece_grads[::-1], 0)
    grad_out = lax.dynamic_slice_in_dim(doubled, head_count - 1 - head_index, head_count, 0)
    grad_out = grad_out.reshape(seq_rows, full_width)
    row_delta = jnp.sum(
        grad_out.astype(jnp.float32).reshape(seq_rows, head_pairs, 2, head_dim)
        * attention.astype(jnp.float32).reshape(seq_rows, head_pairs, 2, head_dim),
        -1,
    )
    band_delta = row_delta[:, :, 0].T
    fixed_delta = row_delta[:, :, 1].T
    split_g = grad_out.reshape(seq_rows, head_pairs, 2, head_dim)
    band_g, fixed_g = (split_g[:, :, 0], split_g[:, :, 1])
    ext_dk = jnp.zeros((seq_rows + WIN, head_pairs, head_dim), jnp.float32)
    ext_dv = jnp.zeros((seq_rows + WIN, head_pairs, head_dim), jnp.float32)
    band_dq = []
    fixed_dq = []
    fixed_dk = []
    fixed_dv = []
    number = 0
    row_start = number * block_rows
    row_end = row_start + block_rows
    scores = band_scores()
    prob_rows = jnp.exp(scores - band_lse[:, row_start:row_end, None])
    grad_prob = head_scores(band_g, ext_v, 1.0)
    grad_score = (prob_rows * (grad_prob - band_delta[:, row_start:row_end, None])).astype(
        jnp.bfloat16
    )
    band_dq.append(apply_rows(grad_score, ext_k) * score_scale)
    ext_dk = ext_dk.at[row_start : row_end + WIN].add(apply_cols(grad_score, band_q) * score_scale)
    ext_dv = ext_dv.at[row_start : row_end + WIN].add(
        apply_cols(prob_rows.astype(jnp.bfloat16), band_g)
    )
    scores = own_scores()
    prob_rows = jnp.exp(scores - fixed_lse[:, row_start:row_end, None])
    grad_prob = head_scores(fixed_g, fixed_v, 1.0)
    grad_score = (prob_rows * (grad_prob - fixed_delta[:, row_start:row_end, None])).astype(
        jnp.bfloat16
    )
    fixed_dq.append(apply_rows(grad_score, fixed_k) * score_scale)
    fixed_dk.append(apply_cols(grad_score, fixed_q) * score_scale)
    fixed_dv.append(apply_cols(prob_rows.astype(jnp.bfloat16), fixed_g))
    back_k, back_v = (
        passed_along(ext_dk[:WIN].astype(jnp.bfloat16), "seq", -1).astype(jnp.float32),
        passed_along(ext_dv[:WIN].astype(jnp.bfloat16), "seq", -1).astype(jnp.float32),
    )
    band_dk = ext_dk[WIN:].at[seq_rows - WIN :].add(back_k)
    band_dv = ext_dv[WIN:].at[seq_rows - WIN :].add(back_v)
    band_dq = band_dq[0]
    fixed_dq = fixed_dq[0]
    fixed_dk = fixed_dk[0]
    fixed_dv = fixed_dv[0]

    def far_grads(row_start):
        scores, key_piece, value_piece = far_piece(row_start)
        prob_rows = jnp.exp(scores - fixed_lse[..., None])
        grad_prob = head_scores(fixed_g, value_piece, 1.0)
        grad_score = (prob_rows * (grad_prob - fixed_delta[..., None])).astype(jnp.bfloat16)
        return (grad_score, prob_rows, key_piece)

    key_parts = []
    value_parts = []
    for row_start in range(0, far_count, piece_rows):

        def visit_piece(query_acc, row_start=row_start):
            grad_score, prob_rows, key_piece = far_grads(row_start)
            key_term = (apply_cols(grad_score, fixed_q) * score_scale).reshape(
                piece_rows, head_pairs * head_dim
            )
            value_term = apply_cols(prob_rows.astype(jnp.bfloat16), fixed_g).reshape(
                piece_rows, head_pairs * head_dim
            )
            return (
                query_acc + apply_rows(grad_score, key_piece) * score_scale,
                key_term,
                value_term,
            )

        def skip_piece(query_acc):
            zero_grads = jnp.zeros((piece_rows, head_pairs * head_dim), jnp.float32)
            return (query_acc, zero_grads, zero_grads)

        fixed_dq, key_term, value_term = lax.cond(
            row_start < own_end, visit_piece, skip_piece, fixed_dq
        )
        key_parts.append(key_term)
        value_parts.append(value_term)
    digest_dkv = lax.psum_scatter(
        jnp.concatenate(
            [jnp.concatenate(key_parts, 0), jnp.concatenate(value_parts, 0)], 1
        ).astype(jnp.bfloat16),
        "seq",
        scatter_dimension=0,
        tiled=True,
    )
    digest_dk = digest_dkv[:, :pair_width].reshape(digest_count, head_pairs, head_dim)
    digest_dv = digest_dkv[:, pair_width:].reshape(digest_count, head_pairs, head_dim)
    fixed_dk = fixed_dk + jnp.einsum(
        "hjr,jhc->rhc", select, digest_dk, preferred_element_type=jnp.float32
    )
    fixed_dv = fixed_dv + jnp.einsum(
        "hjr,jhc->rhc", select, digest_dv, preferred_element_type=jnp.float32
    )

    def alternate(band_part, fixed_part):
        return (
            jnp.stack([band_part, fixed_part], 2).reshape(seq_rows, full_width).astype(jnp.bfloat16)
        )

    return (
        attention,
        alternate(band_dq.transpose(1, 0, 2), fixed_dq.transpose(1, 0, 2)),
        alternate(band_dk, fixed_dk),
        alternate(band_dv, fixed_dv),
    )


def solution(mesh):
    in_specs = (
        P("seq", "head"),
        P("seq", "head"),
        P("seq", "head"),
        P("head", None),
        P(("seq", "head"), None),
        P("head", None),
    )
    out_specs = (P("seq", "head"), P("seq", "head"), P("seq", "head"), P("seq", "head"))
    return jax.shard_map(
        on_device, mesh=mesh, in_specs=in_specs, out_specs=out_specs, check_vma=False
    )
```

```python
import jax
import jax.numpy as jnp
from jax import lax
from jax.sharding import PartitionSpec as P

WIN = 256
BLOCK = 128
SUMM = 32


NEG = -1e30


def passed_along(value, axis, steps):
    count = lax.axis_size(axis)
    first, last = (max(0, -steps), min(count, count - steps))
    return lax.ppermute(value, axis, [(source, source + steps) for source in range(first, last)])


def seq_reduce_scatter(parts):
    count = lax.axis_size("seq")
    if count & (count - 1):
        return lax.psum_scatter(
            parts.astype(jnp.bfloat16), "seq", scatter_dimension=0, tiled=True
        )
    me = lax.axis_index("seq")
    bits = count.bit_length() - 1
    chunk = parts.shape[0] // count
    held = parts.reshape((2,) * bits + (chunk, parts.shape[1]))
    for bit in range(bits):
        axis = bits - 1 - bit
        mine = (me >> bit) & 1
        keep = lax.dynamic_index_in_dim(held, mine, axis, keepdims=False)
        send = lax.dynamic_index_in_dim(held, 1 - mine, axis, keepdims=False)
        arrived = lax.ppermute(
            send.astype(jnp.bfloat16), "seq", [(source, source ^ (1 << bit)) for source in range(count)]
        )
        held = keep + arrived.astype(jnp.float32)
    return held.astype(jnp.bfloat16)


def head_scores(left, right, factor):
    return jnp.einsum("qhc,khc->hqk", left, right, preferred_element_type=jnp.float32) * factor


def apply_rows(weights, right):
    return jnp.einsum("hqk,khc->hqc", weights, right, preferred_element_type=jnp.float32)


def apply_cols(weights, left):
    return jnp.einsum("hqk,qhc->khc", weights, left, preferred_element_type=jnp.float32)


def piece_length(total_rows):
    turn_count = max(1, min(8, total_rows // 512))
    while total_rows % turn_count:
        turn_count -= 1
    return total_rows // turn_count


def keep_state(carried):
    return carried


def on_device(queries, keys, values, out_weight, cotangent, offsets):
    seq_rows = queries.shape[0]
    full_width = queries.shape[1]
    head_pairs = offsets.shape[0]
    head_dim = full_width // (2 * head_pairs)
    score_scale = head_dim ** (-0.5)
    block_rows = min(512, seq_rows)
    seq_index = lax.axis_index("seq")
    start_pos = seq_index * seq_rows
    positions = start_pos + jnp.arange(seq_rows, dtype=jnp.int32)
    block_ids = positions // BLOCK
    split_q = queries.reshape(seq_rows, head_pairs, 2, head_dim)
    split_k = keys.reshape(seq_rows, head_pairs, 2, head_dim)
    split_v = values.reshape(seq_rows, head_pairs, 2, head_dim)
    band_q, fixed_q = (split_q[:, :, 0], split_q[:, :, 1])
    band_k, fixed_k = (split_k[:, :, 0], split_k[:, :, 1])
    band_v, fixed_v = (split_v[:, :, 0], split_v[:, :, 1])
    prev_k, prev_v = passed_along((band_k, band_v), "seq", 1)
    ext_k = jnp.concatenate([prev_k, band_k], 0)
    ext_v = jnp.concatenate([prev_v, band_v], 0)
    ext_pos = start_pos - WIN + jnp.arange(seq_rows + WIN, dtype=jnp.int32)

    def band_scores():
        distance = positions[:, None] - ext_pos[None, :]
        visible = (distance >= 0) & (distance < WIN) & (ext_pos[None, :] >= 0)
        scores = head_scores(band_q, ext_k, score_scale)
        return jnp.where(visible[None], scores, NEG)

    def own_scores():
        same_block = positions[:, None] // BLOCK == positions[None, :] // BLOCK
        visible = same_block & (positions[None, :] <= positions[:, None])
        scores = head_scores(fixed_q, fixed_k, score_scale)
        return jnp.where(visible[None], scores, NEG)

    band_out = []
    band_lse = []
    number = 0
    row_start = number * block_rows
    scores = band_scores()
    row_max = scores.max(-1)
    weights = jnp.exp(scores - row_max[..., None])
    row_sum = weights.sum(-1)
    band_out.append(apply_rows(weights.astype(jnp.bfloat16), ext_v) / row_sum[..., None])
    band_lse.append(row_max + jnp.log(row_sum))
    scores = own_scores()
    row_max = scores.max(-1)
    weights = jnp.exp(scores - row_max[..., None])
    fixed_max = row_max
    fixed_sum = weights.sum(-1)
    fixed_acc = apply_rows(weights.astype(jnp.bfloat16), fixed_v)
    band_out = band_out[0]
    band_lse = band_lse[0]
    running = (fixed_max, fixed_sum, fixed_acc)
    digest_count = seq_rows // BLOCK * SUMM
    offset_table = jnp.tile(offsets.T, (seq_rows // BLOCK, 1))
    digest_rows = (jnp.arange(digest_count, dtype=jnp.int32) // SUMM * BLOCK)[
        :, None
    ] + offset_table
    select = (
        digest_rows.T[:, :, None] == jnp.arange(seq_rows, dtype=jnp.int32)[None, None, :]
    ).astype(jnp.bfloat16)
    digest_k = jnp.einsum(
        "hjr,rhc->jhc", select, fixed_k, preferred_element_type=jnp.float32
    ).astype(jnp.bfloat16)
    digest_v = jnp.einsum(
        "hjr,rhc->jhc", select, fixed_v, preferred_element_type=jnp.float32
    ).astype(jnp.bfloat16)
    pair_width = head_pairs * head_dim
    far_kv = lax.all_gather(
        jnp.concatenate(
            [
                digest_k.reshape(digest_count, pair_width),
                digest_v.reshape(digest_count, pair_width),
            ],
            1,
        ),
        "seq",
        axis=0,
        tiled=True,
    )
    far_k, far_v = far_kv[:, :pair_width], far_kv[:, pair_width:]
    far_count = far_k.shape[0]
    piece_rows = piece_length(far_count)
    own_end = (seq_index + 1) * digest_count

    def far_piece(row_start):
        key_piece = far_k[row_start : row_start + piece_rows].reshape(
            piece_rows, head_pairs, head_dim
        )
        value_piece = far_v[row_start : row_start + piece_rows].reshape(
            piece_rows, head_pairs, head_dim
        )
        key_block = (row_start + jnp.arange(piece_rows, dtype=jnp.int32)) // SUMM
        visible = key_block[None, :] < block_ids[:, None]
        scores = jnp.where(visible[None], head_scores(fixed_q, key_piece, score_scale), NEG)
        return (scores, key_piece, value_piece)

    for row_start in range(0, far_count, piece_rows):

        def visit_piece(carried, row_start=row_start):
            row_max, row_sum, weighted = carried
            scores, key_piece, value_piece = far_piece(row_start)
            new_max = jnp.maximum(row_max, scores.max(-1))
            rescale = jnp.exp(row_max - new_max)
            weights = jnp.exp(scores - new_max[..., None])
            return (
                new_max,
                row_sum * rescale + weights.sum(-1),
                weighted * rescale[..., None]
                + apply_rows(weights.astype(jnp.bfloat16), value_piece),
            )

        running = lax.cond(row_start < own_end, visit_piece, keep_state, running)
    fixed_out = running[2] / running[1][..., None]
    fixed_lse = running[0] + jnp.log(running[1])
    attention = jnp.stack([band_out.transpose(1, 0, 2), fixed_out.transpose(1, 0, 2)], 2)
    attention = attention.reshape(seq_rows, full_width).astype(jnp.bfloat16)
    head_count = lax.axis_size("head")
    head_index = lax.axis_index("head")
    pieces = [cotangent] + [
        lax.ppermute(
            cotangent, "head", [(source, (source + shift) % head_count) for source in range(head_count)]
        )
        for shift in range(1, head_count)
    ]
    doubled = jnp.stack(pieces[::-1] + pieces[::-1], 0)
    gathered = lax.dynamic_slice_in_dim(doubled, head_count - 1 - head_index, head_count, 0)
    grad_out = lax.dot_general(
        gathered.reshape(seq_rows, cotangent.shape[1]),
        out_weight,
        (((1,), (1,)), ((), ())),
        preferred_element_type=jnp.float32,
    ).astype(jnp.bfloat16)
    row_delta = jnp.sum(
        grad_out.astype(jnp.float32).reshape(seq_rows, head_pairs, 2, head_dim)
        * attention.astype(jnp.float32).reshape(seq_rows, head_pairs, 2, head_dim),
        -1,
    )
    band_delta = row_delta[:, :, 0].T
    fixed_delta = row_delta[:, :, 1].T
    split_g = grad_out.reshape(seq_rows, head_pairs, 2, head_dim)
    band_g, fixed_g = (split_g[:, :, 0], split_g[:, :, 1])
    ext_dk = jnp.zeros((seq_rows + WIN, head_pairs, head_dim), jnp.float32)
    ext_dv = jnp.zeros((seq_rows + WIN, head_pairs, head_dim), jnp.float32)
    band_dq = []
    fixed_dq = []
    fixed_dk = []
    fixed_dv = []
    number = 0
    row_start = number * block_rows
    row_end = row_start + block_rows
    scores = band_scores()
    prob_rows = jnp.exp(scores - band_lse[:, row_start:row_end, None])
    grad_prob = head_scores(band_g, ext_v, 1.0)
    grad_score = (prob_rows * (grad_prob - band_delta[:, row_start:row_end, None])).astype(
        jnp.bfloat16
    )
    band_dq.append(apply_rows(grad_score, ext_k) * score_scale)
    ext_dk = ext_dk.at[row_start : row_end + WIN].add(apply_cols(grad_score, band_q) * score_scale)
    ext_dv = ext_dv.at[row_start : row_end + WIN].add(
        apply_cols(prob_rows.astype(jnp.bfloat16), band_g)
    )
    scores = own_scores()
    prob_rows = jnp.exp(scores - fixed_lse[:, row_start:row_end, None])
    grad_prob = head_scores(fixed_g, fixed_v, 1.0)
    grad_score = (prob_rows * (grad_prob - fixed_delta[:, row_start:row_end, None])).astype(
        jnp.bfloat16
    )
    fixed_dq.append(apply_rows(grad_score, fixed_k) * score_scale)
    fixed_dk.append(apply_cols(grad_score, fixed_q) * score_scale)
    fixed_dv.append(apply_cols(prob_rows.astype(jnp.bfloat16), fixed_g))
    back_k, back_v = (
        passed_along(ext_dk[:WIN].astype(jnp.bfloat16), "seq", -1).astype(jnp.float32),
        passed_along(ext_dv[:WIN].astype(jnp.bfloat16), "seq", -1).astype(jnp.float32),
    )
    band_dk = ext_dk[WIN:].at[seq_rows - WIN :].add(back_k)
    band_dv = ext_dv[WIN:].at[seq_rows - WIN :].add(back_v)
    band_dq = band_dq[0]
    fixed_dq = fixed_dq[0]
    fixed_dk = fixed_dk[0]
    fixed_dv = fixed_dv[0]

    def far_grads(row_start):
        scores, key_piece, value_piece = far_piece(row_start)
        prob_rows = jnp.exp(scores - fixed_lse[..., None])
        grad_prob = head_scores(fixed_g, value_piece, 1.0)
        grad_score = (prob_rows * (grad_prob - fixed_delta[..., None])).astype(jnp.bfloat16)
        return (grad_score, prob_rows, key_piece)

    key_parts = []
    value_parts = []
    for row_start in range(0, far_count, piece_rows):

        def visit_piece(query_acc, row_start=row_start):
            grad_score, prob_rows, key_piece = far_grads(row_start)
            key_term = (apply_cols(grad_score, fixed_q) * score_scale).reshape(
                piece_rows, head_pairs * head_dim
            )
            value_term = apply_cols(prob_rows.astype(jnp.bfloat16), fixed_g).reshape(
                piece_rows, head_pairs * head_dim
            )
            return (
                query_acc + apply_rows(grad_score, key_piece) * score_scale,
                key_term,
                value_term,
            )

        def skip_piece(query_acc):
            zero_grads = jnp.zeros((piece_rows, head_pairs * head_dim), jnp.float32)
            return (query_acc, zero_grads, zero_grads)

        fixed_dq, key_term, value_term = lax.cond(
            row_start < own_end, visit_piece, skip_piece, fixed_dq
        )
        key_parts.append(key_term)
        value_parts.append(value_term)
    digest_dkv = seq_reduce_scatter(
        jnp.concatenate([jnp.concatenate(key_parts, 0), jnp.concatenate(value_parts, 0)], 1)
    )
    digest_dk = digest_dkv[:, :pair_width].reshape(digest_count, head_pairs, head_dim)
    digest_dv = digest_dkv[:, pair_width:].reshape(digest_count, head_pairs, head_dim)
    fixed_dk = fixed_dk + jnp.einsum(
        "hjr,jhc->rhc", select, digest_dk, preferred_element_type=jnp.float32
    )
    fixed_dv = fixed_dv + jnp.einsum(
        "hjr,jhc->rhc", select, digest_dv, preferred_element_type=jnp.float32
    )

    def alternate(band_part, fixed_part):
        return (
            jnp.stack([band_part, fixed_part], 2).reshape(seq_rows, full_width).astype(jnp.bfloat16)
        )

    return (
        attention,
        alternate(band_dq.transpose(1, 0, 2), fixed_dq.transpose(1, 0, 2)),
        alternate(band_dk, fixed_dk),
        alternate(band_dv, fixed_dv),
    )


def solution(mesh):
    in_specs = (
        P("seq", "head"),
        P("seq", "head"),
        P("seq", "head"),
        P("head", None),
        P(("seq", "head"), None),
        P("head", None),
    )
    out_specs = (P("seq", "head"), P("seq", "head"), P("seq", "head"), P("seq", "head"))
    return jax.shard_map(
        on_device, mesh=mesh, in_specs=in_specs, out_specs=out_specs, check_vma=False
    )
```

```python
import functools

import jax
import jax.numpy as jnp
from jax import lax
from jax.experimental import pallas as pl
from jax.experimental.pallas import tpu as pltpu
from jax.sharding import PartitionSpec as P

WIN = 256
BLOCK = 128
SUMM = 32


NEG = -1e30


def passed_along(value, axis, steps):
    count = lax.axis_size(axis)
    first, last = (max(0, -steps), min(count, count - steps))
    return lax.ppermute(value, axis, [(source, source + steps) for source in range(first, last)])


def seq_reduce_scatter(parts, axis):
    count = lax.axis_size("seq")
    if count & (count - 1):
        return lax.psum_scatter(
            parts.astype(jnp.bfloat16), "seq", scatter_dimension=axis, tiled=True
        )
    me = lax.axis_index("seq")
    bits = count.bit_length() - 1
    chunk = parts.shape[axis] // count
    held = parts.reshape(parts.shape[:axis] + (2,) * bits + (chunk,) + parts.shape[axis + 1 :])
    for bit in range(bits):
        where = axis + bits - 1 - bit
        mine = (me >> bit) & 1
        keep = lax.dynamic_index_in_dim(held, mine, where, keepdims=False)
        send = lax.dynamic_index_in_dim(held, 1 - mine, where, keepdims=False)
        arrived = lax.ppermute(
            send.astype(jnp.bfloat16), "seq", [(source, source ^ (1 << bit)) for source in range(count)]
        )
        held = keep + arrived.astype(jnp.float32)
    return held.astype(jnp.bfloat16)


def nt(left, right):
    return lax.dot_general(left, right, (((1,), (1,)), ((), ())), preferred_element_type=jnp.float32)


def tn(left, right):
    return lax.dot_general(left, right, (((0,), (0,)), ((), ())), preferred_element_type=jnp.float32)


def nn(left, right):
    return lax.dot_general(left, right, (((1,), (0,)), ((), ())), preferred_element_type=jnp.float32)


def two_part_attention(q, g, first, second, scale):
    (k_a, v_a, mask_a), (k_b, v_b, mask_b) = first, second
    s_a = jnp.where(mask_a, nt(q, k_a) * scale, NEG)
    s_b = jnp.where(mask_b, nt(q, k_b) * scale, NEG)
    row_max = jnp.maximum(s_a.max(-1, keepdims=True), s_b.max(-1, keepdims=True))
    w_a = jnp.exp(s_a - row_max)
    w_b = jnp.exp(s_b - row_max)
    row_sum = w_a.sum(-1, keepdims=True) + w_b.sum(-1, keepdims=True)
    mixed = nn(w_a.astype(jnp.bfloat16), v_a) + nn(w_b.astype(jnp.bfloat16), v_b)
    out = (mixed / row_sum).astype(jnp.bfloat16)
    log_total = row_max + jnp.log(row_sum)
    delta = jnp.sum(g.astype(jnp.float32) * out.astype(jnp.float32), -1, keepdims=True)
    p_a = jnp.exp(s_a - log_total)
    p_b = jnp.exp(s_b - log_total)
    gs_a = (p_a * (nt(g, v_a) - delta)).astype(jnp.bfloat16)
    gs_b = (p_b * (nt(g, v_b) - delta)).astype(jnp.bfloat16)
    dq = ((nn(gs_a, k_a) + nn(gs_b, k_b)) * scale).astype(jnp.bfloat16)
    dk_a = tn(gs_a, q) * scale
    dk_b = tn(gs_b, q) * scale
    dv_a = tn(p_a.astype(jnp.bfloat16), g)
    dv_b = tn(p_b.astype(jnp.bfloat16), g)
    return out, dq, (dk_a, dv_a), (dk_b, dv_b)


def pair_kernel(
    seq_ref,
    q_ref,
    k_ref,
    v_ref,
    g_ref,
    kp_ref,
    vp_ref,
    kf_ref,
    vf_ref,
    out_ref,
    dq_ref,
    dk_ref,
    dv_ref,
    dkp_ref,
    dvp_ref,
    dkvf_ref,
    *,
    head_dim,
    scale,
):
    rows = q_ref.shape[0]
    far_rows = kf_ref.shape[0]
    start = seq_ref[0] * rows
    hd = head_dim
    qi = lax.broadcasted_iota(jnp.int32, (rows, rows), 0)
    kj = lax.broadcasted_iota(jnp.int32, (rows, rows), 1)
    causal = kj <= qi
    prev_mask = (kj > qi) & (seq_ref[0] > 0)
    own_band = causal & (qi - kj < WIN)
    out_b, dq_b, (dkp, dvp), (dko, dvo) = two_part_attention(
        q_ref[:, :hd],
        g_ref[:, :hd],
        (kp_ref[:, :hd], vp_ref[:, :hd], prev_mask),
        (k_ref[:, :hd], v_ref[:, :hd], own_band),
        scale,
    )
    out_ref[:, :hd] = out_b
    dq_ref[:, :hd] = dq_b
    dk_ref[:, :hd] = dko
    dv_ref[:, :hd] = dvo
    dkp_ref[...] = dkp.astype(dkp_ref.dtype)
    dvp_ref[...] = dvp.astype(dvp_ref.dtype)
    own_fixed = causal & ((qi // BLOCK) == (kj // BLOCK))
    fq = lax.broadcasted_iota(jnp.int32, (rows, far_rows), 0)
    fr = lax.broadcasted_iota(jnp.int32, (rows, far_rows), 1)
    far_mask = (fr // SUMM) < ((start + fq) // BLOCK)
    out_f, dq_f, (dkf_own, dvf_own), (dkf, dvf) = two_part_attention(
        q_ref[:, hd:],
        g_ref[:, hd:],
        (k_ref[:, hd:], v_ref[:, hd:], own_fixed),
        (kf_ref[...], vf_ref[...], far_mask),
        scale,
    )
    out_ref[:, hd:] = out_f
    dq_ref[:, hd:] = dq_f
    dk_ref[:, hd:] = dkf_own
    dv_ref[:, hd:] = dvf_own
    dkvf_ref[0] = dkf
    dkvf_ref[1] = dvf


def pair_attention(seq_index, q, k, v, g, k_prev, v_prev, far_kv, head_pairs, head_dim, scale):
    rows = q.shape[0]
    far_rows = far_kv.shape[0]
    pair = 2 * head_dim

    def col(width):
        return pl.BlockSpec((rows, width), lambda p, s: (0, p))

    far_k_spec = pl.BlockSpec((far_rows, head_dim), lambda p, s: (0, p))
    far_v_spec = pl.BlockSpec((far_rows, head_dim), lambda p, s: (0, head_pairs + p))
    flops = 2 * rows * head_dim * (2 * rows + rows + far_rows) * 7 * head_pairs
    cost = pl.CostEstimate(
        flops=flops,
        transcendentals=2 * rows * (3 * rows + far_rows) * head_pairs,
        bytes_accessed=rows * pair * 2 * 16 * head_pairs + far_rows * head_dim * 12 * head_pairs,
    )
    grid_spec = pltpu.PrefetchScalarGridSpec(
        num_scalar_prefetch=1,
        grid=(head_pairs,),
        in_specs=[col(pair)] * 6 + [far_k_spec, far_v_spec],
        out_specs=[
            col(pair),
            col(pair),
            col(pair),
            col(pair),
            col(head_dim),
            col(head_dim),
            pl.BlockSpec((2, far_rows, head_dim), lambda p, s: (0, 0, p)),
        ],
    )
    width = head_pairs * pair
    return pl.pallas_call(
        functools.partial(pair_kernel, head_dim=head_dim, scale=scale),
        grid_spec=grid_spec,
        out_shape=[
            jax.ShapeDtypeStruct((rows, width), jnp.bfloat16),
            jax.ShapeDtypeStruct((rows, width), jnp.bfloat16),
            jax.ShapeDtypeStruct((rows, width), jnp.float32),
            jax.ShapeDtypeStruct((rows, width), jnp.float32),
            jax.ShapeDtypeStruct((rows, head_pairs * head_dim), jnp.bfloat16),
            jax.ShapeDtypeStruct((rows, head_pairs * head_dim), jnp.bfloat16),
            jax.ShapeDtypeStruct((2, far_rows, head_pairs * head_dim), jnp.float32),
        ],
        compiler_params=pltpu.CompilerParams(vmem_limit_bytes=48 * 1024 * 1024),
        cost_estimate=cost,
    )(seq_index, q, k, v, g, k_prev, v_prev, far_kv, far_kv)


def on_device(queries, keys, values, out_weight, cotangent, offsets):
    seq_rows = queries.shape[0]
    full_width = queries.shape[1]
    head_pairs = offsets.shape[0]
    head_dim = full_width // (2 * head_pairs)
    score_scale = head_dim ** (-0.5)
    assert seq_rows == WIN and seq_rows % BLOCK == 0
    seq_index = lax.axis_index("seq")
    split_k = keys.reshape(seq_rows, head_pairs, 2, head_dim)
    split_v = values.reshape(seq_rows, head_pairs, 2, head_dim)
    fixed_k = split_k[:, :, 1]
    fixed_v = split_v[:, :, 1]
    prev_k, prev_v = passed_along((keys, values), "seq", 1)
    digest_count = seq_rows // BLOCK * SUMM
    offset_table = jnp.tile(offsets.T, (seq_rows // BLOCK, 1))
    digest_rows = (jnp.arange(digest_count, dtype=jnp.int32) // SUMM * BLOCK)[
        :, None
    ] + offset_table
    select = (
        digest_rows.T[:, :, None] == jnp.arange(seq_rows, dtype=jnp.int32)[None, None, :]
    ).astype(jnp.bfloat16)
    digest_k = jnp.einsum(
        "hjr,rhc->jhc", select, fixed_k, preferred_element_type=jnp.float32
    ).astype(jnp.bfloat16)
    digest_v = jnp.einsum(
        "hjr,rhc->jhc", select, fixed_v, preferred_element_type=jnp.float32
    ).astype(jnp.bfloat16)
    pair_width = head_pairs * head_dim
    far_kv = lax.all_gather(
        jnp.concatenate(
            [
                digest_k.reshape(digest_count, pair_width),
                digest_v.reshape(digest_count, pair_width),
            ],
            1,
        ),
        "seq",
        axis=0,
        tiled=True,
    )
    head_count = lax.axis_size("head")
    head_index = lax.axis_index("head")
    pieces = [cotangent] + [
        lax.ppermute(
            cotangent, "head", [(source, (source + shift) % head_count) for source in range(head_count)]
        )
        for shift in range(1, head_count)
    ]
    doubled = jnp.stack(pieces[::-1] + pieces[::-1], 0)
    gathered = lax.dynamic_slice_in_dim(doubled, head_count - 1 - head_index, head_count, 0)
    grad_out = lax.dot_general(
        gathered.reshape(seq_rows, cotangent.shape[1]),
        out_weight,
        (((1,), (1,)), ((), ())),
        preferred_element_type=jnp.float32,
    ).astype(jnp.bfloat16)
    attention, query_grad, own_dk, own_dv, back_k, back_v, far_dkv = pair_attention(
        seq_index.reshape(1).astype(jnp.int32),
        queries,
        keys,
        values,
        grad_out,
        prev_k,
        prev_v,
        far_kv,
        head_pairs,
        head_dim,
        score_scale,
    )
    back_k, back_v = passed_along((back_k, back_v), "seq", -1)
    digest_dkv = seq_reduce_scatter(far_dkv, 1)
    digest_dk = digest_dkv[0].reshape(digest_count, head_pairs, head_dim)
    digest_dv = digest_dkv[1].reshape(digest_count, head_pairs, head_dim)
    fixed_dk = jnp.einsum("hjr,jhc->rhc", select, digest_dk, preferred_element_type=jnp.float32)
    fixed_dv = jnp.einsum("hjr,jhc->rhc", select, digest_dv, preferred_element_type=jnp.float32)

    def with_extra(own, band_extra, fixed_extra):
        extra = jnp.stack(
            [band_extra.reshape(seq_rows, head_pairs, head_dim).astype(jnp.float32), fixed_extra], 2
        ).reshape(seq_rows, full_width)
        return (own + extra).astype(jnp.bfloat16)

    return (
        attention,
        query_grad,
        with_extra(own_dk, back_k, fixed_dk),
        with_extra(own_dv, back_v, fixed_dv),
    )


def solution(mesh):
    in_specs = (
        P("seq", "head"),
        P("seq", "head"),
        P("seq", "head"),
        P("head", None),
        P(("seq", "head"), None),
        P("head", None),
    )
    out_specs = (P("seq", "head"), P("seq", "head"), P("seq", "head"), P("seq", "head"))
    return jax.shard_map(
        on_device, mesh=mesh, in_specs=in_specs, out_specs=out_specs, check_vma=False
    )
```

```python
import functools

import jax
import jax.numpy as jnp
from jax import lax
from jax.experimental import pallas as pl
from jax.experimental.pallas import tpu as pltpu
from jax.sharding import PartitionSpec as P

WIN = 256
BLOCK = 128
SUMM = 32


NEG = -1e30


def passed_along(value, axis, steps):
    count = lax.axis_size(axis)
    first, last = (max(0, -steps), min(count, count - steps))
    return lax.ppermute(value, axis, [(source, source + steps) for source in range(first, last)])


def seq_reduce_scatter(parts, axis):
    count = lax.axis_size("seq")
    if count & (count - 1):
        return lax.psum_scatter(
            parts.astype(jnp.bfloat16), "seq", scatter_dimension=axis, tiled=True
        )
    me = lax.axis_index("seq")
    bits = count.bit_length() - 1
    chunk = parts.shape[axis] // count
    held = parts.reshape(parts.shape[:axis] + (2,) * bits + (chunk,) + parts.shape[axis + 1 :])
    for bit in range(bits):
        where = axis + bits - 1 - bit
        mine = (me >> bit) & 1
        keep = lax.dynamic_index_in_dim(held, mine, where, keepdims=False)
        send = lax.dynamic_index_in_dim(held, 1 - mine, where, keepdims=False)
        arrived = lax.ppermute(
            send.astype(jnp.bfloat16), "seq", [(source, source ^ (1 << bit)) for source in range(count)]
        )
        held = keep + arrived.astype(jnp.float32)
    return held.astype(jnp.bfloat16)


def nt(left, right):
    return lax.dot_general(left, right, (((1,), (1,)), ((), ())), preferred_element_type=jnp.float32)


def tn(left, right):
    return lax.dot_general(left, right, (((0,), (0,)), ((), ())), preferred_element_type=jnp.float32)


def nn(left, right):
    return lax.dot_general(left, right, (((1,), (0,)), ((), ())), preferred_element_type=jnp.float32)


def two_part_attention(q, g, first, second, scale):
    (k_a, v_a, mask_a), (k_b, v_b, mask_b) = first, second
    s_a = jnp.where(mask_a, nt(q, k_a) * scale, NEG)
    s_b = jnp.where(mask_b, nt(q, k_b) * scale, NEG)
    row_max = jnp.maximum(s_a.max(-1, keepdims=True), s_b.max(-1, keepdims=True))
    w_a = jnp.exp(s_a - row_max)
    w_b = jnp.exp(s_b - row_max)
    row_sum = w_a.sum(-1, keepdims=True) + w_b.sum(-1, keepdims=True)
    mixed = nn(w_a.astype(jnp.bfloat16), v_a) + nn(w_b.astype(jnp.bfloat16), v_b)
    out = (mixed / row_sum).astype(jnp.bfloat16)
    log_total = row_max + jnp.log(row_sum)
    delta = jnp.sum(g.astype(jnp.float32) * out.astype(jnp.float32), -1, keepdims=True)
    p_a = jnp.exp(s_a - log_total)
    p_b = jnp.exp(s_b - log_total)
    gs_a = (p_a * (nt(g, v_a) - delta)).astype(jnp.bfloat16)
    gs_b = (p_b * (nt(g, v_b) - delta)).astype(jnp.bfloat16)
    dq = ((nn(gs_a, k_a) + nn(gs_b, k_b)) * scale).astype(jnp.bfloat16)
    dk_a = tn(gs_a, q) * scale
    dk_b = tn(gs_b, q) * scale
    dv_a = tn(p_a.astype(jnp.bfloat16), g)
    dv_b = tn(p_b.astype(jnp.bfloat16), g)
    return out, dq, (dk_a, dv_a), (dk_b, dv_b)


def pair_kernel(
    seq_ref,
    q_ref,
    k_ref,
    v_ref,
    g_ref,
    kp_ref,
    vp_ref,
    kf_ref,
    vf_ref,
    out_ref,
    dq_ref,
    dk_ref,
    dv_ref,
    dkp_ref,
    dvp_ref,
    dkvf_ref,
    *,
    head_dim,
    scale,
):
    rows = q_ref.shape[0]
    far_rows = kf_ref.shape[0]
    start = seq_ref[0] * rows
    hd = head_dim
    qi = lax.broadcasted_iota(jnp.int32, (rows, rows), 0)
    kj = lax.broadcasted_iota(jnp.int32, (rows, rows), 1)
    causal = kj <= qi
    prev_mask = (kj > qi) & (seq_ref[0] > 0)
    own_band = causal & (qi - kj < WIN)
    out_b, dq_b, (dkp, dvp), (dko, dvo) = two_part_attention(
        q_ref[:, :hd],
        g_ref[:, :hd],
        (kp_ref[:, :hd], vp_ref[:, :hd], prev_mask),
        (k_ref[:, :hd], v_ref[:, :hd], own_band),
        scale,
    )
    out_ref[:, :hd] = out_b
    dq_ref[:, :hd] = dq_b
    dk_ref[:, :hd] = dko
    dv_ref[:, :hd] = dvo
    dkp_ref[...] = dkp.astype(dkp_ref.dtype)
    dvp_ref[...] = dvp.astype(dvp_ref.dtype)
    own_fixed = causal & ((qi // BLOCK) == (kj // BLOCK))
    fq = lax.broadcasted_iota(jnp.int32, (rows, far_rows), 0)
    fr = lax.broadcasted_iota(jnp.int32, (rows, far_rows), 1)
    far_mask = (fr // SUMM) < ((start + fq) // BLOCK)
    out_f, dq_f, (dkf_own, dvf_own), (dkf, dvf) = two_part_attention(
        q_ref[:, hd:],
        g_ref[:, hd:],
        (k_ref[:, hd:], v_ref[:, hd:], own_fixed),
        (kf_ref[...], vf_ref[...], far_mask),
        scale,
    )
    out_ref[:, hd:] = out_f
    dq_ref[:, hd:] = dq_f
    dk_ref[:, hd:] = dkf_own
    dv_ref[:, hd:] = dvf_own
    dkvf_ref[0] = dkf
    dkvf_ref[1] = dvf


def pair_attention(
    seq_index, q, k, v, g, k_prev, v_prev, far_kv, first_pair, pairs, head_pairs, head_dim, scale, earlier
):
    rows = q.shape[0]
    far_rows = far_kv.shape[0]
    pair = 2 * head_dim

    def col(width):
        return pl.BlockSpec((rows, width), lambda p, s: (0, first_pair + p))

    far_k_spec = pl.BlockSpec((far_rows, head_dim), lambda p, s: (0, p))
    far_v_spec = pl.BlockSpec((far_rows, head_dim), lambda p, s: (0, pairs + p))
    flops = 2 * rows * head_dim * (2 * rows + rows + far_rows) * 7 * pairs
    cost = pl.CostEstimate(
        flops=flops,
        transcendentals=2 * rows * (3 * rows + far_rows) * pairs,
        bytes_accessed=rows * pair * 2 * 16 * pairs + far_rows * head_dim * 12 * pairs,
    )
    in_specs = [col(pair)] * 6 + [far_k_spec, far_v_spec]
    operands = [seq_index, q, k, v, g, k_prev, v_prev, far_kv, far_kv]
    aliases = {}
    if earlier is not None:
        for number, array in enumerate(earlier):
            aliases[len(operands) + number] = number
        in_specs = in_specs + [pl.BlockSpec(memory_space=pl.ANY)] * len(earlier)
        operands = operands + list(earlier)
    grid_spec = pltpu.PrefetchScalarGridSpec(
        num_scalar_prefetch=1,
        grid=(pairs,),
        in_specs=in_specs,
        out_specs=[
            col(pair),
            col(pair),
            col(pair),
            col(pair),
            col(head_dim),
            col(head_dim),
            pl.BlockSpec((2, far_rows, head_dim), lambda p, s: (0, 0, p)),
        ],
    )
    width = head_pairs * pair
    kernel = functools.partial(pair_kernel, head_dim=head_dim, scale=scale)
    if earlier is not None:
        kernel = functools.partial(skip_tail, kernel, len(earlier))
    outs = pl.pallas_call(
        kernel,
        grid_spec=grid_spec,
        out_shape=[
            jax.ShapeDtypeStruct((rows, width), jnp.bfloat16),
            jax.ShapeDtypeStruct((rows, width), jnp.bfloat16),
            jax.ShapeDtypeStruct((rows, width), jnp.float32),
            jax.ShapeDtypeStruct((rows, width), jnp.float32),
            jax.ShapeDtypeStruct((rows, head_pairs * head_dim), jnp.bfloat16),
            jax.ShapeDtypeStruct((rows, head_pairs * head_dim), jnp.bfloat16),
            jax.ShapeDtypeStruct((2, far_rows, pairs * head_dim), jnp.float32),
        ],
        input_output_aliases=aliases,
        compiler_params=pltpu.CompilerParams(vmem_limit_bytes=48 * 1024 * 1024),
        cost_estimate=cost,
    )(*operands)
    return outs[:6], outs[6]


def skip_tail(kernel, unused, *refs):
    inputs = refs[: 9]
    outputs = refs[9 + unused :]
    kernel(*inputs, *outputs)


def finalize_kernel(own_k_ref, own_v_ref, back_k_ref, back_v_ref, digest_ref, select_ref, k_out, v_out):
    hd = back_k_ref.shape[1]
    pick = select_ref[0]
    for own_ref, back_ref, side, out_ref in (
        (own_k_ref, back_k_ref, 0, k_out),
        (own_v_ref, back_v_ref, 1, v_out),
    ):
        out_ref[:, :hd] = (own_ref[:, :hd] + back_ref[...].astype(jnp.float32)).astype(out_ref.dtype)
        summary = tn(pick, digest_ref[side])
        out_ref[:, hd:] = (own_ref[:, hd:] + summary).astype(out_ref.dtype)


def finalize(own_k, own_v, back_k, back_v, digest, select, head_pairs, head_dim):
    rows = own_k.shape[0]
    digest_rows = digest.shape[1]
    wide = pl.BlockSpec((rows, 2 * head_dim), lambda p: (0, p))
    narrow = pl.BlockSpec((rows, head_dim), lambda p: (0, p))
    return pl.pallas_call(
        finalize_kernel,
        grid=(head_pairs,),
        in_specs=[
            wide,
            wide,
            narrow,
            narrow,
            pl.BlockSpec((2, digest_rows, head_dim), lambda p: (0, 0, p)),
            pl.BlockSpec((1, digest_rows, rows), lambda p: (p, 0, 0)),
        ],
        out_specs=[wide, wide],
        out_shape=[jax.ShapeDtypeStruct(own_k.shape, jnp.bfloat16)] * 2,
        cost_estimate=pl.CostEstimate(
            flops=4 * rows * digest_rows * head_dim * head_pairs,
            transcendentals=0,
            bytes_accessed=rows * head_dim * head_pairs * 20,
        ),
    )(own_k, own_v, back_k, back_v, digest, select)


def on_device(queries, keys, values, out_weight, cotangent, offsets):
    seq_rows = queries.shape[0]
    full_width = queries.shape[1]
    head_pairs = offsets.shape[0]
    head_dim = full_width // (2 * head_pairs)
    score_scale = head_dim ** (-0.5)
    assert seq_rows == WIN and seq_rows % BLOCK == 0
    seq_index = lax.axis_index("seq")
    split_k = keys.reshape(seq_rows, head_pairs, 2, head_dim)
    split_v = values.reshape(seq_rows, head_pairs, 2, head_dim)
    fixed_k = split_k[:, :, 1]
    fixed_v = split_v[:, :, 1]
    prev_k, prev_v = passed_along((keys, values), "seq", 1)
    digest_count = seq_rows // BLOCK * SUMM
    offset_table = jnp.tile(offsets.T, (seq_rows // BLOCK, 1))
    digest_rows = (jnp.arange(digest_count, dtype=jnp.int32) // SUMM * BLOCK)[
        :, None
    ] + offset_table
    select = (
        digest_rows.T[:, :, None] == jnp.arange(seq_rows, dtype=jnp.int32)[None, None, :]
    ).astype(jnp.bfloat16)
    digest_k = jnp.einsum(
        "hjr,rhc->jhc", select, fixed_k, preferred_element_type=jnp.float32
    ).astype(jnp.bfloat16)
    digest_v = jnp.einsum(
        "hjr,rhc->jhc", select, fixed_v, preferred_element_type=jnp.float32
    ).astype(jnp.bfloat16)
    chunks = 2 if head_pairs % 2 == 0 else 1
    pairs = head_pairs // chunks
    split_dk = digest_k.reshape(digest_count, chunks, pairs * head_dim)
    split_dv = digest_v.reshape(digest_count, chunks, pairs * head_dim)
    far_parts = [
        lax.all_gather(
            jnp.concatenate([split_dk[:, chunk], split_dv[:, chunk]], 1),
            "seq",
            axis=0,
            tiled=True,
        )
        for chunk in range(chunks)
    ]
    head_count = lax.axis_size("head")
    head_index = lax.axis_index("head")
    pieces = [cotangent] + [
        lax.ppermute(
            cotangent, "head", [(source, (source + shift) % head_count) for source in range(head_count)]
        )
        for shift in range(1, head_count)
    ]
    doubled = jnp.stack(pieces[::-1] + pieces[::-1], 0)
    gathered = lax.dynamic_slice_in_dim(doubled, head_count - 1 - head_index, head_count, 0)
    grad_out = lax.dot_general(
        gathered.reshape(seq_rows, cotangent.shape[1]),
        out_weight,
        (((1,), (1,)), ((), ())),
        preferred_element_type=jnp.float32,
    ).astype(jnp.bfloat16)
    seq_scalar = seq_index.reshape(1).astype(jnp.int32)
    outputs = None
    digests = []
    for chunk in range(chunks):
        outputs, far_dkv = pair_attention(
            seq_scalar,
            queries,
            keys,
            values,
            grad_out,
            prev_k,
            prev_v,
            far_parts[chunk],
            chunk * pairs,
            pairs,
            head_pairs,
            head_dim,
            score_scale,
            outputs,
        )
        digests.append(seq_reduce_scatter(far_dkv, 1))
    attention, query_grad, own_dk, own_dv, back_k, back_v = outputs
    back_k, back_v = passed_along((back_k, back_v), "seq", -1)
    digest_dkv = jnp.concatenate(digests, 2) if chunks > 1 else digests[0]
    key_grad, value_grad = finalize(
        own_dk, own_dv, back_k, back_v, digest_dkv, select, head_pairs, head_dim
    )
    return attention, query_grad, key_grad, value_grad


def solution(mesh):
    in_specs = (
        P("seq", "head"),
        P("seq", "head"),
        P("seq", "head"),
        P("head", None),
        P(("seq", "head"), None),
        P("head", None),
    )
    out_specs = (P("seq", "head"), P("seq", "head"), P("seq", "head"), P("seq", "head"))
    return jax.shard_map(
        on_device, mesh=mesh, in_specs=in_specs, out_specs=out_specs, check_vma=False
    )
```

```python
import functools

import jax
import jax.numpy as jnp
from jax import lax
from jax.experimental import pallas as pl
from jax.experimental.pallas import tpu as pltpu
from jax.sharding import PartitionSpec as P

WIN = 256
BLOCK = 128
SUMM = 32


NEG = -1e30


def passed_along(value, axis, steps):
    count = lax.axis_size(axis)
    first, last = (max(0, -steps), min(count, count - steps))
    return lax.ppermute(value, axis, [(source, source + steps) for source in range(first, last)])


def seq_reduce_scatter(parts, axis):
    count = lax.axis_size("seq")
    if count & (count - 1):
        return lax.psum_scatter(
            parts.astype(jnp.bfloat16), "seq", scatter_dimension=axis, tiled=True
        )
    me = lax.axis_index("seq")
    bits = count.bit_length() - 1
    chunk = parts.shape[axis] // count
    held = parts.reshape(parts.shape[:axis] + (2,) * bits + (chunk,) + parts.shape[axis + 1 :])
    for bit in range(bits):
        where = axis + bits - 1 - bit
        mine = (me >> bit) & 1
        keep = lax.dynamic_index_in_dim(held, mine, where, keepdims=False)
        send = lax.dynamic_index_in_dim(held, 1 - mine, where, keepdims=False)
        arrived = lax.ppermute(
            send.astype(jnp.bfloat16), "seq", [(source, source ^ (1 << bit)) for source in range(count)]
        )
        held = keep + arrived.astype(jnp.float32)
    return held.astype(jnp.bfloat16)


def nt(left, right):
    return lax.dot_general(left, right, (((1,), (1,)), ((), ())), preferred_element_type=jnp.float32)


def tn(left, right):
    return lax.dot_general(left, right, (((0,), (0,)), ((), ())), preferred_element_type=jnp.float32)


def nn(left, right):
    return lax.dot_general(left, right, (((1,), (0,)), ((), ())), preferred_element_type=jnp.float32)


def two_part_attention(q, g, first, second, scale):
    (k_a, v_a, mask_a), (k_b, v_b, mask_b) = first, second
    s_a = jnp.where(mask_a, nt(q, k_a) * scale, NEG)
    s_b = jnp.where(mask_b, nt(q, k_b) * scale, NEG)
    row_max = jnp.maximum(s_a.max(-1, keepdims=True), s_b.max(-1, keepdims=True))
    w_a = jnp.exp(s_a - row_max)
    w_b = jnp.exp(s_b - row_max)
    row_sum = w_a.sum(-1, keepdims=True) + w_b.sum(-1, keepdims=True)
    mixed = nn(w_a.astype(jnp.bfloat16), v_a) + nn(w_b.astype(jnp.bfloat16), v_b)
    out = (mixed / row_sum).astype(jnp.bfloat16)
    log_total = row_max + jnp.log(row_sum)
    delta = jnp.sum(g.astype(jnp.float32) * out.astype(jnp.float32), -1, keepdims=True)
    p_a = jnp.exp(s_a - log_total)
    p_b = jnp.exp(s_b - log_total)
    gs_a = (p_a * (nt(g, v_a) - delta)).astype(jnp.bfloat16)
    gs_b = (p_b * (nt(g, v_b) - delta)).astype(jnp.bfloat16)
    dq = ((nn(gs_a, k_a) + nn(gs_b, k_b)) * scale).astype(jnp.bfloat16)
    dk_a = tn(gs_a, q) * scale
    dk_b = tn(gs_b, q) * scale
    dv_a = tn(p_a.astype(jnp.bfloat16), g)
    dv_b = tn(p_b.astype(jnp.bfloat16), g)
    return out, dq, (dk_a, dv_a), (dk_b, dv_b)


def band_kernel(seq_ref, q_ref, k_ref, v_ref, g_ref, kp_ref, vp_ref, out_ref, dq_ref, dk_ref, dv_ref, dkp_ref, dvp_ref, *, scale):
    rows = q_ref.shape[0]
    qi = lax.broadcasted_iota(jnp.int32, (rows, rows), 0)
    kj = lax.broadcasted_iota(jnp.int32, (rows, rows), 1)
    prev_mask = (kj > qi) & (seq_ref[0] > 0)
    own_mask = (kj <= qi) & (qi - kj < WIN)
    out, dq, (dkp, dvp), (dko, dvo) = two_part_attention(
        q_ref[...],
        g_ref[...],
        (kp_ref[...], vp_ref[...], prev_mask),
        (k_ref[...], v_ref[...], own_mask),
        scale,
    )
    out_ref[...] = out
    dq_ref[...] = dq
    dk_ref[...] = dko
    dv_ref[...] = dvo
    dkp_ref[...] = dkp.astype(dkp_ref.dtype)
    dvp_ref[...] = dvp.astype(dvp_ref.dtype)


def fixed_kernel(seq_ref, q_ref, k_ref, v_ref, g_ref, kf_ref, vf_ref, *refs, scale, unused):
    out_ref, dq_ref, dk_ref, dv_ref, dkvf_ref = refs[unused:]
    rows = q_ref.shape[0]
    far_rows = kf_ref.shape[0]
    start = seq_ref[0] * rows
    qi = lax.broadcasted_iota(jnp.int32, (rows, rows), 0)
    kj = lax.broadcasted_iota(jnp.int32, (rows, rows), 1)
    own_mask = (kj <= qi) & ((qi // BLOCK) == (kj // BLOCK))
    fq = lax.broadcasted_iota(jnp.int32, (rows, far_rows), 0)
    fr = lax.broadcasted_iota(jnp.int32, (rows, far_rows), 1)
    far_mask = (fr // SUMM) < ((start + fq) // BLOCK)
    out, dq, (dko, dvo), (dkf, dvf) = two_part_attention(
        q_ref[...],
        g_ref[...],
        (k_ref[...], v_ref[...], own_mask),
        (kf_ref[...], vf_ref[...], far_mask),
        scale,
    )
    out_ref[...] = out
    dq_ref[...] = dq
    dk_ref[...] = dko
    dv_ref[...] = dvo
    dkvf_ref[0] = dkf
    dkvf_ref[1] = dvf


def attention_cost(rows, keys, head_dim, heads):
    return pl.CostEstimate(
        flops=2 * rows * keys * head_dim * 7 * heads,
        transcendentals=3 * rows * keys * heads,
        bytes_accessed=(rows * 16 + keys * 6) * head_dim * heads,
    )


def band_attention(seq_index, q, k, v, g, k_prev, v_prev, head_pairs, head_dim, scale):
    rows = q.shape[0]
    block = pl.BlockSpec((rows, head_dim), lambda p, s: (0, 2 * p))
    narrow = pl.BlockSpec((rows, head_dim), lambda p, s: (0, p))
    width = 2 * head_pairs * head_dim
    grid_spec = pltpu.PrefetchScalarGridSpec(
        num_scalar_prefetch=1,
        grid=(head_pairs,),
        in_specs=[block] * 6,
        out_specs=[block] * 4 + [narrow] * 2,
    )
    return pl.pallas_call(
        functools.partial(band_kernel, scale=scale),
        grid_spec=grid_spec,
        out_shape=[
            jax.ShapeDtypeStruct((rows, width), jnp.bfloat16),
            jax.ShapeDtypeStruct((rows, width), jnp.bfloat16),
            jax.ShapeDtypeStruct((rows, width), jnp.float32),
            jax.ShapeDtypeStruct((rows, width), jnp.float32),
            jax.ShapeDtypeStruct((rows, head_pairs * head_dim), jnp.bfloat16),
            jax.ShapeDtypeStruct((rows, head_pairs * head_dim), jnp.bfloat16),
        ],
        compiler_params=pltpu.CompilerParams(vmem_limit_bytes=48 * 1024 * 1024),
        cost_estimate=attention_cost(rows, 2 * rows, head_dim, head_pairs),
    )(seq_index, q, k, v, g, k_prev, v_prev)


def fixed_attention(seq_index, q, k, v, g, far_kv, first_pair, pairs, head_pairs, head_dim, scale, earlier):
    rows = q.shape[0]
    far_rows = far_kv.shape[0]
    block = pl.BlockSpec((rows, head_dim), lambda p, s: (0, 2 * (first_pair + p) + 1))
    far_k_spec = pl.BlockSpec((far_rows, head_dim), lambda p, s: (0, first_pair + p))
    far_v_spec = pl.BlockSpec((far_rows, head_dim), lambda p, s: (0, head_pairs + first_pair + p))
    operands = [seq_index, q, k, v, g, far_kv, far_kv] + list(earlier)
    aliases = {7 + number: number for number in range(len(earlier))}
    grid_spec = pltpu.PrefetchScalarGridSpec(
        num_scalar_prefetch=1,
        grid=(pairs,),
        in_specs=[block] * 4 + [far_k_spec, far_v_spec]
        + [pl.BlockSpec(memory_space=pl.ANY)] * len(earlier),
        out_specs=[block] * 4 + [pl.BlockSpec((2, far_rows, head_dim), lambda p, s: (0, 0, p))],
    )
    return pl.pallas_call(
        functools.partial(fixed_kernel, scale=scale, unused=len(earlier)),
        grid_spec=grid_spec,
        out_shape=[jax.ShapeDtypeStruct(array.shape, array.dtype) for array in earlier]
        + [jax.ShapeDtypeStruct((2, far_rows, pairs * head_dim), jnp.float32)],
        input_output_aliases=aliases,
        compiler_params=pltpu.CompilerParams(vmem_limit_bytes=48 * 1024 * 1024),
        cost_estimate=attention_cost(rows, rows + far_rows, head_dim, pairs),
    )(*operands)


def finalize_kernel(own_k_ref, own_v_ref, back_k_ref, back_v_ref, digest_ref, select_ref, k_out, v_out):
    hd = back_k_ref.shape[1]
    pick = select_ref[0]
    for own_ref, back_ref, side, out_ref in (
        (own_k_ref, back_k_ref, 0, k_out),
        (own_v_ref, back_v_ref, 1, v_out),
    ):
        out_ref[:, :hd] = (own_ref[:, :hd] + back_ref[...].astype(jnp.float32)).astype(out_ref.dtype)
        summary = tn(pick, digest_ref[side])
        out_ref[:, hd:] = (own_ref[:, hd:] + summary).astype(out_ref.dtype)


def finalize(own_k, own_v, back_k, back_v, digest, select, head_pairs, head_dim):
    rows = own_k.shape[0]
    digest_rows = digest.shape[1]
    wide = pl.BlockSpec((rows, 2 * head_dim), lambda p: (0, p))
    narrow = pl.BlockSpec((rows, head_dim), lambda p: (0, p))
    return pl.pallas_call(
        finalize_kernel,
        grid=(head_pairs,),
        in_specs=[
            wide,
            wide,
            narrow,
            narrow,
            pl.BlockSpec((2, digest_rows, head_dim), lambda p: (0, 0, p)),
            pl.BlockSpec((1, digest_rows, rows), lambda p: (p, 0, 0)),
        ],
        out_specs=[wide, wide],
        out_shape=[jax.ShapeDtypeStruct(own_k.shape, jnp.bfloat16)] * 2,
        cost_estimate=pl.CostEstimate(
            flops=4 * rows * digest_rows * head_dim * head_pairs,
            transcendentals=0,
            bytes_accessed=rows * head_dim * head_pairs * 20,
        ),
    )(own_k, own_v, back_k, back_v, digest, select)


def on_device(queries, keys, values, out_weight, cotangent, offsets):
    seq_rows = queries.shape[0]
    full_width = queries.shape[1]
    head_pairs = offsets.shape[0]
    head_dim = full_width // (2 * head_pairs)
    score_scale = head_dim ** (-0.5)
    assert seq_rows == WIN and seq_rows % BLOCK == 0
    seq_index = lax.axis_index("seq")
    split_k = keys.reshape(seq_rows, head_pairs, 2, head_dim)
    split_v = values.reshape(seq_rows, head_pairs, 2, head_dim)
    fixed_k = split_k[:, :, 1]
    fixed_v = split_v[:, :, 1]
    prev_k, prev_v = passed_along((keys, values), "seq", 1)
    digest_count = seq_rows // BLOCK * SUMM
    offset_table = jnp.tile(offsets.T, (seq_rows // BLOCK, 1))
    digest_rows = (jnp.arange(digest_count, dtype=jnp.int32) // SUMM * BLOCK)[
        :, None
    ] + offset_table
    select = (
        digest_rows.T[:, :, None] == jnp.arange(seq_rows, dtype=jnp.int32)[None, None, :]
    ).astype(jnp.bfloat16)
    digest_k = jnp.einsum(
        "hjr,rhc->jhc", select, fixed_k, preferred_element_type=jnp.float32
    ).astype(jnp.bfloat16)
    digest_v = jnp.einsum(
        "hjr,rhc->jhc", select, fixed_v, preferred_element_type=jnp.float32
    ).astype(jnp.bfloat16)
    pair_width = head_pairs * head_dim
    far_kv = lax.all_gather(
        jnp.concatenate(
            [
                digest_k.reshape(digest_count, pair_width),
                digest_v.reshape(digest_count, pair_width),
            ],
            1,
        ),
        "seq",
        axis=0,
        tiled=True,
    )
    head_count = lax.axis_size("head")
    head_index = lax.axis_index("head")
    pieces = [cotangent] + [
        lax.ppermute(
            cotangent, "head", [(source, (source + shift) % head_count) for source in range(head_count)]
        )
        for shift in range(1, head_count)
    ]
    doubled = jnp.stack(pieces[::-1] + pieces[::-1], 0)
    gathered = lax.dynamic_slice_in_dim(doubled, head_count - 1 - head_index, head_count, 0)
    grad_out = lax.dot_general(
        gathered.reshape(seq_rows, cotangent.shape[1]),
        out_weight,
        (((1,), (1,)), ((), ())),
        preferred_element_type=jnp.float32,
    ).astype(jnp.bfloat16)
    seq_scalar = seq_index.reshape(1).astype(jnp.int32)
    attention, query_grad, own_dk, own_dv, back_k, back_v = band_attention(
        seq_scalar, queries, keys, values, grad_out, prev_k, prev_v, head_pairs, head_dim, score_scale
    )
    chunks = 2 if head_pairs % 2 == 0 else 1
    pairs = head_pairs // chunks
    outputs = (attention, query_grad, own_dk, own_dv)
    digests = []
    for chunk in range(chunks):
        *outputs, far_dkv = fixed_attention(
            seq_scalar,
            queries,
            keys,
            values,
            grad_out,
            far_kv,
            chunk * pairs,
            pairs,
            head_pairs,
            head_dim,
            score_scale,
            outputs,
        )
        digests.append(seq_reduce_scatter(far_dkv, 1))
    attention, query_grad, own_dk, own_dv = outputs
    back_k, back_v = passed_along((back_k, back_v), "seq", -1)
    digest_dkv = jnp.concatenate(digests, 2) if chunks > 1 else digests[0]
    key_grad, value_grad = finalize(
        own_dk, own_dv, back_k, back_v, digest_dkv, select, head_pairs, head_dim
    )
    return attention, query_grad, key_grad, value_grad


def solution(mesh):
    in_specs = (
        P("seq", "head"),
        P("seq", "head"),
        P("seq", "head"),
        P("head", None),
        P(("seq", "head"), None),
        P("head", None),
    )
    out_specs = (P("seq", "head"), P("seq", "head"), P("seq", "head"), P("seq", "head"))
    return jax.shard_map(
        on_device, mesh=mesh, in_specs=in_specs, out_specs=out_specs, check_vma=False
    )
```

```python
import functools

import jax
import jax.numpy as jnp
from jax import lax
from jax.experimental import pallas as pl
from jax.experimental.pallas import tpu as pltpu
from jax.sharding import PartitionSpec as P

WIN = 256
BLOCK = 128
SUMM = 32


NEG = -1e30


def passed_along(value, axis, steps):
    count = lax.axis_size(axis)
    first, last = (max(0, -steps), min(count, count - steps))
    return lax.ppermute(value, axis, [(source, source + steps) for source in range(first, last)])


def seq_reduce_scatter(parts, axis, rotate=0):
    count = lax.axis_size("seq")
    if count & (count - 1):
        return lax.psum_scatter(
            parts.astype(jnp.bfloat16), "seq", scatter_dimension=axis, tiled=True
        )
    me = lax.axis_index("seq")
    bits = count.bit_length() - 1
    chunk = parts.shape[axis] // count
    held = parts.reshape(parts.shape[:axis] + (2,) * bits + (chunk,) + parts.shape[axis + 1 :])
    if bits > 2:
        order = [0] + sorted(range(1, bits - 1), key=lambda b: (b - 1 - rotate) % (bits - 2)) + [bits - 1]
    else:
        order = list(range(bits))
    gone = []
    for bit in order:
        where = axis + bits - 1 - bit - sum(1 for done in gone if done > bit)
        gone.append(bit)
        mine = (me >> bit) & 1
        keep = lax.dynamic_index_in_dim(held, mine, where, keepdims=False)
        send = lax.dynamic_index_in_dim(held, 1 - mine, where, keepdims=False)
        arrived = lax.ppermute(
            send.astype(jnp.bfloat16), "seq", [(source, source ^ (1 << bit)) for source in range(count)]
        )
        held = keep + arrived.astype(jnp.float32)
    return held.astype(jnp.bfloat16)


def nt(left, right):
    return lax.dot_general(left, right, (((1,), (1,)), ((), ())), preferred_element_type=jnp.float32)


def tn(left, right):
    return lax.dot_general(left, right, (((0,), (0,)), ((), ())), preferred_element_type=jnp.float32)


def nn(left, right):
    return lax.dot_general(left, right, (((1,), (0,)), ((), ())), preferred_element_type=jnp.float32)


def two_part_attention(q, g, first, second, scale):
    (k_a, v_a, mask_a), (k_b, v_b, mask_b) = first, second
    s_a = jnp.where(mask_a, nt(q, k_a) * scale, NEG)
    s_b = jnp.where(mask_b, nt(q, k_b) * scale, NEG)
    row_max = jnp.maximum(s_a.max(-1, keepdims=True), s_b.max(-1, keepdims=True))
    w_a = jnp.exp(s_a - row_max)
    w_b = jnp.exp(s_b - row_max)
    row_sum = w_a.sum(-1, keepdims=True) + w_b.sum(-1, keepdims=True)
    mixed = nn(w_a.astype(jnp.bfloat16), v_a) + nn(w_b.astype(jnp.bfloat16), v_b)
    out = (mixed / row_sum).astype(jnp.bfloat16)
    log_total = row_max + jnp.log(row_sum)
    delta = jnp.sum(g.astype(jnp.float32) * out.astype(jnp.float32), -1, keepdims=True)
    p_a = jnp.exp(s_a - log_total)
    p_b = jnp.exp(s_b - log_total)
    gs_a = (p_a * (nt(g, v_a) - delta)).astype(jnp.bfloat16)
    gs_b = (p_b * (nt(g, v_b) - delta)).astype(jnp.bfloat16)
    dq = ((nn(gs_a, k_a) + nn(gs_b, k_b)) * scale).astype(jnp.bfloat16)
    dk_a = tn(gs_a, q) * scale
    dk_b = tn(gs_b, q) * scale
    dv_a = tn(p_a.astype(jnp.bfloat16), g)
    dv_b = tn(p_b.astype(jnp.bfloat16), g)
    return out, dq, (dk_a, dv_a), (dk_b, dv_b)


def band_kernel(seq_ref, q_ref, k_ref, v_ref, g_ref, kp_ref, vp_ref, out_ref, dq_ref, dk_ref, dv_ref, dkp_ref, dvp_ref, *, scale):
    rows = q_ref.shape[0]
    qi = lax.broadcasted_iota(jnp.int32, (rows, rows), 0)
    kj = lax.broadcasted_iota(jnp.int32, (rows, rows), 1)
    prev_mask = (kj > qi) & (seq_ref[0] > 0)
    own_mask = (kj <= qi) & (qi - kj < WIN)
    out, dq, (dkp, dvp), (dko, dvo) = two_part_attention(
        q_ref[...],
        g_ref[...],
        (kp_ref[...], vp_ref[...], prev_mask),
        (k_ref[...], v_ref[...], own_mask),
        scale,
    )
    out_ref[...] = out
    dq_ref[...] = dq
    dk_ref[...] = dko
    dv_ref[...] = dvo
    dkp_ref[...] = dkp.astype(dkp_ref.dtype)
    dvp_ref[...] = dvp.astype(dvp_ref.dtype)


def fixed_kernel(seq_ref, q_ref, k_ref, v_ref, g_ref, kf_ref, vf_ref, *refs, scale, unused):
    out_ref, dq_ref, dk_ref, dv_ref, dkvf_ref = refs[unused:]
    rows = q_ref.shape[0]
    far_rows = kf_ref.shape[0]
    start = seq_ref[0] * rows
    qi = lax.broadcasted_iota(jnp.int32, (rows, rows), 0)
    kj = lax.broadcasted_iota(jnp.int32, (rows, rows), 1)
    own_mask = (kj <= qi) & ((qi // BLOCK) == (kj // BLOCK))
    fq = lax.broadcasted_iota(jnp.int32, (rows, far_rows), 0)
    fr = lax.broadcasted_iota(jnp.int32, (rows, far_rows), 1)
    far_mask = (fr // SUMM) < ((start + fq) // BLOCK)
    out, dq, (dko, dvo), (dkf, dvf) = two_part_attention(
        q_ref[...],
        g_ref[...],
        (k_ref[...], v_ref[...], own_mask),
        (kf_ref[...], vf_ref[...], far_mask),
        scale,
    )
    out_ref[...] = out
    dq_ref[...] = dq
    dk_ref[...] = dko
    dv_ref[...] = dvo
    dkvf_ref[0] = dkf
    dkvf_ref[1] = dvf


def attention_cost(rows, keys, head_dim, heads):
    return pl.CostEstimate(
        flops=2 * rows * keys * head_dim * 7 * heads,
        transcendentals=3 * rows * keys * heads,
        bytes_accessed=(rows * 16 + keys * 6) * head_dim * heads,
    )


def band_attention(seq_index, q, k, v, g, k_prev, v_prev, head_pairs, head_dim, scale):
    rows = q.shape[0]
    block = pl.BlockSpec((rows, head_dim), lambda p, s: (0, 2 * p))
    narrow = pl.BlockSpec((rows, head_dim), lambda p, s: (0, p))
    width = 2 * head_pairs * head_dim
    grid_spec = pltpu.PrefetchScalarGridSpec(
        num_scalar_prefetch=1,
        grid=(head_pairs,),
        in_specs=[block] * 6,
        out_specs=[block] * 4 + [narrow] * 2,
    )
    return pl.pallas_call(
        functools.partial(band_kernel, scale=scale),
        grid_spec=grid_spec,
        out_shape=[
            jax.ShapeDtypeStruct((rows, width), jnp.bfloat16),
            jax.ShapeDtypeStruct((rows, width), jnp.bfloat16),
            jax.ShapeDtypeStruct((rows, width), jnp.float32),
            jax.ShapeDtypeStruct((rows, width), jnp.float32),
            jax.ShapeDtypeStruct((rows, head_pairs * head_dim), jnp.bfloat16),
            jax.ShapeDtypeStruct((rows, head_pairs * head_dim), jnp.bfloat16),
        ],
        compiler_params=pltpu.CompilerParams(vmem_limit_bytes=48 * 1024 * 1024),
        cost_estimate=attention_cost(rows, 2 * rows, head_dim, head_pairs),
    )(seq_index, q, k, v, g, k_prev, v_prev)


def fixed_attention(seq_index, q, k, v, g, far_kv, first_pair, pairs, head_pairs, head_dim, scale, earlier):
    rows = q.shape[0]
    far_rows = far_kv.shape[0]
    block = pl.BlockSpec((rows, head_dim), lambda p, s: (0, 2 * (first_pair + p) + 1))
    far_k_spec = pl.BlockSpec((far_rows, head_dim), lambda p, s: (0, first_pair + p))
    far_v_spec = pl.BlockSpec((far_rows, head_dim), lambda p, s: (0, head_pairs + first_pair + p))
    operands = [seq_index, q, k, v, g, far_kv, far_kv] + list(earlier)
    aliases = {7 + number: number for number in range(len(earlier))}
    grid_spec = pltpu.PrefetchScalarGridSpec(
        num_scalar_prefetch=1,
        grid=(pairs,),
        in_specs=[block] * 4 + [far_k_spec, far_v_spec]
        + [pl.BlockSpec(memory_space=pl.ANY)] * len(earlier),
        out_specs=[block] * 4 + [pl.BlockSpec((2, far_rows, head_dim), lambda p, s: (0, 0, p))],
    )
    return pl.pallas_call(
        functools.partial(fixed_kernel, scale=scale, unused=len(earlier)),
        grid_spec=grid_spec,
        out_shape=[jax.ShapeDtypeStruct(array.shape, array.dtype) for array in earlier]
        + [jax.ShapeDtypeStruct((2, far_rows, pairs * head_dim), jnp.float32)],
        input_output_aliases=aliases,
        compiler_params=pltpu.CompilerParams(vmem_limit_bytes=48 * 1024 * 1024),
        cost_estimate=attention_cost(rows, rows + far_rows, head_dim, pairs),
    )(*operands)


def finalize_kernel(own_k_ref, own_v_ref, back_k_ref, back_v_ref, digest_ref, select_ref, k_out, v_out):
    hd = back_k_ref.shape[1]
    pick = select_ref[0]
    for own_ref, back_ref, side, out_ref in (
        (own_k_ref, back_k_ref, 0, k_out),
        (own_v_ref, back_v_ref, 1, v_out),
    ):
        out_ref[:, :hd] = (own_ref[:, :hd] + back_ref[...].astype(jnp.float32)).astype(out_ref.dtype)
        summary = tn(pick, digest_ref[side])
        out_ref[:, hd:] = (own_ref[:, hd:] + summary).astype(out_ref.dtype)


def finalize(own_k, own_v, back_k, back_v, digest, select, head_pairs, head_dim):
    rows = own_k.shape[0]
    digest_rows = digest.shape[1]
    wide = pl.BlockSpec((rows, 2 * head_dim), lambda p: (0, p))
    narrow = pl.BlockSpec((rows, head_dim), lambda p: (0, p))
    return pl.pallas_call(
        finalize_kernel,
        grid=(head_pairs,),
        in_specs=[
            wide,
            wide,
            narrow,
            narrow,
            pl.BlockSpec((2, digest_rows, head_dim), lambda p: (0, 0, p)),
            pl.BlockSpec((1, digest_rows, rows), lambda p: (p, 0, 0)),
        ],
        out_specs=[wide, wide],
        out_shape=[jax.ShapeDtypeStruct(own_k.shape, jnp.bfloat16)] * 2,
        cost_estimate=pl.CostEstimate(
            flops=4 * rows * digest_rows * head_dim * head_pairs,
            transcendentals=0,
            bytes_accessed=rows * head_dim * head_pairs * 20,
        ),
    )(own_k, own_v, back_k, back_v, digest, select)


def on_device(queries, keys, values, out_weight, cotangent, offsets):
    seq_rows = queries.shape[0]
    full_width = queries.shape[1]
    head_pairs = offsets.shape[0]
    head_dim = full_width // (2 * head_pairs)
    score_scale = head_dim ** (-0.5)
    assert seq_rows == WIN and seq_rows % BLOCK == 0
    seq_index = lax.axis_index("seq")
    split_k = keys.reshape(seq_rows, head_pairs, 2, head_dim)
    split_v = values.reshape(seq_rows, head_pairs, 2, head_dim)
    fixed_k = split_k[:, :, 1]
    fixed_v = split_v[:, :, 1]
    prev_k, prev_v = passed_along((keys, values), "seq", 1)
    digest_count = seq_rows // BLOCK * SUMM
    offset_table = jnp.tile(offsets.T, (seq_rows // BLOCK, 1))
    digest_rows = (jnp.arange(digest_count, dtype=jnp.int32) // SUMM * BLOCK)[
        :, None
    ] + offset_table
    select = (
        digest_rows.T[:, :, None] == jnp.arange(seq_rows, dtype=jnp.int32)[None, None, :]
    ).astype(jnp.bfloat16)
    digest_k = jnp.einsum(
        "hjr,rhc->jhc", select, fixed_k, preferred_element_type=jnp.float32
    ).astype(jnp.bfloat16)
    digest_v = jnp.einsum(
        "hjr,rhc->jhc", select, fixed_v, preferred_element_type=jnp.float32
    ).astype(jnp.bfloat16)
    pair_width = head_pairs * head_dim
    far_kv = lax.all_gather(
        jnp.concatenate(
            [
                digest_k.reshape(digest_count, pair_width),
                digest_v.reshape(digest_count, pair_width),
            ],
            1,
        ),
        "seq",
        axis=0,
        tiled=True,
    )
    head_count = lax.axis_size("head")
    head_index = lax.axis_index("head")
    pieces = [cotangent] + [
        lax.ppermute(
            cotangent, "head", [(source, (source + shift) % head_count) for source in range(head_count)]
        )
        for shift in range(1, head_count)
    ]
    doubled = jnp.stack(pieces[::-1] + pieces[::-1], 0)
    gathered = lax.dynamic_slice_in_dim(doubled, head_count - 1 - head_index, head_count, 0)
    grad_out = lax.dot_general(
        gathered.reshape(seq_rows, cotangent.shape[1]),
        out_weight,
        (((1,), (1,)), ((), ())),
        preferred_element_type=jnp.float32,
    ).astype(jnp.bfloat16)
    seq_scalar = seq_index.reshape(1).astype(jnp.int32)
    attention, query_grad, own_dk, own_dv, back_k, back_v = band_attention(
        seq_scalar, queries, keys, values, grad_out, prev_k, prev_v, head_pairs, head_dim, score_scale
    )
    chunks = 2 if head_pairs % 2 == 0 else 1
    pairs = head_pairs // chunks
    outputs = (attention, query_grad, own_dk, own_dv)
    digests = []
    for chunk in range(chunks):
        *outputs, far_dkv = fixed_attention(
            seq_scalar,
            queries,
            keys,
            values,
            grad_out,
            far_kv,
            chunk * pairs,
            pairs,
            head_pairs,
            head_dim,
            score_scale,
            outputs,
        )
        digests.append(seq_reduce_scatter(far_dkv, 1, chunk))
    attention, query_grad, own_dk, own_dv = outputs
    back_k, back_v = passed_along((back_k, back_v), "seq", -1)
    digest_dkv = jnp.concatenate(digests, 2) if chunks > 1 else digests[0]
    key_grad, value_grad = finalize(
        own_dk, own_dv, back_k, back_v, digest_dkv, select, head_pairs, head_dim
    )
    return attention, query_grad, key_grad, value_grad


def solution(mesh):
    in_specs = (
        P("seq", "head"),
        P("seq", "head"),
        P("seq", "head"),
        P("head", None),
        P(("seq", "head"), None),
        P("head", None),
    )
    out_specs = (P("seq", "head"), P("seq", "head"), P("seq", "head"), P("seq", "head"))
    return jax.shard_map(
        on_device, mesh=mesh, in_specs=in_specs, out_specs=out_specs, check_vma=False
    )
```

```python
import functools

import jax
import jax.numpy as jnp
from jax import lax
from jax.experimental import pallas as pl
from jax.experimental.pallas import tpu as pltpu
from jax.sharding import PartitionSpec as P

WIN = 256
BLOCK = 128
SUMM = 32


NEG = -1e30


def passed_along(value, axis, steps):
    count = lax.axis_size(axis)
    first, last = (max(0, -steps), min(count, count - steps))
    return lax.ppermute(value, axis, [(source, source + steps) for source in range(first, last)])


def seq_reduce_scatter(parts, axis, rotate=0):
    count = lax.axis_size("seq")
    if count & (count - 1):
        return lax.psum_scatter(
            parts.astype(jnp.bfloat16), "seq", scatter_dimension=axis, tiled=True
        )
    me = lax.axis_index("seq")
    bits = count.bit_length() - 1
    chunk = parts.shape[axis] // count
    held = parts.reshape(parts.shape[:axis] + (2,) * bits + (chunk,) + parts.shape[axis + 1 :])
    if bits > 2:
        order = [0] + sorted(range(1, bits - 1), key=lambda b: (b - 1 - rotate) % (bits - 2)) + [bits - 1]
    else:
        order = list(range(bits))
    gone = []
    for bit in order:
        where = axis + bits - 1 - bit - sum(1 for done in gone if done > bit)
        gone.append(bit)
        mine = (me >> bit) & 1
        keep = lax.dynamic_index_in_dim(held, mine, where, keepdims=False)
        send = lax.dynamic_index_in_dim(held, 1 - mine, where, keepdims=False)
        arrived = lax.ppermute(
            send.astype(jnp.bfloat16), "seq", [(source, source ^ (1 << bit)) for source in range(count)]
        )
        held = keep + arrived.astype(jnp.float32)
    return held.astype(jnp.bfloat16)


def nt(left, right):
    return lax.dot_general(left, right, (((1,), (1,)), ((), ())), preferred_element_type=jnp.float32)


def tn(left, right):
    return lax.dot_general(left, right, (((0,), (0,)), ((), ())), preferred_element_type=jnp.float32)


def nn(left, right):
    return lax.dot_general(left, right, (((1,), (0,)), ((), ())), preferred_element_type=jnp.float32)


def two_part_attention(q, g, first, second, scale):
    (k_a, v_a, mask_a), (k_b, v_b, mask_b) = first, second
    s_a = jnp.where(mask_a, nt(q, k_a) * scale, NEG)
    s_b = jnp.where(mask_b, nt(q, k_b) * scale, NEG)
    row_max = jnp.maximum(s_a.max(-1, keepdims=True), s_b.max(-1, keepdims=True))
    w_a = jnp.exp(s_a - row_max)
    w_b = jnp.exp(s_b - row_max)
    row_sum = w_a.sum(-1, keepdims=True) + w_b.sum(-1, keepdims=True)
    mixed = nn(w_a.astype(jnp.bfloat16), v_a) + nn(w_b.astype(jnp.bfloat16), v_b)
    out = (mixed / row_sum).astype(jnp.bfloat16)
    log_total = row_max + jnp.log(row_sum)
    delta = jnp.sum(g.astype(jnp.float32) * out.astype(jnp.float32), -1, keepdims=True)
    p_a = jnp.exp(s_a - log_total)
    p_b = jnp.exp(s_b - log_total)
    gs_a = (p_a * (nt(g, v_a) - delta)).astype(jnp.bfloat16)
    gs_b = (p_b * (nt(g, v_b) - delta)).astype(jnp.bfloat16)
    dq = ((nn(gs_a, k_a) + nn(gs_b, k_b)) * scale).astype(jnp.bfloat16)
    dk_a = tn(gs_a, q) * scale
    dk_b = tn(gs_b, q) * scale
    dv_a = tn(p_a.astype(jnp.bfloat16), g)
    dv_b = tn(p_b.astype(jnp.bfloat16), g)
    return out, dq, (dk_a, dv_a), (dk_b, dv_b)


def band_kernel(seq_ref, q_ref, k_ref, v_ref, g_ref, kp_ref, vp_ref, out_ref, dq_ref, dk_ref, dv_ref, dkp_ref, dvp_ref, *, scale):
    rows = q_ref.shape[0]
    qi = lax.broadcasted_iota(jnp.int32, (rows, rows), 0)
    kj = lax.broadcasted_iota(jnp.int32, (rows, rows), 1)
    prev_mask = (kj > qi) & (seq_ref[0] > 0)
    own_mask = (kj <= qi) & (qi - kj < WIN)
    out, dq, (dkp, dvp), (dko, dvo) = two_part_attention(
        q_ref[...],
        g_ref[...],
        (kp_ref[...], vp_ref[...], prev_mask),
        (k_ref[...], v_ref[...], own_mask),
        scale,
    )
    out_ref[...] = out
    dq_ref[...] = dq
    dk_ref[...] = dko
    dv_ref[...] = dvo
    dkp_ref[...] = dkp.astype(dkp_ref.dtype)
    dvp_ref[...] = dvp.astype(dvp_ref.dtype)


def fixed_kernel(seq_ref, q_ref, k_ref, v_ref, g_ref, kf_ref, vf_ref, *refs, scale, unused):
    out_ref, dq_ref, dk_ref, dv_ref, dkvf_ref = refs[unused:]
    rows = q_ref.shape[0]
    far_rows = kf_ref.shape[0]
    start = seq_ref[0] * rows
    qi = lax.broadcasted_iota(jnp.int32, (rows, rows), 0)
    kj = lax.broadcasted_iota(jnp.int32, (rows, rows), 1)
    own_mask = (kj <= qi) & ((qi // BLOCK) == (kj // BLOCK))
    fq = lax.broadcasted_iota(jnp.int32, (rows, far_rows), 0)
    fr = lax.broadcasted_iota(jnp.int32, (rows, far_rows), 1)
    far_mask = (fr // SUMM) < ((start + fq) // BLOCK)
    out, dq, (dko, dvo), (dkf, dvf) = two_part_attention(
        q_ref[...],
        g_ref[...],
        (k_ref[...], v_ref[...], own_mask),
        (kf_ref[...], vf_ref[...], far_mask),
        scale,
    )
    out_ref[...] = out
    dq_ref[...] = dq
    dk_ref[...] = dko
    dv_ref[...] = dvo
    dkvf_ref[0] = dkf
    dkvf_ref[1] = dvf


def attention_cost(rows, keys, head_dim, heads):
    return pl.CostEstimate(
        flops=2 * rows * keys * head_dim * 7 * heads,
        transcendentals=3 * rows * keys * heads,
        bytes_accessed=(rows * 16 + keys * 6) * head_dim * heads,
    )


def band_attention(seq_index, q, k, v, g, k_prev, v_prev, head_pairs, head_dim, scale):
    rows = q.shape[0]
    block = pl.BlockSpec((rows, head_dim), lambda p, s: (0, 2 * p))
    narrow = pl.BlockSpec((rows, head_dim), lambda p, s: (0, p))
    width = 2 * head_pairs * head_dim
    grid_spec = pltpu.PrefetchScalarGridSpec(
        num_scalar_prefetch=1,
        grid=(head_pairs,),
        in_specs=[block] * 6,
        out_specs=[block] * 4 + [narrow] * 2,
    )
    return pl.pallas_call(
        functools.partial(band_kernel, scale=scale),
        grid_spec=grid_spec,
        out_shape=[
            jax.ShapeDtypeStruct((rows, width), jnp.bfloat16),
            jax.ShapeDtypeStruct((rows, width), jnp.bfloat16),
            jax.ShapeDtypeStruct((rows, width), jnp.float32),
            jax.ShapeDtypeStruct((rows, width), jnp.float32),
            jax.ShapeDtypeStruct((rows, head_pairs * head_dim), jnp.bfloat16),
            jax.ShapeDtypeStruct((rows, head_pairs * head_dim), jnp.bfloat16),
        ],
        compiler_params=pltpu.CompilerParams(vmem_limit_bytes=48 * 1024 * 1024),
        cost_estimate=attention_cost(rows, 2 * rows, head_dim, head_pairs),
    )(seq_index, q, k, v, g, k_prev, v_prev)


def fixed_attention(seq_index, q, k, v, g, far_kv, first_pair, pairs, head_pairs, head_dim, scale, earlier):
    rows = q.shape[0]
    far_rows = far_kv.shape[0]
    block = pl.BlockSpec((rows, head_dim), lambda p, s: (0, 2 * (first_pair + p) + 1))
    far_k_spec = pl.BlockSpec((far_rows, head_dim), lambda p, s: (0, first_pair + p))
    far_v_spec = pl.BlockSpec((far_rows, head_dim), lambda p, s: (0, head_pairs + first_pair + p))
    operands = [seq_index, q, k, v, g, far_kv, far_kv] + list(earlier)
    aliases = {7 + number: number for number in range(len(earlier))}
    grid_spec = pltpu.PrefetchScalarGridSpec(
        num_scalar_prefetch=1,
        grid=(pairs,),
        in_specs=[block] * 4 + [far_k_spec, far_v_spec]
        + [pl.BlockSpec(memory_space=pl.ANY)] * len(earlier),
        out_specs=[block] * 4 + [pl.BlockSpec((2, far_rows, head_dim), lambda p, s: (0, 0, p))],
    )
    return pl.pallas_call(
        functools.partial(fixed_kernel, scale=scale, unused=len(earlier)),
        grid_spec=grid_spec,
        out_shape=[jax.ShapeDtypeStruct(array.shape, array.dtype) for array in earlier]
        + [jax.ShapeDtypeStruct((2, far_rows, pairs * head_dim), jnp.float32)],
        input_output_aliases=aliases,
        compiler_params=pltpu.CompilerParams(vmem_limit_bytes=48 * 1024 * 1024),
        cost_estimate=attention_cost(rows, rows + far_rows, head_dim, pairs),
    )(*operands)


def finalize_kernel(own_k_ref, own_v_ref, back_k_ref, back_v_ref, digest_ref, select_ref, k_out, v_out):
    hd = back_k_ref.shape[1]
    pick = select_ref[0]
    for own_ref, back_ref, side, out_ref in (
        (own_k_ref, back_k_ref, 0, k_out),
        (own_v_ref, back_v_ref, 1, v_out),
    ):
        out_ref[:, :hd] = (own_ref[:, :hd] + back_ref[...].astype(jnp.float32)).astype(out_ref.dtype)
        summary = tn(pick, digest_ref[side])
        out_ref[:, hd:] = (own_ref[:, hd:] + summary).astype(out_ref.dtype)


def finalize(own_k, own_v, back_k, back_v, digest, select, head_pairs, head_dim):
    rows = own_k.shape[0]
    digest_rows = digest.shape[1]
    wide = pl.BlockSpec((rows, 2 * head_dim), lambda p: (0, p))
    narrow = pl.BlockSpec((rows, head_dim), lambda p: (0, p))
    return pl.pallas_call(
        finalize_kernel,
        grid=(head_pairs,),
        in_specs=[
            wide,
            wide,
            narrow,
            narrow,
            pl.BlockSpec((2, digest_rows, head_dim), lambda p: (0, 0, p)),
            pl.BlockSpec((1, digest_rows, rows), lambda p: (p, 0, 0)),
        ],
        out_specs=[wide, wide],
        out_shape=[jax.ShapeDtypeStruct(own_k.shape, jnp.bfloat16)] * 2,
        cost_estimate=pl.CostEstimate(
            flops=4 * rows * digest_rows * head_dim * head_pairs,
            transcendentals=0,
            bytes_accessed=rows * head_dim * head_pairs * 20,
        ),
    )(own_k, own_v, back_k, back_v, digest, select)


def on_device(queries, keys, values, out_weight, cotangent, offsets):
    seq_rows = queries.shape[0]
    full_width = queries.shape[1]
    head_pairs = offsets.shape[0]
    head_dim = full_width // (2 * head_pairs)
    score_scale = head_dim ** (-0.5)
    assert seq_rows == WIN and seq_rows % BLOCK == 0
    seq_index = lax.axis_index("seq")
    split_k = keys.reshape(seq_rows, head_pairs, 2, head_dim)
    split_v = values.reshape(seq_rows, head_pairs, 2, head_dim)
    fixed_k = split_k[:, :, 1]
    fixed_v = split_v[:, :, 1]
    prev_k, prev_v = passed_along((keys, values), "seq", 1)
    digest_count = seq_rows // BLOCK * SUMM
    offset_table = jnp.tile(offsets.T, (seq_rows // BLOCK, 1))
    digest_rows = (jnp.arange(digest_count, dtype=jnp.int32) // SUMM * BLOCK)[
        :, None
    ] + offset_table
    select = (
        digest_rows.T[:, :, None] == jnp.arange(seq_rows, dtype=jnp.int32)[None, None, :]
    ).astype(jnp.bfloat16)
    digest_k = jnp.einsum(
        "hjr,rhc->jhc", select, fixed_k, preferred_element_type=jnp.float32
    ).astype(jnp.bfloat16)
    digest_v = jnp.einsum(
        "hjr,rhc->jhc", select, fixed_v, preferred_element_type=jnp.float32
    ).astype(jnp.bfloat16)
    pair_width = head_pairs * head_dim
    far_kv = lax.all_gather(
        jnp.concatenate(
            [
                digest_k.reshape(digest_count, pair_width),
                digest_v.reshape(digest_count, pair_width),
            ],
            1,
        ),
        "seq",
        axis=0,
        tiled=True,
    )
    head_count = lax.axis_size("head")
    head_index = lax.axis_index("head")
    pieces = [cotangent] + [
        lax.ppermute(
            cotangent, "head", [(source, (source + shift) % head_count) for source in range(head_count)]
        )
        for shift in range(1, head_count)
    ]
    doubled = jnp.stack(pieces[::-1] + pieces[::-1], 0)
    gathered = lax.dynamic_slice_in_dim(doubled, head_count - 1 - head_index, head_count, 0)
    grad_out = lax.dot_general(
        gathered.reshape(seq_rows, cotangent.shape[1]),
        out_weight,
        (((1,), (1,)), ((), ())),
        preferred_element_type=jnp.float32,
    ).astype(jnp.bfloat16)
    seq_scalar = seq_index.reshape(1).astype(jnp.int32)
    attention, query_grad, own_dk, own_dv, back_k, back_v = band_attention(
        seq_scalar, queries, keys, values, grad_out, prev_k, prev_v, head_pairs, head_dim, score_scale
    )
    chunks = 4 if head_pairs % 4 == 0 else (2 if head_pairs % 2 == 0 else 1)
    pairs = head_pairs // chunks
    outputs = (attention, query_grad, own_dk, own_dv)
    digests = []
    for chunk in range(chunks):
        *outputs, far_dkv = fixed_attention(
            seq_scalar,
            queries,
            keys,
            values,
            grad_out,
            far_kv,
            chunk * pairs,
            pairs,
            head_pairs,
            head_dim,
            score_scale,
            outputs,
        )
        digests.append(seq_reduce_scatter(far_dkv, 1, chunk))
    attention, query_grad, own_dk, own_dv = outputs
    back_k, back_v = passed_along((back_k, back_v), "seq", -1)
    digest_dkv = jnp.concatenate(digests, 2) if chunks > 1 else digests[0]
    key_grad, value_grad = finalize(
        own_dk, own_dv, back_k, back_v, digest_dkv, select, head_pairs, head_dim
    )
    return attention, query_grad, key_grad, value_grad


def solution(mesh):
    in_specs = (
        P("seq", "head"),
        P("seq", "head"),
        P("seq", "head"),
        P("head", None),
        P(("seq", "head"), None),
        P("head", None),
    )
    out_specs = (P("seq", "head"), P("seq", "head"), P("seq", "head"), P("seq", "head"))
    return jax.shard_map(
        on_device, mesh=mesh, in_specs=in_specs, out_specs=out_specs, check_vma=False
    )
```

```python
import functools

import jax
import jax.numpy as jnp
from jax import lax
from jax.experimental import pallas as pl
from jax.experimental.pallas import tpu as pltpu
from jax.sharding import PartitionSpec as P

WIN = 256
BLOCK = 128
SUMM = 32


NEG = -1e30


def passed_along(value, axis, steps):
    count = lax.axis_size(axis)
    first, last = (max(0, -steps), min(count, count - steps))
    return lax.ppermute(value, axis, [(source, source + steps) for source in range(first, last)])


def seq_reduce_scatter(parts, axis, rotate=0):
    count = lax.axis_size("seq")
    if count & (count - 1):
        return lax.psum_scatter(
            parts.astype(jnp.bfloat16), "seq", scatter_dimension=axis, tiled=True
        )
    me = lax.axis_index("seq")
    bits = count.bit_length() - 1
    chunk = parts.shape[axis] // count
    held = parts.reshape(parts.shape[:axis] + (2,) * bits + (chunk,) + parts.shape[axis + 1 :])
    if bits > 2:
        order = [0] + sorted(range(1, bits - 1), key=lambda b: (b - 1 - rotate) % (bits - 2)) + [bits - 1]
    else:
        order = list(range(bits))
    gone = []
    for bit in order:
        where = axis + bits - 1 - bit - sum(1 for done in gone if done > bit)
        gone.append(bit)
        mine = (me >> bit) & 1
        keep = lax.dynamic_index_in_dim(held, mine, where, keepdims=False)
        send = lax.dynamic_index_in_dim(held, 1 - mine, where, keepdims=False)
        arrived = lax.ppermute(
            send.astype(jnp.bfloat16), "seq", [(source, source ^ (1 << bit)) for source in range(count)]
        )
        held = keep + arrived.astype(jnp.float32)
    return held.astype(jnp.bfloat16)


def nt(left, right):
    return lax.dot_general(left, right, (((1,), (1,)), ((), ())), preferred_element_type=jnp.float32)


def tn(left, right):
    return lax.dot_general(left, right, (((0,), (0,)), ((), ())), preferred_element_type=jnp.float32)


def nn(left, right):
    return lax.dot_general(left, right, (((1,), (0,)), ((), ())), preferred_element_type=jnp.float32)


def two_part_attention(q, g, first, second, scale):
    (k_a, v_a, mask_a), (k_b, v_b, mask_b) = first, second
    s_a = jnp.where(mask_a, nt(q, k_a) * scale, NEG)
    s_b = jnp.where(mask_b, nt(q, k_b) * scale, NEG)
    row_max = jnp.maximum(s_a.max(-1, keepdims=True), s_b.max(-1, keepdims=True))
    w_a = jnp.exp(s_a - row_max)
    w_b = jnp.exp(s_b - row_max)
    row_sum = w_a.sum(-1, keepdims=True) + w_b.sum(-1, keepdims=True)
    mixed = nn(w_a.astype(jnp.bfloat16), v_a) + nn(w_b.astype(jnp.bfloat16), v_b)
    out = (mixed / row_sum).astype(jnp.bfloat16)
    log_total = row_max + jnp.log(row_sum)
    delta = jnp.sum(g.astype(jnp.float32) * out.astype(jnp.float32), -1, keepdims=True)
    p_a = jnp.exp(s_a - log_total)
    p_b = jnp.exp(s_b - log_total)
    gs_a = (p_a * (nt(g, v_a) - delta)).astype(jnp.bfloat16)
    gs_b = (p_b * (nt(g, v_b) - delta)).astype(jnp.bfloat16)
    dq = ((nn(gs_a, k_a) + nn(gs_b, k_b)) * scale).astype(jnp.bfloat16)
    dk_a = tn(gs_a, q) * scale
    dk_b = tn(gs_b, q) * scale
    dv_a = tn(p_a.astype(jnp.bfloat16), g)
    dv_b = tn(p_b.astype(jnp.bfloat16), g)
    return out, dq, (dk_a, dv_a), (dk_b, dv_b)


def band_kernel(seq_ref, q_ref, k_ref, v_ref, g_ref, kp_ref, vp_ref, out_ref, dq_ref, dk_ref, dv_ref, dkp_ref, dvp_ref, *, scale):
    rows = q_ref.shape[0]
    qi = lax.broadcasted_iota(jnp.int32, (rows, rows), 0)
    kj = lax.broadcasted_iota(jnp.int32, (rows, rows), 1)
    prev_mask = (kj > qi) & (seq_ref[0] > 0)
    own_mask = (kj <= qi) & (qi - kj < WIN)
    out, dq, (dkp, dvp), (dko, dvo) = two_part_attention(
        q_ref[...],
        g_ref[...],
        (kp_ref[...], vp_ref[...], prev_mask),
        (k_ref[...], v_ref[...], own_mask),
        scale,
    )
    out_ref[...] = out
    dq_ref[...] = dq
    dk_ref[...] = dko
    dv_ref[...] = dvo
    dkp_ref[...] = dkp.astype(dkp_ref.dtype)
    dvp_ref[...] = dvp.astype(dvp_ref.dtype)


def fixed_kernel(seq_ref, q_ref, k_ref, v_ref, g_ref, kf_ref, vf_ref, *refs, scale, unused):
    out_ref, dq_ref, dk_ref, dv_ref, dkvf_ref = refs[unused:]
    rows = q_ref.shape[0]
    far_rows = kf_ref.shape[0]
    start = seq_ref[0] * rows
    qi = lax.broadcasted_iota(jnp.int32, (rows, rows), 0)
    kj = lax.broadcasted_iota(jnp.int32, (rows, rows), 1)
    own_mask = (kj <= qi) & ((qi // BLOCK) == (kj // BLOCK))
    fq = lax.broadcasted_iota(jnp.int32, (rows, far_rows), 0)
    fr = lax.broadcasted_iota(jnp.int32, (rows, far_rows), 1)
    far_mask = (fr // SUMM) < ((start + fq) // BLOCK)
    out, dq, (dko, dvo), (dkf, dvf) = two_part_attention(
        q_ref[...],
        g_ref[...],
        (k_ref[...], v_ref[...], own_mask),
        (kf_ref[...], vf_ref[...], far_mask),
        scale,
    )
    out_ref[...] = out
    dq_ref[...] = dq
    dk_ref[...] = dko
    dv_ref[...] = dvo
    dkvf_ref[0] = dkf
    dkvf_ref[1] = dvf


def attention_cost(rows, keys, head_dim, heads):
    return pl.CostEstimate(
        flops=2 * rows * keys * head_dim * 7 * heads,
        transcendentals=3 * rows * keys * heads,
        bytes_accessed=(rows * 16 + keys * 6) * head_dim * heads,
    )


def band_attention(seq_index, q, k, v, g, k_prev, v_prev, head_pairs, head_dim, scale):
    rows = q.shape[0]
    block = pl.BlockSpec((rows, head_dim), lambda p, s: (0, 2 * p))
    narrow = pl.BlockSpec((rows, head_dim), lambda p, s: (0, p))
    width = 2 * head_pairs * head_dim
    grid_spec = pltpu.PrefetchScalarGridSpec(
        num_scalar_prefetch=1,
        grid=(head_pairs,),
        in_specs=[block] * 6,
        out_specs=[block] * 4 + [narrow] * 2,
    )
    return pl.pallas_call(
        functools.partial(band_kernel, scale=scale),
        grid_spec=grid_spec,
        out_shape=[
            jax.ShapeDtypeStruct((rows, width), jnp.bfloat16),
            jax.ShapeDtypeStruct((rows, width), jnp.bfloat16),
            jax.ShapeDtypeStruct((rows, width), jnp.float32),
            jax.ShapeDtypeStruct((rows, width), jnp.float32),
            jax.ShapeDtypeStruct((rows, head_pairs * head_dim), jnp.bfloat16),
            jax.ShapeDtypeStruct((rows, head_pairs * head_dim), jnp.bfloat16),
        ],
        compiler_params=pltpu.CompilerParams(vmem_limit_bytes=48 * 1024 * 1024),
        cost_estimate=attention_cost(rows, 2 * rows, head_dim, head_pairs),
    )(seq_index, q, k, v, g, k_prev, v_prev)


def fixed_attention(seq_index, q, k, v, g, far_kv, first_pair, pairs, head_pairs, head_dim, scale, earlier):
    rows = q.shape[0]
    far_rows = far_kv.shape[0]
    block = pl.BlockSpec((rows, head_dim), lambda p, s: (0, 2 * (first_pair + p) + 1))
    far_k_spec = pl.BlockSpec((far_rows, head_dim), lambda p, s: (0, first_pair + p))
    far_v_spec = pl.BlockSpec((far_rows, head_dim), lambda p, s: (0, head_pairs + first_pair + p))
    operands = [seq_index, q, k, v, g, far_kv, far_kv] + list(earlier)
    aliases = {7 + number: number for number in range(len(earlier))}
    grid_spec = pltpu.PrefetchScalarGridSpec(
        num_scalar_prefetch=1,
        grid=(pairs,),
        in_specs=[block] * 4 + [far_k_spec, far_v_spec]
        + [pl.BlockSpec(memory_space=pl.ANY)] * len(earlier),
        out_specs=[block] * 4 + [pl.BlockSpec((2, far_rows, head_dim), lambda p, s: (0, 0, p))],
    )
    return pl.pallas_call(
        functools.partial(fixed_kernel, scale=scale, unused=len(earlier)),
        grid_spec=grid_spec,
        out_shape=[jax.ShapeDtypeStruct(array.shape, array.dtype) for array in earlier]
        + [jax.ShapeDtypeStruct((2, far_rows, pairs * head_dim), jnp.float32)],
        input_output_aliases=aliases,
        compiler_params=pltpu.CompilerParams(vmem_limit_bytes=48 * 1024 * 1024),
        cost_estimate=attention_cost(rows, rows + far_rows, head_dim, pairs),
    )(*operands)


def finalize_kernel(own_k_ref, own_v_ref, back_k_ref, back_v_ref, digest_ref, select_ref, k_out, v_out):
    hd = back_k_ref.shape[1]
    pick = select_ref[0]
    for own_ref, back_ref, side, out_ref in (
        (own_k_ref, back_k_ref, 0, k_out),
        (own_v_ref, back_v_ref, 1, v_out),
    ):
        out_ref[:, :hd] = (own_ref[:, :hd] + back_ref[...].astype(jnp.float32)).astype(out_ref.dtype)
        summary = tn(pick, digest_ref[side])
        out_ref[:, hd:] = (own_ref[:, hd:] + summary).astype(out_ref.dtype)


def finalize(own_k, own_v, back_k, back_v, digest, select, head_pairs, head_dim):
    rows = own_k.shape[0]
    digest_rows = digest.shape[1]
    wide = pl.BlockSpec((rows, 2 * head_dim), lambda p: (0, p))
    narrow = pl.BlockSpec((rows, head_dim), lambda p: (0, p))
    return pl.pallas_call(
        finalize_kernel,
        grid=(head_pairs,),
        in_specs=[
            wide,
            wide,
            narrow,
            narrow,
            pl.BlockSpec((2, digest_rows, head_dim), lambda p: (0, 0, p)),
            pl.BlockSpec((1, digest_rows, rows), lambda p: (p, 0, 0)),
        ],
        out_specs=[wide, wide],
        out_shape=[jax.ShapeDtypeStruct(own_k.shape, jnp.bfloat16)] * 2,
        cost_estimate=pl.CostEstimate(
            flops=4 * rows * digest_rows * head_dim * head_pairs,
            transcendentals=0,
            bytes_accessed=rows * head_dim * head_pairs * 20,
        ),
    )(own_k, own_v, back_k, back_v, digest, select)


def on_device(queries, keys, values, out_weight, cotangent, offsets):
    seq_rows = queries.shape[0]
    full_width = queries.shape[1]
    head_pairs = offsets.shape[0]
    head_dim = full_width // (2 * head_pairs)
    score_scale = head_dim ** (-0.5)
    assert seq_rows == WIN and seq_rows % BLOCK == 0
    seq_index = lax.axis_index("seq")
    split_k = keys.reshape(seq_rows, head_pairs, 2, head_dim)
    split_v = values.reshape(seq_rows, head_pairs, 2, head_dim)
    fixed_k = split_k[:, :, 1]
    fixed_v = split_v[:, :, 1]
    prev_k, prev_v = passed_along((keys, values), "seq", 1)
    digest_count = seq_rows // BLOCK * SUMM
    offset_table = jnp.tile(offsets.T, (seq_rows // BLOCK, 1))
    digest_rows = (jnp.arange(digest_count, dtype=jnp.int32) // SUMM * BLOCK)[
        :, None
    ] + offset_table
    select = (
        digest_rows.T[:, :, None] == jnp.arange(seq_rows, dtype=jnp.int32)[None, None, :]
    ).astype(jnp.bfloat16)
    digest_k = jnp.einsum(
        "hjr,rhc->jhc", select, fixed_k, preferred_element_type=jnp.float32
    ).astype(jnp.bfloat16)
    digest_v = jnp.einsum(
        "hjr,rhc->jhc", select, fixed_v, preferred_element_type=jnp.float32
    ).astype(jnp.bfloat16)
    pair_width = head_pairs * head_dim
    far_kv = lax.all_gather(
        jnp.concatenate(
            [
                digest_k.reshape(digest_count, pair_width),
                digest_v.reshape(digest_count, pair_width),
            ],
            1,
        ),
        "seq",
        axis=0,
        tiled=True,
    )
    head_count = lax.axis_size("head")
    head_index = lax.axis_index("head")
    pieces = [cotangent] + [
        lax.ppermute(
            cotangent, "head", [(source, (source + shift) % head_count) for source in range(head_count)]
        )
        for shift in range(1, head_count)
    ]
    doubled = jnp.stack(pieces[::-1] + pieces[::-1], 0)
    gathered = lax.dynamic_slice_in_dim(doubled, head_count - 1 - head_index, head_count, 0)
    grad_out = lax.dot_general(
        gathered.reshape(seq_rows, cotangent.shape[1]),
        out_weight,
        (((1,), (1,)), ((), ())),
        preferred_element_type=jnp.float32,
    ).astype(jnp.bfloat16)
    seq_scalar = seq_index.reshape(1).astype(jnp.int32)
    attention, query_grad, own_dk, own_dv, back_k, back_v = band_attention(
        seq_scalar, queries, keys, values, grad_out, prev_k, prev_v, head_pairs, head_dim, score_scale
    )
    chunks = 4 if head_pairs % 4 == 0 else (2 if head_pairs % 2 == 0 else 1)
    pairs = head_pairs // chunks
    outputs = (attention, query_grad, own_dk, own_dv)
    digests = []
    for chunk in range(chunks):
        *outputs, far_dkv = fixed_attention(
            seq_scalar,
            queries,
            keys,
            values,
            grad_out,
            far_kv,
            chunk * pairs,
            pairs,
            head_pairs,
            head_dim,
            score_scale,
            outputs,
        )
        digests.append(seq_reduce_scatter(far_dkv, 1, chunk))
    attention, query_grad, own_dk, own_dv = outputs
    back_k, back_v, attention = lax.optimization_barrier((back_k, back_v, attention))
    back_k, back_v = passed_along((back_k, back_v), "seq", -1)
    digest_dkv = jnp.concatenate(digests, 2) if chunks > 1 else digests[0]
    key_grad, value_grad = finalize(
        own_dk, own_dv, back_k, back_v, digest_dkv, select, head_pairs, head_dim
    )
    return attention, query_grad, key_grad, value_grad


def solution(mesh):
    in_specs = (
        P("seq", "head"),
        P("seq", "head"),
        P("seq", "head"),
        P("head", None),
        P(("seq", "head"), None),
        P("head", None),
    )
    out_specs = (P("seq", "head"), P("seq", "head"), P("seq", "head"), P("seq", "head"))
    return jax.shard_map(
        on_device, mesh=mesh, in_specs=in_specs, out_specs=out_specs, check_vma=False
    )
```

```python
import functools

import jax
import jax.numpy as jnp
from jax import lax
from jax.experimental import pallas as pl
from jax.experimental.pallas import tpu as pltpu
from jax.sharding import PartitionSpec as P

WIN = 256
BLOCK = 128
SUMM = 32


NEG = -1e30


def passed_along(value, axis, steps):
    count = lax.axis_size(axis)
    first, last = (max(0, -steps), min(count, count - steps))
    return lax.ppermute(value, axis, [(source, source + steps) for source in range(first, last)])


def seq_reduce_scatter(parts, axis, rotate=0):
    count = lax.axis_size("seq")
    if count & (count - 1):
        return lax.psum_scatter(
            parts.astype(jnp.bfloat16), "seq", scatter_dimension=axis, tiled=True
        )
    me = lax.axis_index("seq")
    bits = count.bit_length() - 1
    chunk = parts.shape[axis] // count
    held = parts.reshape(parts.shape[:axis] + (2,) * bits + (chunk,) + parts.shape[axis + 1 :])
    if bits > 2:
        order = [0] + sorted(range(1, bits - 1), key=lambda b: (b - 1 - rotate) % (bits - 2)) + [bits - 1]
    else:
        order = list(range(bits))
    gone = []
    for bit in order:
        where = axis + bits - 1 - bit - sum(1 for done in gone if done > bit)
        gone.append(bit)
        mine = (me >> bit) & 1
        keep = lax.dynamic_index_in_dim(held, mine, where, keepdims=False)
        send = lax.dynamic_index_in_dim(held, 1 - mine, where, keepdims=False)
        arrived = lax.ppermute(
            send.astype(jnp.bfloat16), "seq", [(source, source ^ (1 << bit)) for source in range(count)]
        )
        held = keep + arrived.astype(jnp.float32)
    return held.astype(jnp.bfloat16)


def nt(left, right):
    return lax.dot_general(left, right, (((1,), (1,)), ((), ())), preferred_element_type=jnp.float32)


def tn(left, right):
    return lax.dot_general(left, right, (((0,), (0,)), ((), ())), preferred_element_type=jnp.float32)


def nn(left, right):
    return lax.dot_general(left, right, (((1,), (0,)), ((), ())), preferred_element_type=jnp.float32)


def two_part_attention(q, g, first, second, scale):
    (k_a, v_a, mask_a), (k_b, v_b, mask_b) = first, second
    s_a = jnp.where(mask_a, nt(q, k_a) * scale, NEG)
    s_b = jnp.where(mask_b, nt(q, k_b) * scale, NEG)
    row_max = jnp.maximum(s_a.max(-1, keepdims=True), s_b.max(-1, keepdims=True))
    w_a = jnp.exp(s_a - row_max)
    w_b = jnp.exp(s_b - row_max)
    row_sum = w_a.sum(-1, keepdims=True) + w_b.sum(-1, keepdims=True)
    mixed = nn(w_a.astype(jnp.bfloat16), v_a) + nn(w_b.astype(jnp.bfloat16), v_b)
    out = (mixed / row_sum).astype(jnp.bfloat16)
    log_total = row_max + jnp.log(row_sum)
    delta = jnp.sum(g.astype(jnp.float32) * out.astype(jnp.float32), -1, keepdims=True)
    p_a = jnp.exp(s_a - log_total)
    p_b = jnp.exp(s_b - log_total)
    gs_a = (p_a * (nt(g, v_a) - delta)).astype(jnp.bfloat16)
    gs_b = (p_b * (nt(g, v_b) - delta)).astype(jnp.bfloat16)
    dq = ((nn(gs_a, k_a) + nn(gs_b, k_b)) * scale).astype(jnp.bfloat16)
    dk_a = tn(gs_a, q) * scale
    dk_b = tn(gs_b, q) * scale
    dv_a = tn(p_a.astype(jnp.bfloat16), g)
    dv_b = tn(p_b.astype(jnp.bfloat16), g)
    return out, dq, (dk_a, dv_a), (dk_b, dv_b)


def band_kernel(seq_ref, q_ref, k_ref, v_ref, g_ref, kp_ref, vp_ref, out_ref, dq_ref, dk_ref, dv_ref, dkp_ref, dvp_ref, *, scale):
    rows = q_ref.shape[0]
    qi = lax.broadcasted_iota(jnp.int32, (rows, rows), 0)
    kj = lax.broadcasted_iota(jnp.int32, (rows, rows), 1)
    prev_mask = (kj > qi) & (seq_ref[0] > 0)
    own_mask = (kj <= qi) & (qi - kj < WIN)
    out, dq, (dkp, dvp), (dko, dvo) = two_part_attention(
        q_ref[...],
        g_ref[...],
        (kp_ref[...], vp_ref[...], prev_mask),
        (k_ref[...], v_ref[...], own_mask),
        scale,
    )
    out_ref[...] = out
    dq_ref[...] = dq
    dk_ref[...] = dko
    dv_ref[...] = dvo
    dkp_ref[...] = dkp.astype(dkp_ref.dtype)
    dvp_ref[...] = dvp.astype(dvp_ref.dtype)


def fixed_kernel(seq_ref, q_ref, k_ref, v_ref, g_ref, kf_ref, vf_ref, *refs, scale, unused):
    out_ref, dq_ref, dk_ref, dv_ref, dkvf_ref = refs[unused:]
    rows = q_ref.shape[0]
    far_rows = kf_ref.shape[0]
    start = seq_ref[0] * rows
    qi = lax.broadcasted_iota(jnp.int32, (rows, rows), 0)
    kj = lax.broadcasted_iota(jnp.int32, (rows, rows), 1)
    own_mask = (kj <= qi) & ((qi // BLOCK) == (kj // BLOCK))
    fq = lax.broadcasted_iota(jnp.int32, (rows, far_rows), 0)
    fr = lax.broadcasted_iota(jnp.int32, (rows, far_rows), 1)
    far_mask = (fr // SUMM) < ((start + fq) // BLOCK)
    out, dq, (dko, dvo), (dkf, dvf) = two_part_attention(
        q_ref[...],
        g_ref[...],
        (k_ref[...], v_ref[...], own_mask),
        (kf_ref[...], vf_ref[...], far_mask),
        scale,
    )
    out_ref[...] = out
    dq_ref[...] = dq
    dk_ref[...] = dko
    dv_ref[...] = dvo
    dkvf_ref[0] = dkf
    dkvf_ref[1] = dvf


def attention_cost(rows, keys, head_dim, heads):
    return pl.CostEstimate(
        flops=2 * rows * keys * head_dim * 7 * heads,
        transcendentals=3 * rows * keys * heads,
        bytes_accessed=(rows * 16 + keys * 6) * head_dim * heads,
    )


def band_attention(seq_index, q, k, v, g, k_prev, v_prev, head_pairs, head_dim, scale):
    rows = q.shape[0]
    block = pl.BlockSpec((rows, head_dim), lambda p, s: (0, 2 * p))
    narrow = pl.BlockSpec((rows, head_dim), lambda p, s: (0, p))
    width = 2 * head_pairs * head_dim
    grid_spec = pltpu.PrefetchScalarGridSpec(
        num_scalar_prefetch=1,
        grid=(head_pairs,),
        in_specs=[block] * 4 + [narrow] * 2,
        out_specs=[block] * 4 + [narrow] * 2,
    )
    return pl.pallas_call(
        functools.partial(band_kernel, scale=scale),
        grid_spec=grid_spec,
        out_shape=[
            jax.ShapeDtypeStruct((rows, width), jnp.bfloat16),
            jax.ShapeDtypeStruct((rows, width), jnp.bfloat16),
            jax.ShapeDtypeStruct((rows, width), jnp.float32),
            jax.ShapeDtypeStruct((rows, width), jnp.float32),
            jax.ShapeDtypeStruct((rows, head_pairs * head_dim), jnp.bfloat16),
            jax.ShapeDtypeStruct((rows, head_pairs * head_dim), jnp.bfloat16),
        ],
        compiler_params=pltpu.CompilerParams(vmem_limit_bytes=48 * 1024 * 1024),
        cost_estimate=attention_cost(rows, 2 * rows, head_dim, head_pairs),
    )(seq_index, q, k, v, g, k_prev, v_prev)


def fixed_attention(seq_index, q, k, v, g, far_kv, first_pair, pairs, head_pairs, head_dim, scale, earlier):
    rows = q.shape[0]
    far_rows = far_kv.shape[0]
    block = pl.BlockSpec((rows, head_dim), lambda p, s: (0, 2 * (first_pair + p) + 1))
    far_k_spec = pl.BlockSpec((far_rows, head_dim), lambda p, s: (0, first_pair + p))
    far_v_spec = pl.BlockSpec((far_rows, head_dim), lambda p, s: (0, head_pairs + first_pair + p))
    operands = [seq_index, q, k, v, g, far_kv, far_kv] + list(earlier)
    aliases = {7 + number: number for number in range(len(earlier))}
    grid_spec = pltpu.PrefetchScalarGridSpec(
        num_scalar_prefetch=1,
        grid=(pairs,),
        in_specs=[block] * 4 + [far_k_spec, far_v_spec]
        + [pl.BlockSpec(memory_space=pl.ANY)] * len(earlier),
        out_specs=[block] * 4 + [pl.BlockSpec((2, far_rows, head_dim), lambda p, s: (0, 0, p))],
    )
    return pl.pallas_call(
        functools.partial(fixed_kernel, scale=scale, unused=len(earlier)),
        grid_spec=grid_spec,
        out_shape=[jax.ShapeDtypeStruct(array.shape, array.dtype) for array in earlier]
        + [jax.ShapeDtypeStruct((2, far_rows, pairs * head_dim), jnp.float32)],
        input_output_aliases=aliases,
        compiler_params=pltpu.CompilerParams(vmem_limit_bytes=48 * 1024 * 1024),
        cost_estimate=attention_cost(rows, rows + far_rows, head_dim, pairs),
    )(*operands)


def finalize_kernel(own_k_ref, own_v_ref, back_k_ref, back_v_ref, digest_ref, select_ref, k_out, v_out):
    hd = back_k_ref.shape[1]
    pick = select_ref[0]
    for own_ref, back_ref, side, out_ref in (
        (own_k_ref, back_k_ref, 0, k_out),
        (own_v_ref, back_v_ref, 1, v_out),
    ):
        out_ref[:, :hd] = (own_ref[:, :hd] + back_ref[...].astype(jnp.float32)).astype(out_ref.dtype)
        summary = tn(pick, digest_ref[side])
        out_ref[:, hd:] = (own_ref[:, hd:] + summary).astype(out_ref.dtype)


def finalize(own_k, own_v, back_k, back_v, digest, select, head_pairs, head_dim):
    rows = own_k.shape[0]
    digest_rows = digest.shape[1]
    wide = pl.BlockSpec((rows, 2 * head_dim), lambda p: (0, p))
    narrow = pl.BlockSpec((rows, head_dim), lambda p: (0, p))
    return pl.pallas_call(
        finalize_kernel,
        grid=(head_pairs,),
        in_specs=[
            wide,
            wide,
            narrow,
            narrow,
            pl.BlockSpec((2, digest_rows, head_dim), lambda p: (0, 0, p)),
            pl.BlockSpec((1, digest_rows, rows), lambda p: (p, 0, 0)),
        ],
        out_specs=[wide, wide],
        out_shape=[jax.ShapeDtypeStruct(own_k.shape, jnp.bfloat16)] * 2,
        cost_estimate=pl.CostEstimate(
            flops=4 * rows * digest_rows * head_dim * head_pairs,
            transcendentals=0,
            bytes_accessed=rows * head_dim * head_pairs * 20,
        ),
    )(own_k, own_v, back_k, back_v, digest, select)


def on_device(queries, keys, values, out_weight, cotangent, offsets):
    seq_rows = queries.shape[0]
    full_width = queries.shape[1]
    head_pairs = offsets.shape[0]
    head_dim = full_width // (2 * head_pairs)
    score_scale = head_dim ** (-0.5)
    assert seq_rows == WIN and seq_rows % BLOCK == 0
    seq_index = lax.axis_index("seq")
    split_k = keys.reshape(seq_rows, head_pairs, 2, head_dim)
    split_v = values.reshape(seq_rows, head_pairs, 2, head_dim)
    fixed_k = split_k[:, :, 1]
    fixed_v = split_v[:, :, 1]
    band_k = split_k[:, :, 0].reshape(seq_rows, head_pairs * head_dim)
    band_v = split_v[:, :, 0].reshape(seq_rows, head_pairs * head_dim)
    prev_k, prev_v = passed_along((band_k, band_v), "seq", 1)
    digest_count = seq_rows // BLOCK * SUMM
    offset_table = jnp.tile(offsets.T, (seq_rows // BLOCK, 1))
    digest_rows = (jnp.arange(digest_count, dtype=jnp.int32) // SUMM * BLOCK)[
        :, None
    ] + offset_table
    select = (
        digest_rows.T[:, :, None] == jnp.arange(seq_rows, dtype=jnp.int32)[None, None, :]
    ).astype(jnp.bfloat16)
    digest_k = jnp.einsum(
        "hjr,rhc->jhc", select, fixed_k, preferred_element_type=jnp.float32
    ).astype(jnp.bfloat16)
    digest_v = jnp.einsum(
        "hjr,rhc->jhc", select, fixed_v, preferred_element_type=jnp.float32
    ).astype(jnp.bfloat16)
    pair_width = head_pairs * head_dim
    far_kv = lax.all_gather(
        jnp.concatenate(
            [
                digest_k.reshape(digest_count, pair_width),
                digest_v.reshape(digest_count, pair_width),
            ],
            1,
        ),
        "seq",
        axis=0,
        tiled=True,
    )
    head_count = lax.axis_size("head")
    head_index = lax.axis_index("head")
    pieces = [cotangent] + [
        lax.ppermute(
            cotangent, "head", [(source, (source + shift) % head_count) for source in range(head_count)]
        )
        for shift in range(1, head_count)
    ]
    doubled = jnp.stack(pieces[::-1] + pieces[::-1], 0)
    gathered = lax.dynamic_slice_in_dim(doubled, head_count - 1 - head_index, head_count, 0)
    grad_out = lax.dot_general(
        gathered.reshape(seq_rows, cotangent.shape[1]),
        out_weight,
        (((1,), (1,)), ((), ())),
        preferred_element_type=jnp.float32,
    ).astype(jnp.bfloat16)
    seq_scalar = seq_index.reshape(1).astype(jnp.int32)
    attention, query_grad, own_dk, own_dv, back_k, back_v = band_attention(
        seq_scalar, queries, keys, values, grad_out, prev_k, prev_v, head_pairs, head_dim, score_scale
    )
    chunks = 4 if head_pairs % 4 == 0 else (2 if head_pairs % 2 == 0 else 1)
    pairs = head_pairs // chunks
    outputs = (attention, query_grad, own_dk, own_dv)
    digests = []
    for chunk in range(chunks):
        *outputs, far_dkv = fixed_attention(
            seq_scalar,
            queries,
            keys,
            values,
            grad_out,
            far_kv,
            chunk * pairs,
            pairs,
            head_pairs,
            head_dim,
            score_scale,
            outputs,
        )
        digests.append(seq_reduce_scatter(far_dkv, 1, chunk))
    attention, query_grad, own_dk, own_dv = outputs
    back_k, back_v = passed_along((back_k, back_v), "seq", -1)
    digest_dkv = jnp.concatenate(digests, 2) if chunks > 1 else digests[0]
    key_grad, value_grad = finalize(
        own_dk, own_dv, back_k, back_v, digest_dkv, select, head_pairs, head_dim
    )
    return attention, query_grad, key_grad, value_grad


def solution(mesh):
    in_specs = (
        P("seq", "head"),
        P("seq", "head"),
        P("seq", "head"),
        P("head", None),
        P(("seq", "head"), None),
        P("head", None),
    )
    out_specs = (P("seq", "head"), P("seq", "head"), P("seq", "head"), P("seq", "head"))
    return jax.shard_map(
        on_device, mesh=mesh, in_specs=in_specs, out_specs=out_specs, check_vma=False
    )
```

```python
import functools

import jax
import jax.numpy as jnp
from jax import lax
from jax.experimental import pallas as pl
from jax.experimental.pallas import tpu as pltpu
from jax.sharding import PartitionSpec as P

WIN = 256
BLOCK = 128
SUMM = 32


NEG = -1e30


def passed_along(value, axis, steps):
    count = lax.axis_size(axis)
    first, last = (max(0, -steps), min(count, count - steps))
    return lax.ppermute(value, axis, [(source, source + steps) for source in range(first, last)])


def seq_reduce_scatter(parts, axis, rotate=0):
    count = lax.axis_size("seq")
    if count & (count - 1):
        return lax.psum_scatter(
            parts.astype(jnp.bfloat16), "seq", scatter_dimension=axis, tiled=True
        )
    me = lax.axis_index("seq")
    bits = count.bit_length() - 1
    chunk = parts.shape[axis] // count
    held = parts.reshape(parts.shape[:axis] + (2,) * bits + (chunk,) + parts.shape[axis + 1 :])
    if bits > 2:
        order = [0] + sorted(range(1, bits - 1), key=lambda b: (b - 1 - rotate) % (bits - 2)) + [bits - 1]
    else:
        order = list(range(bits))
    gone = []
    for bit in order:
        where = axis + bits - 1 - bit - sum(1 for done in gone if done > bit)
        gone.append(bit)
        mine = (me >> bit) & 1
        keep = lax.dynamic_index_in_dim(held, mine, where, keepdims=False)
        send = lax.dynamic_index_in_dim(held, 1 - mine, where, keepdims=False)
        arrived = lax.ppermute(
            send.astype(jnp.bfloat16), "seq", [(source, source ^ (1 << bit)) for source in range(count)]
        )
        held = keep + arrived.astype(jnp.float32)
    return held.astype(jnp.bfloat16)


def nt(left, right):
    return lax.dot_general(left, right, (((1,), (1,)), ((), ())), preferred_element_type=jnp.float32)


def tn(left, right):
    return lax.dot_general(left, right, (((0,), (0,)), ((), ())), preferred_element_type=jnp.float32)


def nn(left, right):
    return lax.dot_general(left, right, (((1,), (0,)), ((), ())), preferred_element_type=jnp.float32)


def two_part_attention(q, g, first, second, scale):
    (k_a, v_a, mask_a), (k_b, v_b, mask_b) = first, second
    s_a = jnp.where(mask_a, nt(q, k_a) * scale, NEG)
    s_b = jnp.where(mask_b, nt(q, k_b) * scale, NEG)
    row_max = jnp.maximum(s_a.max(-1, keepdims=True), s_b.max(-1, keepdims=True))
    w_a = jnp.exp(s_a - row_max)
    w_b = jnp.exp(s_b - row_max)
    row_sum = w_a.sum(-1, keepdims=True) + w_b.sum(-1, keepdims=True)
    mixed = nn(w_a.astype(jnp.bfloat16), v_a) + nn(w_b.astype(jnp.bfloat16), v_b)
    out = (mixed / row_sum).astype(jnp.bfloat16)
    log_total = row_max + jnp.log(row_sum)
    delta = jnp.sum(g.astype(jnp.float32) * out.astype(jnp.float32), -1, keepdims=True)
    p_a = jnp.exp(s_a - log_total)
    p_b = jnp.exp(s_b - log_total)
    gs_a = (p_a * (nt(g, v_a) - delta)).astype(jnp.bfloat16)
    gs_b = (p_b * (nt(g, v_b) - delta)).astype(jnp.bfloat16)
    dq = ((nn(gs_a, k_a) + nn(gs_b, k_b)) * scale).astype(jnp.bfloat16)
    dk_a = tn(gs_a, q) * scale
    dk_b = tn(gs_b, q) * scale
    dv_a = tn(p_a.astype(jnp.bfloat16), g)
    dv_b = tn(p_b.astype(jnp.bfloat16), g)
    return out, dq, (dk_a, dv_a), (dk_b, dv_b)


def band_kernel(seq_ref, q_ref, k_ref, v_ref, g_ref, kp_ref, vp_ref, out_ref, dq_ref, dk_ref, dv_ref, dkp_ref, dvp_ref, *, scale):
    rows = q_ref.shape[0]
    qi = lax.broadcasted_iota(jnp.int32, (rows, rows), 0)
    kj = lax.broadcasted_iota(jnp.int32, (rows, rows), 1)
    prev_mask = (kj > qi) & (seq_ref[0] > 0)
    own_mask = (kj <= qi) & (qi - kj < WIN)
    out, dq, (dkp, dvp), (dko, dvo) = two_part_attention(
        q_ref[...],
        g_ref[...],
        (kp_ref[...], vp_ref[...], prev_mask),
        (k_ref[...], v_ref[...], own_mask),
        scale,
    )
    out_ref[...] = out
    dq_ref[...] = dq
    dk_ref[...] = dko
    dv_ref[...] = dvo
    dkp_ref[...] = dkp.astype(dkp_ref.dtype)
    dvp_ref[...] = dvp.astype(dvp_ref.dtype)


def fixed_kernel(seq_ref, q_ref, k_ref, v_ref, g_ref, kf_ref, vf_ref, *refs, scale, unused):
    out_ref, dq_ref, dk_ref, dv_ref, dkvf_ref = refs[unused:]
    rows = q_ref.shape[0]
    far_rows = kf_ref.shape[0]
    start = seq_ref[0] * rows
    qi = lax.broadcasted_iota(jnp.int32, (rows, rows), 0)
    kj = lax.broadcasted_iota(jnp.int32, (rows, rows), 1)
    own_mask = (kj <= qi) & ((qi // BLOCK) == (kj // BLOCK))
    fq = lax.broadcasted_iota(jnp.int32, (rows, far_rows), 0)
    fr = lax.broadcasted_iota(jnp.int32, (rows, far_rows), 1)
    far_mask = (fr // SUMM) < ((start + fq) // BLOCK)
    out, dq, (dko, dvo), (dkf, dvf) = two_part_attention(
        q_ref[...],
        g_ref[...],
        (k_ref[...], v_ref[...], own_mask),
        (kf_ref[...], vf_ref[...], far_mask),
        scale,
    )
    out_ref[...] = out
    dq_ref[...] = dq
    dk_ref[...] = dko
    dv_ref[...] = dvo
    dkvf_ref[0] = dkf
    dkvf_ref[1] = dvf


def attention_cost(rows, keys, head_dim, heads):
    return pl.CostEstimate(
        flops=2 * rows * keys * head_dim * 7 * heads,
        transcendentals=3 * rows * keys * heads,
        bytes_accessed=(rows * 16 + keys * 6) * head_dim * heads,
    )


def band_attention(seq_index, q, k, v, g, k_prev, v_prev, head_pairs, head_dim, scale):
    rows = q.shape[0]
    block = pl.BlockSpec((rows, head_dim), lambda p, s: (0, 2 * p))
    narrow = pl.BlockSpec((rows, head_dim), lambda p, s: (0, p))
    width = 2 * head_pairs * head_dim
    grid_spec = pltpu.PrefetchScalarGridSpec(
        num_scalar_prefetch=1,
        grid=(head_pairs,),
        in_specs=[block] * 4 + [narrow] * 2,
        out_specs=[block] * 4 + [narrow] * 2,
    )
    return pl.pallas_call(
        functools.partial(band_kernel, scale=scale),
        grid_spec=grid_spec,
        out_shape=[
            jax.ShapeDtypeStruct((rows, width), jnp.bfloat16),
            jax.ShapeDtypeStruct((rows, width), jnp.bfloat16),
            jax.ShapeDtypeStruct((rows, width), jnp.float32),
            jax.ShapeDtypeStruct((rows, width), jnp.float32),
            jax.ShapeDtypeStruct((rows, head_pairs * head_dim), jnp.bfloat16),
            jax.ShapeDtypeStruct((rows, head_pairs * head_dim), jnp.bfloat16),
        ],
        compiler_params=pltpu.CompilerParams(vmem_limit_bytes=48 * 1024 * 1024),
        cost_estimate=attention_cost(rows, 2 * rows, head_dim, head_pairs),
    )(seq_index, q, k, v, g, k_prev, v_prev)


def fixed_attention(seq_index, q, k, v, g, far_kv, first_pair, pairs, head_pairs, head_dim, scale, earlier):
    rows = q.shape[0]
    far_rows = far_kv.shape[0]
    block = pl.BlockSpec((rows, head_dim), lambda p, s: (0, 2 * (first_pair + p) + 1))
    far_k_spec = pl.BlockSpec((far_rows, head_dim), lambda p, s: (0, first_pair + p))
    far_v_spec = pl.BlockSpec((far_rows, head_dim), lambda p, s: (0, head_pairs + first_pair + p))
    operands = [seq_index, q, k, v, g, far_kv, far_kv] + list(earlier)
    aliases = {7 + number: number for number in range(len(earlier))}
    grid_spec = pltpu.PrefetchScalarGridSpec(
        num_scalar_prefetch=1,
        grid=(pairs,),
        in_specs=[block] * 4 + [far_k_spec, far_v_spec]
        + [pl.BlockSpec(memory_space=pl.ANY)] * len(earlier),
        out_specs=[block] * 4 + [pl.BlockSpec((2, far_rows, head_dim), lambda p, s: (0, 0, p))],
    )
    return pl.pallas_call(
        functools.partial(fixed_kernel, scale=scale, unused=len(earlier)),
        grid_spec=grid_spec,
        out_shape=[jax.ShapeDtypeStruct(array.shape, array.dtype) for array in earlier]
        + [jax.ShapeDtypeStruct((2, far_rows, pairs * head_dim), jnp.float32)],
        input_output_aliases=aliases,
        compiler_params=pltpu.CompilerParams(vmem_limit_bytes=48 * 1024 * 1024),
        cost_estimate=attention_cost(rows, rows + far_rows, head_dim, pairs),
    )(*operands)


def prep_kernel(k_ref, v_ref, select_ref, bk_ref, bv_ref, dk_ref, dv_ref):
    hd = bk_ref.shape[1]
    pick = select_ref[0]
    bk_ref[...] = k_ref[:, :hd]
    bv_ref[...] = v_ref[:, :hd]
    dk_ref[...] = nn(pick, k_ref[:, hd:]).astype(dk_ref.dtype)
    dv_ref[...] = nn(pick, v_ref[:, hd:]).astype(dv_ref.dtype)


def prep(keys, values, select, head_pairs, head_dim):
    rows = keys.shape[0]
    digest_rows = select.shape[1]
    wide = pl.BlockSpec((rows, 2 * head_dim), lambda p: (0, p))
    narrow = pl.BlockSpec((rows, head_dim), lambda p: (0, p))
    digest = pl.BlockSpec((digest_rows, head_dim), lambda p: (0, p))
    width = head_pairs * head_dim
    return pl.pallas_call(
        prep_kernel,
        grid=(head_pairs,),
        in_specs=[wide, wide, pl.BlockSpec((1, digest_rows, rows), lambda p: (p, 0, 0))],
        out_specs=[narrow, narrow, digest, digest],
        out_shape=[
            jax.ShapeDtypeStruct((rows, width), keys.dtype),
            jax.ShapeDtypeStruct((rows, width), keys.dtype),
            jax.ShapeDtypeStruct((digest_rows, width), keys.dtype),
            jax.ShapeDtypeStruct((digest_rows, width), keys.dtype),
        ],
        cost_estimate=pl.CostEstimate(
            flops=4 * digest_rows * rows * head_dim * head_pairs,
            transcendentals=0,
            bytes_accessed=rows * head_dim * head_pairs * 12,
        ),
    )(keys, values, select)


def grad_out_kernel(head_ref, *refs):
    pieces = refs[:-2]
    w_ref, out_ref = refs[-2:]
    count = len(pieces)
    piece_rows = pieces[0].shape[0]
    block = w_ref[...]
    for shift, piece in enumerate(pieces):
        owner = lax.rem(head_ref[0] - shift + count, count)
        start = pl.multiple_of(owner * piece_rows, piece_rows)
        out_ref[pl.ds(start, piece_rows), :] = nt(piece[...], block).astype(out_ref.dtype)


def grad_out_matmul(head_index, pieces, out_weight):
    piece_rows, model = pieces[0].shape
    width = out_weight.shape[0]
    tile = 256 if width % 256 == 0 else width
    rows = piece_rows * len(pieces)
    grid_spec = pltpu.PrefetchScalarGridSpec(
        num_scalar_prefetch=1,
        grid=(width // tile,),
        in_specs=[pl.BlockSpec((piece_rows, model), lambda j, h: (0, 0))] * len(pieces)
        + [pl.BlockSpec((tile, model), lambda j, h: (j, 0))],
        out_specs=pl.BlockSpec((rows, tile), lambda j, h: (0, j)),
    )
    return pl.pallas_call(
        grad_out_kernel,
        grid_spec=grid_spec,
        out_shape=jax.ShapeDtypeStruct((rows, width), jnp.bfloat16),
        compiler_params=pltpu.CompilerParams(vmem_limit_bytes=48 * 1024 * 1024),
        cost_estimate=pl.CostEstimate(
            flops=2 * rows * model * width,
            transcendentals=0,
            bytes_accessed=2 * (width * model + rows * model + rows * width),
        ),
    )(head_index, *pieces, out_weight)


def finalize_kernel(own_k_ref, own_v_ref, back_k_ref, back_v_ref, digest_ref, select_ref, k_out, v_out):
    hd = back_k_ref.shape[1]
    pick = select_ref[0]
    for own_ref, back_ref, side, out_ref in (
        (own_k_ref, back_k_ref, 0, k_out),
        (own_v_ref, back_v_ref, 1, v_out),
    ):
        out_ref[:, :hd] = (own_ref[:, :hd] + back_ref[...].astype(jnp.float32)).astype(out_ref.dtype)
        summary = tn(pick, digest_ref[side])
        out_ref[:, hd:] = (own_ref[:, hd:] + summary).astype(out_ref.dtype)


def finalize(own_k, own_v, back_k, back_v, digest, select, head_pairs, head_dim):
    rows = own_k.shape[0]
    digest_rows = digest.shape[1]
    wide = pl.BlockSpec((rows, 2 * head_dim), lambda p: (0, p))
    narrow = pl.BlockSpec((rows, head_dim), lambda p: (0, p))
    return pl.pallas_call(
        finalize_kernel,
        grid=(head_pairs,),
        in_specs=[
            wide,
            wide,
            narrow,
            narrow,
            pl.BlockSpec((2, digest_rows, head_dim), lambda p: (0, 0, p)),
            pl.BlockSpec((1, digest_rows, rows), lambda p: (p, 0, 0)),
        ],
        out_specs=[wide, wide],
        out_shape=[jax.ShapeDtypeStruct(own_k.shape, jnp.bfloat16)] * 2,
        cost_estimate=pl.CostEstimate(
            flops=4 * rows * digest_rows * head_dim * head_pairs,
            transcendentals=0,
            bytes_accessed=rows * head_dim * head_pairs * 20,
        ),
    )(own_k, own_v, back_k, back_v, digest, select)


def on_device(queries, keys, values, out_weight, cotangent, offsets):
    seq_rows = queries.shape[0]
    full_width = queries.shape[1]
    head_pairs = offsets.shape[0]
    head_dim = full_width // (2 * head_pairs)
    score_scale = head_dim ** (-0.5)
    assert seq_rows == WIN and seq_rows % BLOCK == 0
    seq_index = lax.axis_index("seq")
    digest_count = seq_rows // BLOCK * SUMM
    offset_table = jnp.tile(offsets.T, (seq_rows // BLOCK, 1))
    digest_rows = (jnp.arange(digest_count, dtype=jnp.int32) // SUMM * BLOCK)[
        :, None
    ] + offset_table
    select = (
        digest_rows.T[:, :, None] == jnp.arange(seq_rows, dtype=jnp.int32)[None, None, :]
    ).astype(jnp.bfloat16)
    band_k, band_v, digest_k, digest_v = prep(keys, values, select, head_pairs, head_dim)
    prev_k, prev_v = passed_along((band_k, band_v), "seq", 1)
    far_kv = lax.all_gather(
        jnp.concatenate([digest_k, digest_v], 1), "seq", axis=0, tiled=True
    )
    head_count = lax.axis_size("head")
    head_index = lax.axis_index("head")
    pieces = [cotangent] + [
        lax.ppermute(
            cotangent, "head", [(source, (source + shift) % head_count) for source in range(head_count)]
        )
        for shift in range(1, head_count)
    ]
    grad_out = grad_out_matmul(head_index.reshape(1).astype(jnp.int32), pieces, out_weight)
    seq_scalar = seq_index.reshape(1).astype(jnp.int32)
    attention, query_grad, own_dk, own_dv, back_k, back_v = band_attention(
        seq_scalar, queries, keys, values, grad_out, prev_k, prev_v, head_pairs, head_dim, score_scale
    )
    chunks = 4 if head_pairs % 4 == 0 else (2 if head_pairs % 2 == 0 else 1)
    pairs = head_pairs // chunks
    outputs = (attention, query_grad, own_dk, own_dv)
    digests = []
    for chunk in range(chunks):
        *outputs, far_dkv = fixed_attention(
            seq_scalar,
            queries,
            keys,
            values,
            grad_out,
            far_kv,
            chunk * pairs,
            pairs,
            head_pairs,
            head_dim,
            score_scale,
            outputs,
        )
        digests.append(seq_reduce_scatter(far_dkv, 1, chunk))
    attention, query_grad, own_dk, own_dv = outputs
    back_k, back_v = passed_along((back_k, back_v), "seq", -1)
    digest_dkv = jnp.concatenate(digests, 2) if chunks > 1 else digests[0]
    key_grad, value_grad = finalize(
        own_dk, own_dv, back_k, back_v, digest_dkv, select, head_pairs, head_dim
    )
    return attention, query_grad, key_grad, value_grad


def solution(mesh):
    in_specs = (
        P("seq", "head"),
        P("seq", "head"),
        P("seq", "head"),
        P("head", None),
        P(("seq", "head"), None),
        P("head", None),
    )
    out_specs = (P("seq", "head"), P("seq", "head"), P("seq", "head"), P("seq", "head"))
    return jax.shard_map(
        on_device, mesh=mesh, in_specs=in_specs, out_specs=out_specs, check_vma=False
    )
```

```python
import functools

import jax
import jax.numpy as jnp
from jax import lax
from jax.experimental import pallas as pl
from jax.experimental.pallas import tpu as pltpu
from jax.sharding import PartitionSpec as P

WIN = 256
BLOCK = 128
SUMM = 32


NEG = -1e30


def passed_along(value, axis, steps):
    count = lax.axis_size(axis)
    first, last = (max(0, -steps), min(count, count - steps))
    return lax.ppermute(value, axis, [(source, source + steps) for source in range(first, last)])


def seq_reduce_scatter(parts, axis, rotate=0):
    count = lax.axis_size("seq")
    if count & (count - 1):
        return lax.psum_scatter(
            parts.astype(jnp.bfloat16), "seq", scatter_dimension=axis, tiled=True
        )
    me = lax.axis_index("seq")
    bits = count.bit_length() - 1
    chunk = parts.shape[axis] // count
    held = parts.reshape(parts.shape[:axis] + (2,) * bits + (chunk,) + parts.shape[axis + 1 :])
    order = rotated_order(bits, rotate)
    gone = []
    for bit in order:
        where = axis + bits - 1 - bit - sum(1 for done in gone if done > bit)
        gone.append(bit)
        mine = (me >> bit) & 1
        keep = lax.dynamic_index_in_dim(held, mine, where, keepdims=False)
        send = lax.dynamic_index_in_dim(held, 1 - mine, where, keepdims=False)
        arrived = lax.ppermute(
            send.astype(jnp.bfloat16), "seq", [(source, source ^ (1 << bit)) for source in range(count)]
        )
        held = keep + arrived.astype(jnp.float32)
    return held.astype(jnp.bfloat16)


def rotated_order(bits, rotate):
    if bits > 2:
        return [0] + sorted(range(1, bits - 1), key=lambda b: (b - 1 - rotate) % (bits - 2)) + [bits - 1]
    return list(range(bits))


def seq_all_gather(local, rotate):
    count = lax.axis_size("seq")
    if count & (count - 1):
        return lax.all_gather(local, "seq", axis=0, tiled=True)
    me = lax.axis_index("seq")
    bits = count.bit_length() - 1
    order = rotated_order(bits, rotate)[::-1]
    held = local
    for step, bit in enumerate(order):
        mine = (me >> bit) & 1
        arrived = lax.ppermute(held, "seq", [(source, source ^ (1 << bit)) for source in range(count)])
        pair = jnp.stack([held, arrived], step)
        swapped = jnp.stack([arrived, held], step)
        held = jnp.where(mine == 0, pair, swapped)
    placed = sorted(range(bits), key=lambda b: order.index(b))
    axes = [placed.index(b) for b in range(bits - 1, -1, -1)]
    held = held.transpose(axes + list(range(bits, held.ndim)))
    return held.reshape((count * local.shape[0],) + local.shape[1:])


def nt(left, right):
    return lax.dot_general(left, right, (((1,), (1,)), ((), ())), preferred_element_type=jnp.float32)


def tn(left, right):
    return lax.dot_general(left, right, (((0,), (0,)), ((), ())), preferred_element_type=jnp.float32)


def nn(left, right):
    return lax.dot_general(left, right, (((1,), (0,)), ((), ())), preferred_element_type=jnp.float32)


def two_part_attention(q, g, first, second, scale):
    (k_a, v_a, mask_a), (k_b, v_b, mask_b) = first, second
    s_a = jnp.where(mask_a, nt(q, k_a) * scale, NEG)
    s_b = jnp.where(mask_b, nt(q, k_b) * scale, NEG)
    row_max = jnp.maximum(s_a.max(-1, keepdims=True), s_b.max(-1, keepdims=True))
    w_a = jnp.exp(s_a - row_max)
    w_b = jnp.exp(s_b - row_max)
    row_sum = w_a.sum(-1, keepdims=True) + w_b.sum(-1, keepdims=True)
    mixed = nn(w_a.astype(jnp.bfloat16), v_a) + nn(w_b.astype(jnp.bfloat16), v_b)
    out = (mixed / row_sum).astype(jnp.bfloat16)
    log_total = row_max + jnp.log(row_sum)
    delta = jnp.sum(g.astype(jnp.float32) * out.astype(jnp.float32), -1, keepdims=True)
    p_a = jnp.exp(s_a - log_total)
    p_b = jnp.exp(s_b - log_total)
    gs_a = (p_a * (nt(g, v_a) - delta)).astype(jnp.bfloat16)
    gs_b = (p_b * (nt(g, v_b) - delta)).astype(jnp.bfloat16)
    dq = ((nn(gs_a, k_a) + nn(gs_b, k_b)) * scale).astype(jnp.bfloat16)
    dk_a = tn(gs_a, q) * scale
    dk_b = tn(gs_b, q) * scale
    dv_a = tn(p_a.astype(jnp.bfloat16), g)
    dv_b = tn(p_b.astype(jnp.bfloat16), g)
    return out, dq, (dk_a, dv_a), (dk_b, dv_b)


def band_kernel(seq_ref, q_ref, k_ref, v_ref, g_ref, kp_ref, vp_ref, out_ref, dq_ref, dk_ref, dv_ref, dkp_ref, dvp_ref, *, scale):
    rows = q_ref.shape[0]
    qi = lax.broadcasted_iota(jnp.int32, (rows, rows), 0)
    kj = lax.broadcasted_iota(jnp.int32, (rows, rows), 1)
    prev_mask = (kj > qi) & (seq_ref[0] > 0)
    own_mask = (kj <= qi) & (qi - kj < WIN)
    out, dq, (dkp, dvp), (dko, dvo) = two_part_attention(
        q_ref[...],
        g_ref[...],
        (kp_ref[...], vp_ref[...], prev_mask),
        (k_ref[...], v_ref[...], own_mask),
        scale,
    )
    out_ref[...] = out
    dq_ref[...] = dq
    dk_ref[...] = dko
    dv_ref[...] = dvo
    dkp_ref[...] = dkp.astype(dkp_ref.dtype)
    dvp_ref[...] = dvp.astype(dvp_ref.dtype)


def fixed_kernel(seq_ref, q_ref, k_ref, v_ref, g_ref, kf_ref, vf_ref, *refs, scale, unused):
    out_ref, dq_ref, dk_ref, dv_ref, dkvf_ref = refs[unused:]
    rows = q_ref.shape[0]
    far_rows = kf_ref.shape[0]
    start = seq_ref[0] * rows
    qi = lax.broadcasted_iota(jnp.int32, (rows, rows), 0)
    kj = lax.broadcasted_iota(jnp.int32, (rows, rows), 1)
    own_mask = (kj <= qi) & ((qi // BLOCK) == (kj // BLOCK))
    fq = lax.broadcasted_iota(jnp.int32, (rows, far_rows), 0)
    fr = lax.broadcasted_iota(jnp.int32, (rows, far_rows), 1)
    far_mask = (fr // SUMM) < ((start + fq) // BLOCK)
    out, dq, (dko, dvo), (dkf, dvf) = two_part_attention(
        q_ref[...],
        g_ref[...],
        (k_ref[...], v_ref[...], own_mask),
        (kf_ref[...], vf_ref[...], far_mask),
        scale,
    )
    out_ref[...] = out
    dq_ref[...] = dq
    dk_ref[...] = dko
    dv_ref[...] = dvo
    dkvf_ref[0] = dkf
    dkvf_ref[1] = dvf


def attention_cost(rows, keys, head_dim, heads):
    return pl.CostEstimate(
        flops=2 * rows * keys * head_dim * 7 * heads,
        transcendentals=3 * rows * keys * heads,
        bytes_accessed=(rows * 16 + keys * 6) * head_dim * heads,
    )


def band_attention(seq_index, q, k, v, g, k_prev, v_prev, head_pairs, head_dim, scale):
    rows = q.shape[0]
    block = pl.BlockSpec((rows, head_dim), lambda p, s: (0, 2 * p))
    narrow = pl.BlockSpec((rows, head_dim), lambda p, s: (0, p))
    width = 2 * head_pairs * head_dim
    grid_spec = pltpu.PrefetchScalarGridSpec(
        num_scalar_prefetch=1,
        grid=(head_pairs,),
        in_specs=[block] * 4 + [narrow] * 2,
        out_specs=[block] * 4 + [narrow] * 2,
    )
    return pl.pallas_call(
        functools.partial(band_kernel, scale=scale),
        grid_spec=grid_spec,
        out_shape=[
            jax.ShapeDtypeStruct((rows, width), jnp.bfloat16),
            jax.ShapeDtypeStruct((rows, width), jnp.bfloat16),
            jax.ShapeDtypeStruct((rows, width), jnp.float32),
            jax.ShapeDtypeStruct((rows, width), jnp.float32),
            jax.ShapeDtypeStruct((rows, head_pairs * head_dim), jnp.bfloat16),
            jax.ShapeDtypeStruct((rows, head_pairs * head_dim), jnp.bfloat16),
        ],
        compiler_params=pltpu.CompilerParams(vmem_limit_bytes=48 * 1024 * 1024),
        cost_estimate=attention_cost(rows, 2 * rows, head_dim, head_pairs),
    )(seq_index, q, k, v, g, k_prev, v_prev)


def fixed_attention(seq_index, q, k, v, g, far_kv, first_pair, pairs, far_first, head_dim, scale, earlier):
    rows = q.shape[0]
    far_rows = far_kv.shape[0]
    far_pairs = far_kv.shape[1] // (2 * head_dim)
    block = pl.BlockSpec((rows, head_dim), lambda p, s: (0, 2 * (first_pair + p) + 1))
    far_k_spec = pl.BlockSpec((far_rows, head_dim), lambda p, s: (0, far_first + p))
    far_v_spec = pl.BlockSpec((far_rows, head_dim), lambda p, s: (0, far_pairs + far_first + p))
    operands = [seq_index, q, k, v, g, far_kv, far_kv] + list(earlier)
    aliases = {7 + number: number for number in range(len(earlier))}
    grid_spec = pltpu.PrefetchScalarGridSpec(
        num_scalar_prefetch=1,
        grid=(pairs,),
        in_specs=[block] * 4 + [far_k_spec, far_v_spec]
        + [pl.BlockSpec(memory_space=pl.ANY)] * len(earlier),
        out_specs=[block] * 4 + [pl.BlockSpec((2, far_rows, head_dim), lambda p, s: (0, 0, p))],
    )
    return pl.pallas_call(
        functools.partial(fixed_kernel, scale=scale, unused=len(earlier)),
        grid_spec=grid_spec,
        out_shape=[jax.ShapeDtypeStruct(array.shape, array.dtype) for array in earlier]
        + [jax.ShapeDtypeStruct((2, far_rows, pairs * head_dim), jnp.float32)],
        input_output_aliases=aliases,
        compiler_params=pltpu.CompilerParams(vmem_limit_bytes=48 * 1024 * 1024),
        cost_estimate=attention_cost(rows, rows + far_rows, head_dim, pairs),
    )(*operands)


def finalize_kernel(own_k_ref, own_v_ref, back_k_ref, back_v_ref, digest_ref, select_ref, k_out, v_out):
    hd = back_k_ref.shape[1]
    pick = select_ref[0]
    for own_ref, back_ref, side, out_ref in (
        (own_k_ref, back_k_ref, 0, k_out),
        (own_v_ref, back_v_ref, 1, v_out),
    ):
        out_ref[:, :hd] = (own_ref[:, :hd] + back_ref[...].astype(jnp.float32)).astype(out_ref.dtype)
        summary = tn(pick, digest_ref[side])
        out_ref[:, hd:] = (own_ref[:, hd:] + summary).astype(out_ref.dtype)


def finalize(own_k, own_v, back_k, back_v, digest, select, head_pairs, head_dim):
    rows = own_k.shape[0]
    digest_rows = digest.shape[1]
    wide = pl.BlockSpec((rows, 2 * head_dim), lambda p: (0, p))
    narrow = pl.BlockSpec((rows, head_dim), lambda p: (0, p))
    return pl.pallas_call(
        finalize_kernel,
        grid=(head_pairs,),
        in_specs=[
            wide,
            wide,
            narrow,
            narrow,
            pl.BlockSpec((2, digest_rows, head_dim), lambda p: (0, 0, p)),
            pl.BlockSpec((1, digest_rows, rows), lambda p: (p, 0, 0)),
        ],
        out_specs=[wide, wide],
        out_shape=[jax.ShapeDtypeStruct(own_k.shape, jnp.bfloat16)] * 2,
        cost_estimate=pl.CostEstimate(
            flops=4 * rows * digest_rows * head_dim * head_pairs,
            transcendentals=0,
            bytes_accessed=rows * head_dim * head_pairs * 20,
        ),
    )(own_k, own_v, back_k, back_v, digest, select)


def on_device(queries, keys, values, out_weight, cotangent, offsets):
    seq_rows = queries.shape[0]
    full_width = queries.shape[1]
    head_pairs = offsets.shape[0]
    head_dim = full_width // (2 * head_pairs)
    score_scale = head_dim ** (-0.5)
    assert seq_rows == WIN and seq_rows % BLOCK == 0
    seq_index = lax.axis_index("seq")
    split_k = keys.reshape(seq_rows, head_pairs, 2, head_dim)
    split_v = values.reshape(seq_rows, head_pairs, 2, head_dim)
    fixed_k = split_k[:, :, 1]
    fixed_v = split_v[:, :, 1]
    band_k = split_k[:, :, 0].reshape(seq_rows, head_pairs * head_dim)
    band_v = split_v[:, :, 0].reshape(seq_rows, head_pairs * head_dim)
    prev_k, prev_v = passed_along((band_k, band_v), "seq", 1)
    digest_count = seq_rows // BLOCK * SUMM
    offset_table = jnp.tile(offsets.T, (seq_rows // BLOCK, 1))
    digest_rows = (jnp.arange(digest_count, dtype=jnp.int32) // SUMM * BLOCK)[
        :, None
    ] + offset_table
    select = (
        digest_rows.T[:, :, None] == jnp.arange(seq_rows, dtype=jnp.int32)[None, None, :]
    ).astype(jnp.bfloat16)
    digest_k = jnp.einsum(
        "hjr,rhc->jhc", select, fixed_k, preferred_element_type=jnp.float32
    ).astype(jnp.bfloat16)
    digest_v = jnp.einsum(
        "hjr,rhc->jhc", select, fixed_v, preferred_element_type=jnp.float32
    ).astype(jnp.bfloat16)
    gathers = 2 if head_pairs % 2 == 0 else 1
    gather_pairs = head_pairs // gathers
    split_dk = digest_k.reshape(digest_count, gathers, gather_pairs * head_dim)
    split_dv = digest_v.reshape(digest_count, gathers, gather_pairs * head_dim)
    far_parts = [
        seq_all_gather(jnp.concatenate([split_dk[:, part], split_dv[:, part]], 1), part)
        for part in range(gathers)
    ]
    head_count = lax.axis_size("head")
    head_index = lax.axis_index("head")
    pieces = [cotangent] + [
        lax.ppermute(
            cotangent, "head", [(source, (source + shift) % head_count) for source in range(head_count)]
        )
        for shift in range(1, head_count)
    ]
    doubled = jnp.stack(pieces[::-1] + pieces[::-1], 0)
    gathered = lax.dynamic_slice_in_dim(doubled, head_count - 1 - head_index, head_count, 0)
    grad_out = lax.dot_general(
        gathered.reshape(seq_rows, cotangent.shape[1]),
        out_weight,
        (((1,), (1,)), ((), ())),
        preferred_element_type=jnp.float32,
    ).astype(jnp.bfloat16)
    seq_scalar = seq_index.reshape(1).astype(jnp.int32)
    attention, query_grad, own_dk, own_dv, back_k, back_v = band_attention(
        seq_scalar, queries, keys, values, grad_out, prev_k, prev_v, head_pairs, head_dim, score_scale
    )
    chunks = 4 if head_pairs % 4 == 0 else (2 if head_pairs % 2 == 0 else 1)
    pairs = head_pairs // chunks
    outputs = (attention, query_grad, own_dk, own_dv)
    digests = []
    for chunk in range(chunks):
        part = chunk * pairs // gather_pairs
        *outputs, far_dkv = fixed_attention(
            seq_scalar,
            queries,
            keys,
            values,
            grad_out,
            far_parts[part],
            chunk * pairs,
            pairs,
            chunk * pairs - part * gather_pairs,
            head_dim,
            score_scale,
            outputs,
        )
        digests.append(seq_reduce_scatter(far_dkv, 1, chunk))
    attention, query_grad, own_dk, own_dv = outputs
    back_k, back_v = passed_along((back_k, back_v), "seq", -1)
    digest_dkv = jnp.concatenate(digests, 2) if chunks > 1 else digests[0]
    key_grad, value_grad = finalize(
        own_dk, own_dv, back_k, back_v, digest_dkv, select, head_pairs, head_dim
    )
    return attention, query_grad, key_grad, value_grad


def solution(mesh):
    in_specs = (
        P("seq", "head"),
        P("seq", "head"),
        P("seq", "head"),
        P("head", None),
        P(("seq", "head"), None),
        P("head", None),
    )
    out_specs = (P("seq", "head"), P("seq", "head"), P("seq", "head"), P("seq", "head"))
    return jax.shard_map(
        on_device, mesh=mesh, in_specs=in_specs, out_specs=out_specs, check_vma=False
    )
```

```python
import functools

import jax
import jax.numpy as jnp
from jax import lax
from jax.experimental import pallas as pl
from jax.experimental.pallas import tpu as pltpu
from jax.sharding import PartitionSpec as P

WIN = 256
BLOCK = 128
SUMM = 32


NEG = -1e30


def passed_along(value, axis, steps):
    count = lax.axis_size(axis)
    first, last = (max(0, -steps), min(count, count - steps))
    return lax.ppermute(value, axis, [(source, source + steps) for source in range(first, last)])


def seq_reduce_scatter(parts, axis, rotate=0):
    count = lax.axis_size("seq")
    if count & (count - 1):
        return lax.psum_scatter(
            parts.astype(jnp.bfloat16), "seq", scatter_dimension=axis, tiled=True
        )
    me = lax.axis_index("seq")
    bits = count.bit_length() - 1
    chunk = parts.shape[axis] // count
    held = parts.reshape(parts.shape[:axis] + (2,) * bits + (chunk,) + parts.shape[axis + 1 :])
    if bits > 2:
        order = [0] + sorted(range(1, bits - 1), key=lambda b: (b - 1 - rotate) % (bits - 2)) + [bits - 1]
    else:
        order = list(range(bits))
    gone = []
    for bit in order:
        where = axis + bits - 1 - bit - sum(1 for done in gone if done > bit)
        gone.append(bit)
        mine = (me >> bit) & 1
        keep = lax.dynamic_index_in_dim(held, mine, where, keepdims=False)
        send = lax.dynamic_index_in_dim(held, 1 - mine, where, keepdims=False)
        arrived = lax.ppermute(
            send.astype(jnp.bfloat16), "seq", [(source, source ^ (1 << bit)) for source in range(count)]
        )
        held = keep + arrived.astype(jnp.float32)
    return held.astype(jnp.bfloat16)


def nt(left, right):
    return lax.dot_general(left, right, (((1,), (1,)), ((), ())), preferred_element_type=jnp.float32)


def tn(left, right):
    return lax.dot_general(left, right, (((0,), (0,)), ((), ())), preferred_element_type=jnp.float32)


def nn(left, right):
    return lax.dot_general(left, right, (((1,), (0,)), ((), ())), preferred_element_type=jnp.float32)


def two_part_attention(q, g, first, second, scale):
    (k_a, v_a, mask_a), (k_b, v_b, mask_b) = first, second
    s_a = jnp.where(mask_a, nt(q, k_a) * scale, NEG)
    s_b = jnp.where(mask_b, nt(q, k_b) * scale, NEG)
    row_max = jnp.maximum(s_a.max(-1, keepdims=True), s_b.max(-1, keepdims=True))
    w_a = jnp.exp(s_a - row_max)
    w_b = jnp.exp(s_b - row_max)
    row_sum = w_a.sum(-1, keepdims=True) + w_b.sum(-1, keepdims=True)
    mixed = nn(w_a.astype(jnp.bfloat16), v_a) + nn(w_b.astype(jnp.bfloat16), v_b)
    out = (mixed / row_sum).astype(jnp.bfloat16)
    delta = jnp.sum(g.astype(jnp.float32) * out.astype(jnp.float32), -1, keepdims=True)
    inverse = 1.0 / row_sum
    p_a = w_a * inverse
    p_b = w_b * inverse
    gs_a = (p_a * (nt(g, v_a) - delta)).astype(jnp.bfloat16)
    gs_b = (p_b * (nt(g, v_b) - delta)).astype(jnp.bfloat16)
    dq = ((nn(gs_a, k_a) + nn(gs_b, k_b)) * scale).astype(jnp.bfloat16)
    dk_a = tn(gs_a, q) * scale
    dk_b = tn(gs_b, q) * scale
    dv_a = tn(p_a.astype(jnp.bfloat16), g)
    dv_b = tn(p_b.astype(jnp.bfloat16), g)
    return out, dq, (dk_a, dv_a), (dk_b, dv_b)


def band_kernel(seq_ref, q_ref, k_ref, v_ref, g_ref, kp_ref, vp_ref, out_ref, dq_ref, dk_ref, dv_ref, dkp_ref, dvp_ref, *, scale):
    rows = q_ref.shape[0]
    qi = lax.broadcasted_iota(jnp.int32, (rows, rows), 0)
    kj = lax.broadcasted_iota(jnp.int32, (rows, rows), 1)
    prev_mask = (kj > qi) & (seq_ref[0] > 0)
    own_mask = (kj <= qi) & (qi - kj < WIN)
    out, dq, (dkp, dvp), (dko, dvo) = two_part_attention(
        q_ref[...],
        g_ref[...],
        (kp_ref[...], vp_ref[...], prev_mask),
        (k_ref[...], v_ref[...], own_mask),
        scale,
    )
    out_ref[...] = out
    dq_ref[...] = dq
    dk_ref[...] = dko
    dv_ref[...] = dvo
    dkp_ref[...] = dkp.astype(dkp_ref.dtype)
    dvp_ref[...] = dvp.astype(dvp_ref.dtype)


def fixed_kernel(seq_ref, q_ref, k_ref, v_ref, g_ref, kf_ref, vf_ref, *refs, scale, unused):
    out_ref, dq_ref, dk_ref, dv_ref, dkvf_ref = refs[unused:]
    rows = q_ref.shape[0]
    far_rows = kf_ref.shape[0]
    start = seq_ref[0] * rows
    qi = lax.broadcasted_iota(jnp.int32, (rows, rows), 0)
    kj = lax.broadcasted_iota(jnp.int32, (rows, rows), 1)
    own_mask = (kj <= qi) & ((qi // BLOCK) == (kj // BLOCK))
    fq = lax.broadcasted_iota(jnp.int32, (rows, far_rows), 0)
    fr = lax.broadcasted_iota(jnp.int32, (rows, far_rows), 1)
    far_mask = (fr // SUMM) < ((start + fq) // BLOCK)
    out, dq, (dko, dvo), (dkf, dvf) = two_part_attention(
        q_ref[...],
        g_ref[...],
        (k_ref[...], v_ref[...], own_mask),
        (kf_ref[...], vf_ref[...], far_mask),
        scale,
    )
    out_ref[...] = out
    dq_ref[...] = dq
    dk_ref[...] = dko
    dv_ref[...] = dvo
    dkvf_ref[0] = dkf.astype(dkvf_ref.dtype)
    dkvf_ref[1] = dvf.astype(dkvf_ref.dtype)


def attention_cost(rows, keys, head_dim, heads):
    return pl.CostEstimate(
        flops=2 * rows * keys * head_dim * 7 * heads,
        transcendentals=3 * rows * keys * heads,
        bytes_accessed=(rows * 16 + keys * 6) * head_dim * heads,
    )


def band_attention(seq_index, q, k, v, g, k_prev, v_prev, head_pairs, head_dim, scale):
    rows = q.shape[0]
    block = pl.BlockSpec((rows, head_dim), lambda p, s: (0, 2 * p))
    narrow = pl.BlockSpec((rows, head_dim), lambda p, s: (0, p))
    width = 2 * head_pairs * head_dim
    grid_spec = pltpu.PrefetchScalarGridSpec(
        num_scalar_prefetch=1,
        grid=(head_pairs,),
        in_specs=[block] * 4 + [narrow] * 2,
        out_specs=[block] * 4 + [narrow] * 2,
    )
    return pl.pallas_call(
        functools.partial(band_kernel, scale=scale),
        grid_spec=grid_spec,
        out_shape=[
            jax.ShapeDtypeStruct((rows, width), jnp.bfloat16),
            jax.ShapeDtypeStruct((rows, width), jnp.bfloat16),
            jax.ShapeDtypeStruct((rows, width), jnp.float32),
            jax.ShapeDtypeStruct((rows, width), jnp.float32),
            jax.ShapeDtypeStruct((rows, head_pairs * head_dim), jnp.bfloat16),
            jax.ShapeDtypeStruct((rows, head_pairs * head_dim), jnp.bfloat16),
        ],
        compiler_params=pltpu.CompilerParams(vmem_limit_bytes=48 * 1024 * 1024),
        cost_estimate=attention_cost(rows, 2 * rows, head_dim, head_pairs),
    )(seq_index, q, k, v, g, k_prev, v_prev)


def fixed_attention(seq_index, q, k, v, g, far_kv, first_pair, pairs, head_pairs, head_dim, scale, earlier):
    rows = q.shape[0]
    far_rows = far_kv.shape[0]
    block = pl.BlockSpec((rows, head_dim), lambda p, s: (0, 2 * (first_pair + p) + 1))
    far_k_spec = pl.BlockSpec((far_rows, head_dim), lambda p, s: (0, first_pair + p))
    far_v_spec = pl.BlockSpec((far_rows, head_dim), lambda p, s: (0, head_pairs + first_pair + p))
    operands = [seq_index, q, k, v, g, far_kv, far_kv] + list(earlier)
    aliases = {7 + number: number for number in range(len(earlier))}
    grid_spec = pltpu.PrefetchScalarGridSpec(
        num_scalar_prefetch=1,
        grid=(pairs,),
        in_specs=[block] * 4 + [far_k_spec, far_v_spec]
        + [pl.BlockSpec(memory_space=pl.ANY)] * len(earlier),
        out_specs=[block] * 4 + [pl.BlockSpec((2, far_rows, head_dim), lambda p, s: (0, 0, p))],
    )
    return pl.pallas_call(
        functools.partial(fixed_kernel, scale=scale, unused=len(earlier)),
        grid_spec=grid_spec,
        out_shape=[jax.ShapeDtypeStruct(array.shape, array.dtype) for array in earlier]
        + [jax.ShapeDtypeStruct((2, far_rows, pairs * head_dim), jnp.bfloat16)],
        input_output_aliases=aliases,
        compiler_params=pltpu.CompilerParams(vmem_limit_bytes=48 * 1024 * 1024),
        cost_estimate=attention_cost(rows, rows + far_rows, head_dim, pairs),
    )(*operands)


def finalize_kernel(own_k_ref, own_v_ref, back_k_ref, back_v_ref, digest_ref, select_ref, k_out, v_out):
    hd = back_k_ref.shape[1]
    pick = select_ref[0]
    for own_ref, back_ref, side, out_ref in (
        (own_k_ref, back_k_ref, 0, k_out),
        (own_v_ref, back_v_ref, 1, v_out),
    ):
        out_ref[:, :hd] = (own_ref[:, :hd] + back_ref[...].astype(jnp.float32)).astype(out_ref.dtype)
        summary = tn(pick, digest_ref[side])
        out_ref[:, hd:] = (own_ref[:, hd:] + summary).astype(out_ref.dtype)


def finalize(own_k, own_v, back_k, back_v, digest, select, head_pairs, head_dim):
    rows = own_k.shape[0]
    digest_rows = digest.shape[1]
    wide = pl.BlockSpec((rows, 2 * head_dim), lambda p: (0, p))
    narrow = pl.BlockSpec((rows, head_dim), lambda p: (0, p))
    return pl.pallas_call(
        finalize_kernel,
        grid=(head_pairs,),
        in_specs=[
            wide,
            wide,
            narrow,
            narrow,
            pl.BlockSpec((2, digest_rows, head_dim), lambda p: (0, 0, p)),
            pl.BlockSpec((1, digest_rows, rows), lambda p: (p, 0, 0)),
        ],
        out_specs=[wide, wide],
        out_shape=[jax.ShapeDtypeStruct(own_k.shape, jnp.bfloat16)] * 2,
        cost_estimate=pl.CostEstimate(
            flops=4 * rows * digest_rows * head_dim * head_pairs,
            transcendentals=0,
            bytes_accessed=rows * head_dim * head_pairs * 20,
        ),
    )(own_k, own_v, back_k, back_v, digest, select)


def on_device(queries, keys, values, out_weight, cotangent, offsets):
    seq_rows = queries.shape[0]
    full_width = queries.shape[1]
    head_pairs = offsets.shape[0]
    head_dim = full_width // (2 * head_pairs)
    score_scale = head_dim ** (-0.5)
    assert seq_rows == WIN and seq_rows % BLOCK == 0
    seq_index = lax.axis_index("seq")
    split_k = keys.reshape(seq_rows, head_pairs, 2, head_dim)
    split_v = values.reshape(seq_rows, head_pairs, 2, head_dim)
    fixed_k = split_k[:, :, 1]
    fixed_v = split_v[:, :, 1]
    band_k = split_k[:, :, 0].reshape(seq_rows, head_pairs * head_dim)
    band_v = split_v[:, :, 0].reshape(seq_rows, head_pairs * head_dim)
    prev_k, prev_v = passed_along((band_k, band_v), "seq", 1)
    digest_count = seq_rows // BLOCK * SUMM
    offset_table = jnp.tile(offsets.T, (seq_rows // BLOCK, 1))
    digest_rows = (jnp.arange(digest_count, dtype=jnp.int32) // SUMM * BLOCK)[
        :, None
    ] + offset_table
    select = (
        digest_rows.T[:, :, None] == jnp.arange(seq_rows, dtype=jnp.int32)[None, None, :]
    ).astype(jnp.bfloat16)
    digest_k = jnp.einsum(
        "hjr,rhc->jhc", select, fixed_k, preferred_element_type=jnp.float32
    ).astype(jnp.bfloat16)
    digest_v = jnp.einsum(
        "hjr,rhc->jhc", select, fixed_v, preferred_element_type=jnp.float32
    ).astype(jnp.bfloat16)
    pair_width = head_pairs * head_dim
    far_kv = lax.all_gather(
        jnp.concatenate(
            [
                digest_k.reshape(digest_count, pair_width),
                digest_v.reshape(digest_count, pair_width),
            ],
            1,
        ),
        "seq",
        axis=0,
        tiled=True,
    )
    head_count = lax.axis_size("head")
    head_index = lax.axis_index("head")
    pieces = [cotangent] + [
        lax.ppermute(
            cotangent, "head", [(source, (source + shift) % head_count) for source in range(head_count)]
        )
        for shift in range(1, head_count)
    ]
    doubled = jnp.stack(pieces[::-1] + pieces[::-1], 0)
    gathered = lax.dynamic_slice_in_dim(doubled, head_count - 1 - head_index, head_count, 0)
    grad_out = lax.dot_general(
        gathered.reshape(seq_rows, cotangent.shape[1]),
        out_weight,
        (((1,), (1,)), ((), ())),
        preferred_element_type=jnp.float32,
    ).astype(jnp.bfloat16)
    seq_scalar = seq_index.reshape(1).astype(jnp.int32)
    attention, query_grad, own_dk, own_dv, back_k, back_v = band_attention(
        seq_scalar, queries, keys, values, grad_out, prev_k, prev_v, head_pairs, head_dim, score_scale
    )
    chunks = 4 if head_pairs % 4 == 0 else (2 if head_pairs % 2 == 0 else 1)
    pairs = head_pairs // chunks
    outputs = (attention, query_grad, own_dk, own_dv)
    digests = []
    for chunk in range(chunks):
        *outputs, far_dkv = fixed_attention(
            seq_scalar,
            queries,
            keys,
            values,
            grad_out,
            far_kv,
            chunk * pairs,
            pairs,
            head_pairs,
            head_dim,
            score_scale,
            outputs,
        )
        digests.append(seq_reduce_scatter(far_dkv, 1, chunk))
    attention, query_grad, own_dk, own_dv = outputs
    back_k, back_v = passed_along((back_k, back_v), "seq", -1)
    digest_dkv = jnp.concatenate(digests, 2) if chunks > 1 else digests[0]
    key_grad, value_grad = finalize(
        own_dk, own_dv, back_k, back_v, digest_dkv, select, head_pairs, head_dim
    )
    return attention, query_grad, key_grad, value_grad


def solution(mesh):
    in_specs = (
        P("seq", "head"),
        P("seq", "head"),
        P("seq", "head"),
        P("head", None),
        P(("seq", "head"), None),
        P("head", None),
    )
    out_specs = (P("seq", "head"), P("seq", "head"), P("seq", "head"), P("seq", "head"))
    return jax.shard_map(
        on_device, mesh=mesh, in_specs=in_specs, out_specs=out_specs, check_vma=False
    )
```

```python
import functools

import jax
import jax.numpy as jnp
from jax import lax
from jax.experimental import pallas as pl
from jax.experimental.pallas import tpu as pltpu
from jax.sharding import PartitionSpec as P

WIN = 256
BLOCK = 128
SUMM = 32


NEG = -1e30


def passed_along(value, axis, steps):
    count = lax.axis_size(axis)
    first, last = (max(0, -steps), min(count, count - steps))
    return lax.ppermute(value, axis, [(source, source + steps) for source in range(first, last)])


def seq_reduce_scatter(parts, axis, rotate=0):
    count = lax.axis_size("seq")
    if count & (count - 1):
        return lax.psum_scatter(
            parts.astype(jnp.bfloat16), "seq", scatter_dimension=axis, tiled=True
        )
    me = lax.axis_index("seq")
    bits = count.bit_length() - 1
    chunk = parts.shape[axis] // count
    held = parts.reshape(parts.shape[:axis] + (2,) * bits + (chunk,) + parts.shape[axis + 1 :])
    if bits > 2:
        order = [0] + sorted(range(1, bits - 1), key=lambda b: (b - 1 - rotate) % (bits - 2)) + [bits - 1]
    else:
        order = list(range(bits))
    gone = []
    for bit in order:
        where = axis + bits - 1 - bit - sum(1 for done in gone if done > bit)
        gone.append(bit)
        mine = (me >> bit) & 1
        keep = lax.dynamic_index_in_dim(held, mine, where, keepdims=False)
        send = lax.dynamic_index_in_dim(held, 1 - mine, where, keepdims=False)
        arrived = lax.ppermute(
            send.astype(jnp.bfloat16), "seq", [(source, source ^ (1 << bit)) for source in range(count)]
        )
        held = keep + arrived.astype(jnp.float32)
    return held.astype(jnp.bfloat16)


def nt(left, right):
    return lax.dot_general(left, right, (((1,), (1,)), ((), ())), preferred_element_type=jnp.float32)


def tn(left, right):
    return lax.dot_general(left, right, (((0,), (0,)), ((), ())), preferred_element_type=jnp.float32)


def nn(left, right):
    return lax.dot_general(left, right, (((1,), (0,)), ((), ())), preferred_element_type=jnp.float32)


def two_part_attention(q, g, first, second, scale):
    (k_a, v_a, mask_a), (k_b, v_b, mask_b) = first, second
    s_a = jnp.where(mask_a, nt(q, k_a) * scale, NEG)
    s_b = jnp.where(mask_b, nt(q, k_b) * scale, NEG)
    row_max = jnp.maximum(s_a.max(-1, keepdims=True), s_b.max(-1, keepdims=True))
    w_a = jnp.exp(s_a - row_max)
    w_b = jnp.exp(s_b - row_max)
    row_sum = w_a.sum(-1, keepdims=True) + w_b.sum(-1, keepdims=True)
    mixed = nn(w_a.astype(jnp.bfloat16), v_a) + nn(w_b.astype(jnp.bfloat16), v_b)
    out = (mixed / row_sum).astype(jnp.bfloat16)
    delta = jnp.sum(g.astype(jnp.float32) * out.astype(jnp.float32), -1, keepdims=True)
    inverse = 1.0 / row_sum
    p_a = w_a * inverse
    p_b = w_b * inverse
    gs_a = (p_a * (nt(g, v_a) - delta)).astype(jnp.bfloat16)
    gs_b = (p_b * (nt(g, v_b) - delta)).astype(jnp.bfloat16)
    dq = ((nn(gs_a, k_a) + nn(gs_b, k_b)) * scale).astype(jnp.bfloat16)
    dk_a = tn(gs_a, q) * scale
    dk_b = tn(gs_b, q) * scale
    dv_a = tn(p_a.astype(jnp.bfloat16), g)
    dv_b = tn(p_b.astype(jnp.bfloat16), g)
    return out, dq, (dk_a, dv_a), (dk_b, dv_b)


def band_kernel(seq_ref, q_ref, k_ref, v_ref, g_ref, kp_ref, vp_ref, out_ref, dq_ref, dk_ref, dv_ref, dkp_ref, dvp_ref, *, scale):
    rows = q_ref.shape[0]
    qi = lax.broadcasted_iota(jnp.int32, (rows, rows), 0)
    kj = lax.broadcasted_iota(jnp.int32, (rows, rows), 1)
    prev_mask = (kj > qi) & (seq_ref[0] > 0)
    own_mask = (kj <= qi) & (qi - kj < WIN)
    out, dq, (dkp, dvp), (dko, dvo) = two_part_attention(
        q_ref[...],
        g_ref[...],
        (kp_ref[...], vp_ref[...], prev_mask),
        (k_ref[...], v_ref[...], own_mask),
        scale,
    )
    out_ref[...] = out
    dq_ref[...] = dq
    dk_ref[...] = dko
    dv_ref[...] = dvo
    dkp_ref[...] = dkp.astype(dkp_ref.dtype)
    dvp_ref[...] = dvp.astype(dvp_ref.dtype)


def fixed_kernel(seq_ref, q_ref, k_ref, v_ref, g_ref, kf_ref, vf_ref, *refs, scale, unused):
    out_ref, dq_ref, dk_ref, dv_ref, dkvf_ref = refs[unused:]
    rows = q_ref.shape[0]
    far_rows = kf_ref.shape[0]
    start = seq_ref[0] * rows
    qi = lax.broadcasted_iota(jnp.int32, (rows, rows), 0)
    kj = lax.broadcasted_iota(jnp.int32, (rows, rows), 1)
    own_mask = (kj <= qi) & ((qi // BLOCK) == (kj // BLOCK))
    fq = lax.broadcasted_iota(jnp.int32, (rows, far_rows), 0)
    fr = lax.broadcasted_iota(jnp.int32, (rows, far_rows), 1)
    far_mask = (fr // SUMM) < ((start + fq) // BLOCK)
    out, dq, (dko, dvo), (dkf, dvf) = two_part_attention(
        q_ref[...],
        g_ref[...],
        (k_ref[...], v_ref[...], own_mask),
        (kf_ref[...], vf_ref[...], far_mask),
        scale,
    )
    out_ref[...] = out
    dq_ref[...] = dq
    dk_ref[...] = dko
    dv_ref[...] = dvo
    dkvf_ref[0] = dkf.astype(dkvf_ref.dtype)
    dkvf_ref[1] = dvf.astype(dkvf_ref.dtype)


def attention_cost(rows, keys, head_dim, heads):
    return pl.CostEstimate(
        flops=2 * rows * keys * head_dim * 7 * heads,
        transcendentals=3 * rows * keys * heads,
        bytes_accessed=(rows * 16 + keys * 6) * head_dim * heads,
    )


def band_attention(seq_index, q, k, v, g, k_prev, v_prev, head_pairs, head_dim, scale):
    rows = q.shape[0]
    block = pl.BlockSpec((rows, head_dim), lambda p, s: (0, 2 * p))
    narrow = pl.BlockSpec((rows, head_dim), lambda p, s: (0, p))
    width = 2 * head_pairs * head_dim
    grid_spec = pltpu.PrefetchScalarGridSpec(
        num_scalar_prefetch=1,
        grid=(head_pairs,),
        in_specs=[block] * 4 + [narrow] * 2,
        out_specs=[block] * 4 + [narrow] * 2,
    )
    return pl.pallas_call(
        functools.partial(band_kernel, scale=scale),
        grid_spec=grid_spec,
        out_shape=[
            jax.ShapeDtypeStruct((rows, width), jnp.bfloat16),
            jax.ShapeDtypeStruct((rows, width), jnp.bfloat16),
            jax.ShapeDtypeStruct((rows, width), jnp.float32),
            jax.ShapeDtypeStruct((rows, width), jnp.float32),
            jax.ShapeDtypeStruct((rows, head_pairs * head_dim), jnp.bfloat16),
            jax.ShapeDtypeStruct((rows, head_pairs * head_dim), jnp.bfloat16),
        ],
        compiler_params=pltpu.CompilerParams(vmem_limit_bytes=48 * 1024 * 1024),
        cost_estimate=attention_cost(rows, 2 * rows, head_dim, head_pairs),
    )(seq_index, q, k, v, g, k_prev, v_prev)


def fixed_attention(seq_index, q, k, v, g, far_kv, first_pair, pairs, head_pairs, head_dim, scale, earlier):
    rows = q.shape[0]
    far_rows = far_kv.shape[0]
    block = pl.BlockSpec((rows, head_dim), lambda p, s: (0, 2 * (first_pair + p) + 1))
    far_k_spec = pl.BlockSpec((far_rows, head_dim), lambda p, s: (0, first_pair + p))
    far_v_spec = pl.BlockSpec((far_rows, head_dim), lambda p, s: (0, head_pairs + first_pair + p))
    operands = [seq_index, q, k, v, g, far_kv, far_kv] + list(earlier)
    aliases = {7 + number: number for number in range(len(earlier))}
    grid_spec = pltpu.PrefetchScalarGridSpec(
        num_scalar_prefetch=1,
        grid=(pairs,),
        in_specs=[block] * 4 + [far_k_spec, far_v_spec]
        + [pl.BlockSpec(memory_space=pl.ANY)] * len(earlier),
        out_specs=[block] * 4 + [pl.BlockSpec((2, far_rows, head_dim), lambda p, s: (0, 0, p))],
    )
    return pl.pallas_call(
        functools.partial(fixed_kernel, scale=scale, unused=len(earlier)),
        grid_spec=grid_spec,
        out_shape=[jax.ShapeDtypeStruct(array.shape, array.dtype) for array in earlier]
        + [jax.ShapeDtypeStruct((2, far_rows, pairs * head_dim), jnp.bfloat16)],
        input_output_aliases=aliases,
        compiler_params=pltpu.CompilerParams(vmem_limit_bytes=48 * 1024 * 1024),
        cost_estimate=attention_cost(rows, rows + far_rows, head_dim, pairs),
    )(*operands)


def finalize_band_kernel(own_k_ref, own_v_ref, back_k_ref, back_v_ref, k_out, v_out):
    for own_ref, back_ref, out_ref in ((own_k_ref, back_k_ref, k_out), (own_v_ref, back_v_ref, v_out)):
        out_ref[...] = (own_ref[...] + back_ref[...].astype(jnp.float32)).astype(out_ref.dtype)


def finalize_fixed_kernel(own_k_ref, own_v_ref, digest_ref, select_ref, k_in, v_in, k_out, v_out):
    pick = select_ref[0]
    for own_ref, side, out_ref in ((own_k_ref, 0, k_out), (own_v_ref, 1, v_out)):
        summary = tn(pick, digest_ref[side])
        out_ref[...] = (own_ref[...] + summary).astype(out_ref.dtype)


def finalize_band(own_k, own_v, back_k, back_v, head_pairs, head_dim):
    rows = own_k.shape[0]
    band = pl.BlockSpec((rows, head_dim), lambda p: (0, 2 * p))
    narrow = pl.BlockSpec((rows, head_dim), lambda p: (0, p))
    return pl.pallas_call(
        finalize_band_kernel,
        grid=(head_pairs,),
        in_specs=[band, band, narrow, narrow],
        out_specs=[band, band],
        out_shape=[jax.ShapeDtypeStruct(own_k.shape, jnp.bfloat16)] * 2,
        cost_estimate=pl.CostEstimate(
            flops=2 * rows * head_dim * head_pairs,
            transcendentals=0,
            bytes_accessed=rows * head_dim * head_pairs * 16,
        ),
    )(own_k, own_v, back_k, back_v)


def finalize_fixed(own_k, own_v, digest, select, partial, head_pairs, head_dim):
    rows = own_k.shape[0]
    digest_rows = digest.shape[1]
    fixed = pl.BlockSpec((rows, head_dim), lambda p: (0, 2 * p + 1))
    return pl.pallas_call(
        finalize_fixed_kernel,
        grid=(head_pairs,),
        in_specs=[
            fixed,
            fixed,
            pl.BlockSpec((2, digest_rows, head_dim), lambda p: (0, 0, p)),
            pl.BlockSpec((1, digest_rows, rows), lambda p: (p, 0, 0)),
            pl.BlockSpec(memory_space=pl.ANY),
            pl.BlockSpec(memory_space=pl.ANY),
        ],
        out_specs=[fixed, fixed],
        out_shape=[jax.ShapeDtypeStruct(own_k.shape, jnp.bfloat16)] * 2,
        input_output_aliases={4: 0, 5: 1},
        cost_estimate=pl.CostEstimate(
            flops=4 * rows * digest_rows * head_dim * head_pairs,
            transcendentals=0,
            bytes_accessed=rows * head_dim * head_pairs * 12,
        ),
    )(own_k, own_v, digest, select, *partial)


def on_device(queries, keys, values, out_weight, cotangent, offsets):
    seq_rows = queries.shape[0]
    full_width = queries.shape[1]
    head_pairs = offsets.shape[0]
    head_dim = full_width // (2 * head_pairs)
    score_scale = head_dim ** (-0.5)
    assert seq_rows == WIN and seq_rows % BLOCK == 0
    seq_index = lax.axis_index("seq")
    split_k = keys.reshape(seq_rows, head_pairs, 2, head_dim)
    split_v = values.reshape(seq_rows, head_pairs, 2, head_dim)
    fixed_k = split_k[:, :, 1]
    fixed_v = split_v[:, :, 1]
    band_k = split_k[:, :, 0].reshape(seq_rows, head_pairs * head_dim)
    band_v = split_v[:, :, 0].reshape(seq_rows, head_pairs * head_dim)
    prev_k, prev_v = passed_along((band_k, band_v), "seq", 1)
    digest_count = seq_rows // BLOCK * SUMM
    offset_table = jnp.tile(offsets.T, (seq_rows // BLOCK, 1))
    digest_rows = (jnp.arange(digest_count, dtype=jnp.int32) // SUMM * BLOCK)[
        :, None
    ] + offset_table
    select = (
        digest_rows.T[:, :, None] == jnp.arange(seq_rows, dtype=jnp.int32)[None, None, :]
    ).astype(jnp.bfloat16)
    digest_k = jnp.einsum(
        "hjr,rhc->jhc", select, fixed_k, preferred_element_type=jnp.float32
    ).astype(jnp.bfloat16)
    digest_v = jnp.einsum(
        "hjr,rhc->jhc", select, fixed_v, preferred_element_type=jnp.float32
    ).astype(jnp.bfloat16)
    pair_width = head_pairs * head_dim
    far_kv = lax.all_gather(
        jnp.concatenate(
            [
                digest_k.reshape(digest_count, pair_width),
                digest_v.reshape(digest_count, pair_width),
            ],
            1,
        ),
        "seq",
        axis=0,
        tiled=True,
    )
    head_count = lax.axis_size("head")
    head_index = lax.axis_index("head")
    pieces = [cotangent] + [
        lax.ppermute(
            cotangent, "head", [(source, (source + shift) % head_count) for source in range(head_count)]
        )
        for shift in range(1, head_count)
    ]
    doubled = jnp.stack(pieces[::-1] + pieces[::-1], 0)
    gathered = lax.dynamic_slice_in_dim(doubled, head_count - 1 - head_index, head_count, 0)
    grad_out = lax.dot_general(
        gathered.reshape(seq_rows, cotangent.shape[1]),
        out_weight,
        (((1,), (1,)), ((), ())),
        preferred_element_type=jnp.float32,
    ).astype(jnp.bfloat16)
    seq_scalar = seq_index.reshape(1).astype(jnp.int32)
    attention, query_grad, own_dk, own_dv, back_k, back_v = band_attention(
        seq_scalar, queries, keys, values, grad_out, prev_k, prev_v, head_pairs, head_dim, score_scale
    )
    chunks = 4 if head_pairs % 4 == 0 else (2 if head_pairs % 2 == 0 else 1)
    pairs = head_pairs // chunks
    outputs = (attention, query_grad, own_dk, own_dv)
    digests = []
    for chunk in range(chunks):
        *outputs, far_dkv = fixed_attention(
            seq_scalar,
            queries,
            keys,
            values,
            grad_out,
            far_kv,
            chunk * pairs,
            pairs,
            head_pairs,
            head_dim,
            score_scale,
            outputs,
        )
        digests.append(seq_reduce_scatter(far_dkv, 1, chunk))
    attention, query_grad, own_dk, own_dv = outputs
    back_k, back_v = passed_along((back_k, back_v), "seq", -1)
    digest_dkv = jnp.concatenate(digests, 2) if chunks > 1 else digests[0]
    partial = finalize_band(own_dk, own_dv, back_k, back_v, head_pairs, head_dim)
    key_grad, value_grad = finalize_fixed(
        own_dk, own_dv, digest_dkv, select, partial, head_pairs, head_dim
    )
    return attention, query_grad, key_grad, value_grad


def solution(mesh):
    in_specs = (
        P("seq", "head"),
        P("seq", "head"),
        P("seq", "head"),
        P("head", None),
        P(("seq", "head"), None),
        P("head", None),
    )
    out_specs = (P("seq", "head"), P("seq", "head"), P("seq", "head"), P("seq", "head"))
    return jax.shard_map(
        on_device, mesh=mesh, in_specs=in_specs, out_specs=out_specs, check_vma=False
    )
```

```python
import functools

import jax
import jax.numpy as jnp
from jax import lax
from jax.experimental import pallas as pl
from jax.experimental.pallas import tpu as pltpu
from jax.sharding import PartitionSpec as P

WIN = 256
BLOCK = 128
SUMM = 32


NEG = -1e30


def passed_along(value, axis, steps):
    count = lax.axis_size(axis)
    first, last = (max(0, -steps), min(count, count - steps))
    return lax.ppermute(value, axis, [(source, source + steps) for source in range(first, last)])


def seq_reduce_scatter(parts, axis, rotate=0):
    count = lax.axis_size("seq")
    if count & (count - 1):
        return lax.psum_scatter(
            parts.astype(jnp.bfloat16), "seq", scatter_dimension=axis, tiled=True
        )
    me = lax.axis_index("seq")
    bits = count.bit_length() - 1
    chunk = parts.shape[axis] // count
    held = parts.reshape(parts.shape[:axis] + (2,) * bits + (chunk,) + parts.shape[axis + 1 :])
    if bits > 2:
        order = [0] + sorted(range(1, bits - 1), key=lambda b: (b - 1 - rotate) % (bits - 2)) + [bits - 1]
    else:
        order = list(range(bits))
    gone = []
    for bit in order:
        where = axis + bits - 1 - bit - sum(1 for done in gone if done > bit)
        gone.append(bit)
        mine = (me >> bit) & 1
        keep = lax.dynamic_index_in_dim(held, mine, where, keepdims=False)
        send = lax.dynamic_index_in_dim(held, 1 - mine, where, keepdims=False)
        arrived = lax.ppermute(
            send.astype(jnp.bfloat16), "seq", [(source, source ^ (1 << bit)) for source in range(count)]
        )
        held = keep + arrived.astype(jnp.float32)
    return held.astype(jnp.bfloat16)


def nt(left, right):
    return lax.dot_general(left, right, (((1,), (1,)), ((), ())), preferred_element_type=jnp.float32)


def tn(left, right):
    return lax.dot_general(left, right, (((0,), (0,)), ((), ())), preferred_element_type=jnp.float32)


def nn(left, right):
    return lax.dot_general(left, right, (((1,), (0,)), ((), ())), preferred_element_type=jnp.float32)


def two_part_attention(q, g, first, second, scale):
    (k_a, v_a, mask_a), (k_b, v_b, mask_b) = first, second
    s_a = jnp.where(mask_a, nt(q, k_a) * scale, NEG)
    s_b = jnp.where(mask_b, nt(q, k_b) * scale, NEG)
    row_max = jnp.maximum(s_a.max(-1, keepdims=True), s_b.max(-1, keepdims=True))
    w_a = jnp.exp(s_a - row_max)
    w_b = jnp.exp(s_b - row_max)
    row_sum = w_a.sum(-1, keepdims=True) + w_b.sum(-1, keepdims=True)
    mixed = nn(w_a.astype(jnp.bfloat16), v_a) + nn(w_b.astype(jnp.bfloat16), v_b)
    out = (mixed / row_sum).astype(jnp.bfloat16)
    delta = jnp.sum(g.astype(jnp.float32) * out.astype(jnp.float32), -1, keepdims=True)
    inverse = 1.0 / row_sum
    p_a = w_a * inverse
    p_b = w_b * inverse
    gs_a = (p_a * (nt(g, v_a) - delta)).astype(jnp.bfloat16)
    gs_b = (p_b * (nt(g, v_b) - delta)).astype(jnp.bfloat16)
    dq = ((nn(gs_a, k_a) + nn(gs_b, k_b)) * scale).astype(jnp.bfloat16)
    dk_a = tn(gs_a, q) * scale
    dk_b = tn(gs_b, q) * scale
    dv_a = tn(p_a.astype(jnp.bfloat16), g)
    dv_b = tn(p_b.astype(jnp.bfloat16), g)
    return out, dq, (dk_a, dv_a), (dk_b, dv_b)


def band_kernel(seq_ref, q_ref, k_ref, v_ref, g_ref, kp_ref, vp_ref, out_ref, dq_ref, dk_ref, dv_ref, dkp_ref, dvp_ref, *, scale):
    rows = q_ref.shape[0]
    qi = lax.broadcasted_iota(jnp.int32, (rows, rows), 0)
    kj = lax.broadcasted_iota(jnp.int32, (rows, rows), 1)
    prev_mask = (kj > qi) & (seq_ref[0] > 0)
    own_mask = (kj <= qi) & (qi - kj < WIN)
    out, dq, (dkp, dvp), (dko, dvo) = two_part_attention(
        q_ref[...],
        g_ref[...],
        (kp_ref[...], vp_ref[...], prev_mask),
        (k_ref[...], v_ref[...], own_mask),
        scale,
    )
    out_ref[...] = out
    dq_ref[...] = dq
    dk_ref[...] = dko
    dv_ref[...] = dvo
    dkp_ref[...] = dkp.astype(dkp_ref.dtype)
    dvp_ref[...] = dvp.astype(dvp_ref.dtype)


def fixed_kernel(seq_ref, q_ref, k_ref, v_ref, g_ref, kf_ref, vf_ref, *refs, scale, unused):
    out_ref, dq_ref, dk_ref, dv_ref, dkvf_ref = refs[unused:]
    rows = q_ref.shape[0]
    far_rows = kf_ref.shape[0]
    start = seq_ref[0] * rows
    qi = lax.broadcasted_iota(jnp.int32, (rows, rows), 0)
    kj = lax.broadcasted_iota(jnp.int32, (rows, rows), 1)
    own_mask = (kj <= qi) & ((qi // BLOCK) == (kj // BLOCK))
    fq = lax.broadcasted_iota(jnp.int32, (rows, far_rows), 0)
    fr = lax.broadcasted_iota(jnp.int32, (rows, far_rows), 1)
    far_mask = (fr // SUMM) < ((start + fq) // BLOCK)
    out, dq, (dko, dvo), (dkf, dvf) = two_part_attention(
        q_ref[...],
        g_ref[...],
        (k_ref[...], v_ref[...], own_mask),
        (kf_ref[...], vf_ref[...], far_mask),
        scale,
    )
    out_ref[...] = out
    dq_ref[...] = dq
    dk_ref[...] = dko
    dv_ref[...] = dvo
    dkvf_ref[0] = dkf.astype(dkvf_ref.dtype)
    dkvf_ref[1] = dvf.astype(dkvf_ref.dtype)


def attention_cost(rows, keys, head_dim, heads):
    return pl.CostEstimate(
        flops=2 * rows * keys * head_dim * 7 * heads,
        transcendentals=3 * rows * keys * heads,
        bytes_accessed=(rows * 16 + keys * 6) * head_dim * heads,
    )


def band_attention(seq_index, q, k, v, g, k_prev, v_prev, head_pairs, head_dim, scale):
    rows = q.shape[0]
    block = pl.BlockSpec((rows, head_dim), lambda p, s: (0, 2 * p))
    narrow = pl.BlockSpec((rows, head_dim), lambda p, s: (0, p))
    width = 2 * head_pairs * head_dim
    grid_spec = pltpu.PrefetchScalarGridSpec(
        num_scalar_prefetch=1,
        grid=(head_pairs,),
        in_specs=[block] * 4 + [narrow] * 2,
        out_specs=[block] * 4 + [narrow] * 2,
    )
    return pl.pallas_call(
        functools.partial(band_kernel, scale=scale),
        grid_spec=grid_spec,
        out_shape=[
            jax.ShapeDtypeStruct((rows, width), jnp.bfloat16),
            jax.ShapeDtypeStruct((rows, width), jnp.bfloat16),
            jax.ShapeDtypeStruct((rows, width), jnp.float32),
            jax.ShapeDtypeStruct((rows, width), jnp.float32),
            jax.ShapeDtypeStruct((rows, head_pairs * head_dim), jnp.bfloat16),
            jax.ShapeDtypeStruct((rows, head_pairs * head_dim), jnp.bfloat16),
        ],
        compiler_params=pltpu.CompilerParams(vmem_limit_bytes=48 * 1024 * 1024),
        cost_estimate=attention_cost(rows, 2 * rows, head_dim, head_pairs),
    )(seq_index, q, k, v, g, k_prev, v_prev)


def fixed_attention(seq_index, q, k, v, g, far_kv, first_pair, pairs, head_pairs, head_dim, scale, earlier):
    rows = q.shape[0]
    far_rows = far_kv.shape[0]
    block = pl.BlockSpec((rows, head_dim), lambda p, s: (0, 2 * (first_pair + p) + 1))
    far_k_spec = pl.BlockSpec((far_rows, head_dim), lambda p, s: (0, first_pair + p))
    far_v_spec = pl.BlockSpec((far_rows, head_dim), lambda p, s: (0, head_pairs + first_pair + p))
    operands = [seq_index, q, k, v, g, far_kv, far_kv] + list(earlier)
    aliases = {7 + number: number for number in range(len(earlier))}
    grid_spec = pltpu.PrefetchScalarGridSpec(
        num_scalar_prefetch=1,
        grid=(pairs,),
        in_specs=[block] * 4 + [far_k_spec, far_v_spec]
        + [pl.BlockSpec(memory_space=pl.ANY)] * len(earlier),
        out_specs=[block] * 4 + [pl.BlockSpec((2, far_rows, head_dim), lambda p, s: (0, 0, p))],
    )
    return pl.pallas_call(
        functools.partial(fixed_kernel, scale=scale, unused=len(earlier)),
        grid_spec=grid_spec,
        out_shape=[jax.ShapeDtypeStruct(array.shape, array.dtype) for array in earlier]
        + [jax.ShapeDtypeStruct((2, far_rows, pairs * head_dim), jnp.bfloat16)],
        input_output_aliases=aliases,
        compiler_params=pltpu.CompilerParams(vmem_limit_bytes=48 * 1024 * 1024),
        cost_estimate=attention_cost(rows, rows + far_rows, head_dim, pairs),
    )(*operands)


def finalize_kernel(own_k_ref, own_v_ref, back_k_ref, back_v_ref, digest_ref, select_ref, k_out, v_out):
    hd = back_k_ref.shape[1]
    pick = select_ref[0]
    for own_ref, back_ref, side, out_ref in (
        (own_k_ref, back_k_ref, 0, k_out),
        (own_v_ref, back_v_ref, 1, v_out),
    ):
        out_ref[:, :hd] = (own_ref[:, :hd] + back_ref[...].astype(jnp.float32)).astype(out_ref.dtype)
        summary = tn(pick, digest_ref[side])
        out_ref[:, hd:] = (own_ref[:, hd:] + summary).astype(out_ref.dtype)


def finalize(own_k, own_v, back_k, back_v, digest, select, head_pairs, head_dim):
    rows = own_k.shape[0]
    digest_rows = digest.shape[1]
    wide = pl.BlockSpec((rows, 2 * head_dim), lambda p: (0, p))
    narrow = pl.BlockSpec((rows, head_dim), lambda p: (0, p))
    return pl.pallas_call(
        finalize_kernel,
        grid=(head_pairs,),
        in_specs=[
            wide,
            wide,
            narrow,
            narrow,
            pl.BlockSpec((2, digest_rows, head_dim), lambda p: (0, 0, p)),
            pl.BlockSpec((1, digest_rows, rows), lambda p: (p, 0, 0)),
        ],
        out_specs=[wide, wide],
        out_shape=[jax.ShapeDtypeStruct(own_k.shape, jnp.bfloat16)] * 2,
        cost_estimate=pl.CostEstimate(
            flops=4 * rows * digest_rows * head_dim * head_pairs,
            transcendentals=0,
            bytes_accessed=rows * head_dim * head_pairs * 20,
        ),
    )(own_k, own_v, back_k, back_v, digest, select)


def on_device(queries, keys, values, out_weight, cotangent, offsets):
    seq_rows = queries.shape[0]
    full_width = queries.shape[1]
    head_pairs = offsets.shape[0]
    head_dim = full_width // (2 * head_pairs)
    score_scale = head_dim ** (-0.5)
    assert seq_rows == WIN and seq_rows % BLOCK == 0
    seq_index = lax.axis_index("seq")
    split_k = keys.reshape(seq_rows, head_pairs, 2, head_dim)
    split_v = values.reshape(seq_rows, head_pairs, 2, head_dim)
    fixed_k = split_k[:, :, 1]
    fixed_v = split_v[:, :, 1]
    band_k = split_k[:, :, 0].reshape(seq_rows, head_pairs * head_dim)
    band_v = split_v[:, :, 0].reshape(seq_rows, head_pairs * head_dim)
    prev_k, prev_v = passed_along((band_k, band_v), "seq", 1)
    digest_count = seq_rows // BLOCK * SUMM
    offset_table = jnp.tile(offsets.T, (seq_rows // BLOCK, 1))
    digest_rows = (jnp.arange(digest_count, dtype=jnp.int32) // SUMM * BLOCK)[
        :, None
    ] + offset_table
    select = (
        digest_rows.T[:, :, None] == jnp.arange(seq_rows, dtype=jnp.int32)[None, None, :]
    ).astype(jnp.bfloat16)
    digest_k = jnp.einsum(
        "hjr,rhc->jhc", select, fixed_k, preferred_element_type=jnp.float32
    ).astype(jnp.bfloat16)
    digest_v = jnp.einsum(
        "hjr,rhc->jhc", select, fixed_v, preferred_element_type=jnp.float32
    ).astype(jnp.bfloat16)
    pair_width = head_pairs * head_dim
    far_kv = lax.all_gather(
        jnp.concatenate(
            [
                digest_k.reshape(digest_count, pair_width),
                digest_v.reshape(digest_count, pair_width),
            ],
            1,
        ),
        "seq",
        axis=0,
        tiled=True,
    )
    head_count = lax.axis_size("head")
    head_index = lax.axis_index("head")
    pieces = [cotangent] + [
        lax.ppermute(
            cotangent, "head", [(source, (source + shift) % head_count) for source in range(head_count)]
        )
        for shift in range(1, head_count)
    ]
    doubled = jnp.stack(pieces[::-1] + pieces[::-1], 0)
    gathered = lax.dynamic_slice_in_dim(doubled, head_count - 1 - head_index, head_count, 0)
    grad_out = lax.dot_general(
        gathered.reshape(seq_rows, cotangent.shape[1]),
        out_weight,
        (((1,), (1,)), ((), ())),
        preferred_element_type=jnp.float32,
    ).astype(jnp.bfloat16)
    seq_scalar = seq_index.reshape(1).astype(jnp.int32)
    attention, query_grad, own_dk, own_dv, back_k, back_v = band_attention(
        seq_scalar, queries, keys, values, grad_out, prev_k, prev_v, head_pairs, head_dim, score_scale
    )
    back_k, back_v = passed_along((back_k, back_v), "seq", -1)
    back_k, back_v, far_kv = lax.optimization_barrier((back_k, back_v, far_kv))
    chunks = 4 if head_pairs % 4 == 0 else (2 if head_pairs % 2 == 0 else 1)
    pairs = head_pairs // chunks
    outputs = (attention, query_grad, own_dk, own_dv)
    digests = []
    for chunk in range(chunks):
        *outputs, far_dkv = fixed_attention(
            seq_scalar,
            queries,
            keys,
            values,
            grad_out,
            far_kv,
            chunk * pairs,
            pairs,
            head_pairs,
            head_dim,
            score_scale,
            outputs,
        )
        digests.append(seq_reduce_scatter(far_dkv, 1, chunk))
    attention, query_grad, own_dk, own_dv = outputs
    digest_dkv = jnp.concatenate(digests, 2) if chunks > 1 else digests[0]
    key_grad, value_grad = finalize(
        own_dk, own_dv, back_k, back_v, digest_dkv, select, head_pairs, head_dim
    )
    return attention, query_grad, key_grad, value_grad


def solution(mesh):
    in_specs = (
        P("seq", "head"),
        P("seq", "head"),
        P("seq", "head"),
        P("head", None),
        P(("seq", "head"), None),
        P("head", None),
    )
    out_specs = (P("seq", "head"), P("seq", "head"), P("seq", "head"), P("seq", "head"))
    return jax.shard_map(
        on_device, mesh=mesh, in_specs=in_specs, out_specs=out_specs, check_vma=False
    )
```

```python
import functools

import jax
import jax.numpy as jnp
from jax import lax
from jax.experimental import pallas as pl
from jax.experimental.pallas import tpu as pltpu
from jax.sharding import PartitionSpec as P

WIN = 256
BLOCK = 128
SUMM = 32


NEG = -1e30


def passed_along(value, axis, steps):
    count = lax.axis_size(axis)
    first, last = (max(0, -steps), min(count, count - steps))
    return lax.ppermute(value, axis, [(source, source + steps) for source in range(first, last)])


def seq_reduce_scatter(parts, axis, rotate=0):
    count = lax.axis_size("seq")
    if count & (count - 1):
        return lax.psum_scatter(
            parts.astype(jnp.bfloat16), "seq", scatter_dimension=axis, tiled=True
        )
    me = lax.axis_index("seq")
    bits = count.bit_length() - 1
    chunk = parts.shape[axis] // count
    held = parts.reshape(parts.shape[:axis] + (2,) * bits + (chunk,) + parts.shape[axis + 1 :])
    order = rotated_order(bits, rotate)
    gone = []
    for bit in order:
        where = axis + bits - 1 - bit - sum(1 for done in gone if done > bit)
        gone.append(bit)
        mine = (me >> bit) & 1
        keep = lax.dynamic_index_in_dim(held, mine, where, keepdims=False)
        send = lax.dynamic_index_in_dim(held, 1 - mine, where, keepdims=False)
        arrived = lax.ppermute(
            send.astype(jnp.bfloat16), "seq", [(source, source ^ (1 << bit)) for source in range(count)]
        )
        held = keep + arrived.astype(jnp.float32)
    return held.astype(jnp.bfloat16)


def seq_all_gather(local, rotate):
    count = lax.axis_size("seq")
    if count & (count - 1):
        return lax.all_gather(local, "seq", axis=0, tiled=True)
    me = lax.axis_index("seq")
    bits = count.bit_length() - 1
    order = rotated_order(bits, rotate)[::-1]
    held = local
    for step, bit in enumerate(order):
        mine = (me >> bit) & 1
        arrived = lax.ppermute(held, "seq", [(source, source ^ (1 << bit)) for source in range(count)])
        pair = jnp.stack([held, arrived], step)
        swapped = jnp.stack([arrived, held], step)
        held = jnp.where(mine == 0, pair, swapped)
    axes = [order.index(b) for b in range(bits - 1, -1, -1)]
    held = held.transpose(axes + list(range(bits, held.ndim)))
    return held.reshape((count * local.shape[0],) + local.shape[1:])


def rotated_order(bits, rotate):
    if bits > 2:
        return [0] + sorted(range(1, bits - 1), key=lambda b: (b - 1 - rotate) % (bits - 2)) + [bits - 1]
    return list(range(bits))


def nt(left, right):
    return lax.dot_general(left, right, (((1,), (1,)), ((), ())), preferred_element_type=jnp.float32)


def tn(left, right):
    return lax.dot_general(left, right, (((0,), (0,)), ((), ())), preferred_element_type=jnp.float32)


def nn(left, right):
    return lax.dot_general(left, right, (((1,), (0,)), ((), ())), preferred_element_type=jnp.float32)


def two_part_attention(q, g, first, second, scale):
    (k_a, v_a, mask_a), (k_b, v_b, mask_b) = first, second
    s_a = jnp.where(mask_a, nt(q, k_a) * scale, NEG)
    s_b = jnp.where(mask_b, nt(q, k_b) * scale, NEG)
    row_max = jnp.maximum(s_a.max(-1, keepdims=True), s_b.max(-1, keepdims=True))
    w_a = jnp.exp(s_a - row_max)
    w_b = jnp.exp(s_b - row_max)
    row_sum = w_a.sum(-1, keepdims=True) + w_b.sum(-1, keepdims=True)
    mixed = nn(w_a.astype(jnp.bfloat16), v_a) + nn(w_b.astype(jnp.bfloat16), v_b)
    out = (mixed / row_sum).astype(jnp.bfloat16)
    delta = jnp.sum(g.astype(jnp.float32) * out.astype(jnp.float32), -1, keepdims=True)
    inverse = 1.0 / row_sum
    p_a = w_a * inverse
    p_b = w_b * inverse
    gs_a = (p_a * (nt(g, v_a) - delta)).astype(jnp.bfloat16)
    gs_b = (p_b * (nt(g, v_b) - delta)).astype(jnp.bfloat16)
    dq = ((nn(gs_a, k_a) + nn(gs_b, k_b)) * scale).astype(jnp.bfloat16)
    dk_a = tn(gs_a, q) * scale
    dk_b = tn(gs_b, q) * scale
    dv_a = tn(p_a.astype(jnp.bfloat16), g)
    dv_b = tn(p_b.astype(jnp.bfloat16), g)
    return out, dq, (dk_a, dv_a), (dk_b, dv_b)


def band_kernel(seq_ref, q_ref, k_ref, v_ref, g_ref, kp_ref, vp_ref, out_ref, dq_ref, dk_ref, dv_ref, dkp_ref, dvp_ref, *, scale):
    rows = q_ref.shape[0]
    qi = lax.broadcasted_iota(jnp.int32, (rows, rows), 0)
    kj = lax.broadcasted_iota(jnp.int32, (rows, rows), 1)
    prev_mask = (kj > qi) & (seq_ref[0] > 0)
    own_mask = (kj <= qi) & (qi - kj < WIN)
    out, dq, (dkp, dvp), (dko, dvo) = two_part_attention(
        q_ref[...],
        g_ref[...],
        (kp_ref[...], vp_ref[...], prev_mask),
        (k_ref[...], v_ref[...], own_mask),
        scale,
    )
    out_ref[...] = out
    dq_ref[...] = dq
    dk_ref[...] = dko
    dv_ref[...] = dvo
    dkp_ref[...] = dkp.astype(dkp_ref.dtype)
    dvp_ref[...] = dvp.astype(dvp_ref.dtype)


def fixed_kernel(seq_ref, q_ref, k_ref, v_ref, g_ref, kf_ref, vf_ref, *refs, scale, unused):
    out_ref, dq_ref, dk_ref, dv_ref, dkvf_ref = refs[unused:]
    rows = q_ref.shape[0]
    far_rows = kf_ref.shape[0]
    start = seq_ref[0] * rows
    qi = lax.broadcasted_iota(jnp.int32, (rows, rows), 0)
    kj = lax.broadcasted_iota(jnp.int32, (rows, rows), 1)
    own_mask = (kj <= qi) & ((qi // BLOCK) == (kj // BLOCK))
    fq = lax.broadcasted_iota(jnp.int32, (rows, far_rows), 0)
    fr = lax.broadcasted_iota(jnp.int32, (rows, far_rows), 1)
    far_mask = (fr // SUMM) < ((start + fq) // BLOCK)
    out, dq, (dko, dvo), (dkf, dvf) = two_part_attention(
        q_ref[...],
        g_ref[...],
        (k_ref[...], v_ref[...], own_mask),
        (kf_ref[...], vf_ref[...], far_mask),
        scale,
    )
    out_ref[...] = out
    dq_ref[...] = dq
    dk_ref[...] = dko
    dv_ref[...] = dvo
    dkvf_ref[0] = dkf.astype(dkvf_ref.dtype)
    dkvf_ref[1] = dvf.astype(dkvf_ref.dtype)


def attention_cost(rows, keys, head_dim, heads):
    return pl.CostEstimate(
        flops=2 * rows * keys * head_dim * 7 * heads,
        transcendentals=3 * rows * keys * heads,
        bytes_accessed=(rows * 16 + keys * 6) * head_dim * heads,
    )


def band_attention(seq_index, q, k, v, g, k_prev, v_prev, head_pairs, head_dim, scale):
    rows = q.shape[0]
    block = pl.BlockSpec((rows, head_dim), lambda p, s: (0, 2 * p))
    narrow = pl.BlockSpec((rows, head_dim), lambda p, s: (0, p))
    width = 2 * head_pairs * head_dim
    grid_spec = pltpu.PrefetchScalarGridSpec(
        num_scalar_prefetch=1,
        grid=(head_pairs,),
        in_specs=[block] * 4 + [narrow] * 2,
        out_specs=[block] * 4 + [narrow] * 2,
    )
    return pl.pallas_call(
        functools.partial(band_kernel, scale=scale),
        grid_spec=grid_spec,
        out_shape=[
            jax.ShapeDtypeStruct((rows, width), jnp.bfloat16),
            jax.ShapeDtypeStruct((rows, width), jnp.bfloat16),
            jax.ShapeDtypeStruct((rows, width), jnp.float32),
            jax.ShapeDtypeStruct((rows, width), jnp.float32),
            jax.ShapeDtypeStruct((rows, head_pairs * head_dim), jnp.bfloat16),
            jax.ShapeDtypeStruct((rows, head_pairs * head_dim), jnp.bfloat16),
        ],
        compiler_params=pltpu.CompilerParams(vmem_limit_bytes=48 * 1024 * 1024),
        cost_estimate=attention_cost(rows, 2 * rows, head_dim, head_pairs),
    )(seq_index, q, k, v, g, k_prev, v_prev)


def fixed_attention(seq_index, q, k, v, g, far_kv, first_pair, pairs, far_first, head_dim, scale, earlier):
    rows = q.shape[0]
    far_rows = far_kv.shape[0]
    far_pairs = far_kv.shape[1] // (2 * head_dim)
    block = pl.BlockSpec((rows, head_dim), lambda p, s: (0, 2 * (first_pair + p) + 1))
    far_k_spec = pl.BlockSpec((far_rows, head_dim), lambda p, s: (0, far_first + p))
    far_v_spec = pl.BlockSpec((far_rows, head_dim), lambda p, s: (0, far_pairs + far_first + p))
    operands = [seq_index, q, k, v, g, far_kv, far_kv] + list(earlier)
    aliases = {7 + number: number for number in range(len(earlier))}
    grid_spec = pltpu.PrefetchScalarGridSpec(
        num_scalar_prefetch=1,
        grid=(pairs,),
        in_specs=[block] * 4 + [far_k_spec, far_v_spec]
        + [pl.BlockSpec(memory_space=pl.ANY)] * len(earlier),
        out_specs=[block] * 4 + [pl.BlockSpec((2, far_rows, head_dim), lambda p, s: (0, 0, p))],
    )
    return pl.pallas_call(
        functools.partial(fixed_kernel, scale=scale, unused=len(earlier)),
        grid_spec=grid_spec,
        out_shape=[jax.ShapeDtypeStruct(array.shape, array.dtype) for array in earlier]
        + [jax.ShapeDtypeStruct((2, far_rows, pairs * head_dim), jnp.bfloat16)],
        input_output_aliases=aliases,
        compiler_params=pltpu.CompilerParams(vmem_limit_bytes=48 * 1024 * 1024),
        cost_estimate=attention_cost(rows, rows + far_rows, head_dim, pairs),
    )(*operands)


def finalize_kernel(own_k_ref, own_v_ref, back_k_ref, back_v_ref, digest_ref, select_ref, k_out, v_out):
    hd = back_k_ref.shape[1]
    pick = select_ref[0]
    for own_ref, back_ref, side, out_ref in (
        (own_k_ref, back_k_ref, 0, k_out),
        (own_v_ref, back_v_ref, 1, v_out),
    ):
        out_ref[:, :hd] = (own_ref[:, :hd] + back_ref[...].astype(jnp.float32)).astype(out_ref.dtype)
        summary = tn(pick, digest_ref[side])
        out_ref[:, hd:] = (own_ref[:, hd:] + summary).astype(out_ref.dtype)


def finalize(own_k, own_v, back_k, back_v, digest, select, head_pairs, head_dim):
    rows = own_k.shape[0]
    digest_rows = digest.shape[1]
    wide = pl.BlockSpec((rows, 2 * head_dim), lambda p: (0, p))
    narrow = pl.BlockSpec((rows, head_dim), lambda p: (0, p))
    return pl.pallas_call(
        finalize_kernel,
        grid=(head_pairs,),
        in_specs=[
            wide,
            wide,
            narrow,
            narrow,
            pl.BlockSpec((2, digest_rows, head_dim), lambda p: (0, 0, p)),
            pl.BlockSpec((1, digest_rows, rows), lambda p: (p, 0, 0)),
        ],
        out_specs=[wide, wide],
        out_shape=[jax.ShapeDtypeStruct(own_k.shape, jnp.bfloat16)] * 2,
        cost_estimate=pl.CostEstimate(
            flops=4 * rows * digest_rows * head_dim * head_pairs,
            transcendentals=0,
            bytes_accessed=rows * head_dim * head_pairs * 20,
        ),
    )(own_k, own_v, back_k, back_v, digest, select)


def on_device(queries, keys, values, out_weight, cotangent, offsets):
    seq_rows = queries.shape[0]
    full_width = queries.shape[1]
    head_pairs = offsets.shape[0]
    head_dim = full_width // (2 * head_pairs)
    score_scale = head_dim ** (-0.5)
    assert seq_rows == WIN and seq_rows % BLOCK == 0
    seq_index = lax.axis_index("seq")
    split_k = keys.reshape(seq_rows, head_pairs, 2, head_dim)
    split_v = values.reshape(seq_rows, head_pairs, 2, head_dim)
    fixed_k = split_k[:, :, 1]
    fixed_v = split_v[:, :, 1]
    band_k = split_k[:, :, 0].reshape(seq_rows, head_pairs * head_dim)
    band_v = split_v[:, :, 0].reshape(seq_rows, head_pairs * head_dim)
    prev_k, prev_v = passed_along((band_k, band_v), "seq", 1)
    digest_count = seq_rows // BLOCK * SUMM
    offset_table = jnp.tile(offsets.T, (seq_rows // BLOCK, 1))
    digest_rows = (jnp.arange(digest_count, dtype=jnp.int32) // SUMM * BLOCK)[
        :, None
    ] + offset_table
    select = (
        digest_rows.T[:, :, None] == jnp.arange(seq_rows, dtype=jnp.int32)[None, None, :]
    ).astype(jnp.bfloat16)
    digest_k = jnp.einsum(
        "hjr,rhc->jhc", select, fixed_k, preferred_element_type=jnp.float32
    ).astype(jnp.bfloat16)
    digest_v = jnp.einsum(
        "hjr,rhc->jhc", select, fixed_v, preferred_element_type=jnp.float32
    ).astype(jnp.bfloat16)
    gathers = 2 if head_pairs % 2 == 0 else 1
    gather_pairs = head_pairs // gathers
    split_dk = digest_k.reshape(digest_count, gathers, gather_pairs * head_dim)
    split_dv = digest_v.reshape(digest_count, gathers, gather_pairs * head_dim)
    far_parts = []
    for part in range(gathers):
        joined = jnp.concatenate([split_dk[:, part], split_dv[:, part]], 1)
        if part == 0:
            far_parts.append(lax.all_gather(joined, "seq", axis=0, tiled=True))
        else:
            far_parts.append(seq_all_gather(joined, 0))
    head_count = lax.axis_size("head")
    head_index = lax.axis_index("head")
    pieces = [cotangent] + [
        lax.ppermute(
            cotangent, "head", [(source, (source + shift) % head_count) for source in range(head_count)]
        )
        for shift in range(1, head_count)
    ]
    doubled = jnp.stack(pieces[::-1] + pieces[::-1], 0)
    gathered = lax.dynamic_slice_in_dim(doubled, head_count - 1 - head_index, head_count, 0)
    grad_out = lax.dot_general(
        gathered.reshape(seq_rows, cotangent.shape[1]),
        out_weight,
        (((1,), (1,)), ((), ())),
        preferred_element_type=jnp.float32,
    ).astype(jnp.bfloat16)
    seq_scalar = seq_index.reshape(1).astype(jnp.int32)
    attention, query_grad, own_dk, own_dv, back_k, back_v = band_attention(
        seq_scalar, queries, keys, values, grad_out, prev_k, prev_v, head_pairs, head_dim, score_scale
    )
    chunks = 4 if head_pairs % 4 == 0 else (2 if head_pairs % 2 == 0 else 1)
    pairs = head_pairs // chunks
    outputs = (attention, query_grad, own_dk, own_dv)
    digests = []
    for chunk in range(chunks):
        part = chunk * pairs // gather_pairs
        *outputs, far_dkv = fixed_attention(
            seq_scalar,
            queries,
            keys,
            values,
            grad_out,
            far_parts[part],
            chunk * pairs,
            pairs,
            chunk * pairs - part * gather_pairs,
            head_dim,
            score_scale,
            outputs,
        )
        digests.append(seq_reduce_scatter(far_dkv, 1, chunk))
    attention, query_grad, own_dk, own_dv = outputs
    back_k, back_v = passed_along((back_k, back_v), "seq", -1)
    digest_dkv = jnp.concatenate(digests, 2) if chunks > 1 else digests[0]
    key_grad, value_grad = finalize(
        own_dk, own_dv, back_k, back_v, digest_dkv, select, head_pairs, head_dim
    )
    return attention, query_grad, key_grad, value_grad


def solution(mesh):
    in_specs = (
        P("seq", "head"),
        P("seq", "head"),
        P("seq", "head"),
        P("head", None),
        P(("seq", "head"), None),
        P("head", None),
    )
    out_specs = (P("seq", "head"), P("seq", "head"), P("seq", "head"), P("seq", "head"))
    return jax.shard_map(
        on_device, mesh=mesh, in_specs=in_specs, out_specs=out_specs, check_vma=False
    )
```

```python
import functools

import jax
import jax.numpy as jnp
from jax import lax
from jax.experimental import pallas as pl
from jax.experimental.pallas import tpu as pltpu
from jax.sharding import PartitionSpec as P

WIN = 256
BLOCK = 128
SUMM = 32


NEG = -1e30


def passed_along(value, axis, steps):
    count = lax.axis_size(axis)
    first, last = (max(0, -steps), min(count, count - steps))
    return lax.ppermute(value, axis, [(source, source + steps) for source in range(first, last)])


def seq_reduce_scatter(parts, axis, rotate=0):
    count = lax.axis_size("seq")
    if count & (count - 1):
        return lax.psum_scatter(
            parts.astype(jnp.bfloat16), "seq", scatter_dimension=axis, tiled=True
        )
    me = lax.axis_index("seq")
    bits = count.bit_length() - 1
    chunk = parts.shape[axis] // count
    held = parts.reshape(parts.shape[:axis] + (2,) * bits + (chunk,) + parts.shape[axis + 1 :])
    if bits > 2:
        order = [0] + sorted(range(1, bits - 1), key=lambda b: (b - 1 - rotate) % (bits - 2)) + [bits - 1]
    else:
        order = list(range(bits))
    gone = []
    for bit in order:
        where = axis + bits - 1 - bit - sum(1 for done in gone if done > bit)
        gone.append(bit)
        mine = (me >> bit) & 1
        keep = lax.dynamic_index_in_dim(held, mine, where, keepdims=False)
        send = lax.dynamic_index_in_dim(held, 1 - mine, where, keepdims=False)
        arrived = lax.ppermute(
            send.astype(jnp.bfloat16), "seq", [(source, source ^ (1 << bit)) for source in range(count)]
        )
        held = keep + arrived.astype(jnp.float32)
    return held.astype(jnp.bfloat16)


def nt(left, right):
    return lax.dot_general(left, right, (((1,), (1,)), ((), ())), preferred_element_type=jnp.float32)


def tn(left, right):
    return lax.dot_general(left, right, (((0,), (0,)), ((), ())), preferred_element_type=jnp.float32)


def nn(left, right):
    return lax.dot_general(left, right, (((1,), (0,)), ((), ())), preferred_element_type=jnp.float32)


def two_part_attention(q, g, first, second, scale):
    (k_a, v_a, mask_a), (k_b, v_b, mask_b) = first, second
    s_a = jnp.where(mask_a, nt(q, k_a) * scale, NEG)
    s_b = jnp.where(mask_b, nt(q, k_b) * scale, NEG)
    row_max = jnp.maximum(s_a.max(-1, keepdims=True), s_b.max(-1, keepdims=True))
    w_a = jnp.exp(s_a - row_max)
    w_b = jnp.exp(s_b - row_max)
    row_sum = w_a.sum(-1, keepdims=True) + w_b.sum(-1, keepdims=True)
    mixed = nn(w_a.astype(jnp.bfloat16), v_a) + nn(w_b.astype(jnp.bfloat16), v_b)
    out = (mixed / row_sum).astype(jnp.bfloat16)
    delta = jnp.sum(g.astype(jnp.float32) * out.astype(jnp.float32), -1, keepdims=True)
    inverse = 1.0 / row_sum
    p_a = w_a * inverse
    p_b = w_b * inverse
    gs_a = (p_a * (nt(g, v_a) - delta)).astype(jnp.bfloat16)
    gs_b = (p_b * (nt(g, v_b) - delta)).astype(jnp.bfloat16)
    dq = ((nn(gs_a, k_a) + nn(gs_b, k_b)) * scale).astype(jnp.bfloat16)
    dk_a = tn(gs_a, q) * scale
    dk_b = tn(gs_b, q) * scale
    dv_a = tn(p_a.astype(jnp.bfloat16), g)
    dv_b = tn(p_b.astype(jnp.bfloat16), g)
    return out, dq, (dk_a, dv_a), (dk_b, dv_b)


def band_kernel(seq_ref, q_ref, k_ref, v_ref, g_ref, kvp_ref, out_ref, dq_ref, dk_ref, dv_ref, dkvp_ref, *, scale):
    rows = q_ref.shape[0]
    qi = lax.broadcasted_iota(jnp.int32, (rows, rows), 0)
    kj = lax.broadcasted_iota(jnp.int32, (rows, rows), 1)
    prev_mask = (kj > qi) & (seq_ref[0] > 0)
    own_mask = (kj <= qi) & (qi - kj < WIN)
    out, dq, (dkp, dvp), (dko, dvo) = two_part_attention(
        q_ref[...],
        g_ref[...],
        (kvp_ref[0], kvp_ref[1], prev_mask),
        (k_ref[...], v_ref[...], own_mask),
        scale,
    )
    out_ref[...] = out
    dq_ref[...] = dq
    dk_ref[...] = dko
    dv_ref[...] = dvo
    dkvp_ref[0] = dkp.astype(dkvp_ref.dtype)
    dkvp_ref[1] = dvp.astype(dkvp_ref.dtype)


def fixed_kernel(seq_ref, q_ref, k_ref, v_ref, g_ref, kf_ref, vf_ref, *refs, scale, unused):
    out_ref, dq_ref, dk_ref, dv_ref, dkvf_ref = refs[unused:]
    rows = q_ref.shape[0]
    far_rows = kf_ref.shape[0]
    start = seq_ref[0] * rows
    qi = lax.broadcasted_iota(jnp.int32, (rows, rows), 0)
    kj = lax.broadcasted_iota(jnp.int32, (rows, rows), 1)
    own_mask = (kj <= qi) & ((qi // BLOCK) == (kj // BLOCK))
    fq = lax.broadcasted_iota(jnp.int32, (rows, far_rows), 0)
    fr = lax.broadcasted_iota(jnp.int32, (rows, far_rows), 1)
    far_mask = (fr // SUMM) < ((start + fq) // BLOCK)
    out, dq, (dko, dvo), (dkf, dvf) = two_part_attention(
        q_ref[...],
        g_ref[...],
        (k_ref[...], v_ref[...], own_mask),
        (kf_ref[...], vf_ref[...], far_mask),
        scale,
    )
    out_ref[...] = out
    dq_ref[...] = dq
    dk_ref[...] = dko
    dv_ref[...] = dvo
    dkvf_ref[0] = dkf.astype(dkvf_ref.dtype)
    dkvf_ref[1] = dvf.astype(dkvf_ref.dtype)


def attention_cost(rows, keys, head_dim, heads):
    return pl.CostEstimate(
        flops=2 * rows * keys * head_dim * 7 * heads,
        transcendentals=3 * rows * keys * heads,
        bytes_accessed=(rows * 16 + keys * 6) * head_dim * heads,
    )


def band_attention(seq_index, q, k, v, g, kv_prev, head_pairs, head_dim, scale):
    rows = q.shape[0]
    block = pl.BlockSpec((rows, head_dim), lambda p, s: (0, 2 * p))
    narrow = pl.BlockSpec((2, rows, head_dim), lambda p, s: (0, 0, p))
    width = 2 * head_pairs * head_dim
    grid_spec = pltpu.PrefetchScalarGridSpec(
        num_scalar_prefetch=1,
        grid=(head_pairs,),
        in_specs=[block] * 4 + [narrow],
        out_specs=[block] * 4 + [narrow],
    )
    return pl.pallas_call(
        functools.partial(band_kernel, scale=scale),
        grid_spec=grid_spec,
        out_shape=[
            jax.ShapeDtypeStruct((rows, width), jnp.bfloat16),
            jax.ShapeDtypeStruct((rows, width), jnp.bfloat16),
            jax.ShapeDtypeStruct((rows, width), jnp.float32),
            jax.ShapeDtypeStruct((rows, width), jnp.float32),
            jax.ShapeDtypeStruct((2, rows, head_pairs * head_dim), jnp.bfloat16),
        ],
        compiler_params=pltpu.CompilerParams(vmem_limit_bytes=48 * 1024 * 1024),
        cost_estimate=attention_cost(rows, 2 * rows, head_dim, head_pairs),
    )(seq_index, q, k, v, g, kv_prev)


def fixed_attention(seq_index, q, k, v, g, far_kv, first_pair, pairs, head_pairs, head_dim, scale, earlier):
    rows = q.shape[0]
    far_rows = far_kv.shape[0]
    block = pl.BlockSpec((rows, head_dim), lambda p, s: (0, 2 * (first_pair + p) + 1))
    far_k_spec = pl.BlockSpec((far_rows, head_dim), lambda p, s: (0, first_pair + p))
    far_v_spec = pl.BlockSpec((far_rows, head_dim), lambda p, s: (0, head_pairs + first_pair + p))
    operands = [seq_index, q, k, v, g, far_kv, far_kv] + list(earlier)
    aliases = {7 + number: number for number in range(len(earlier))}
    grid_spec = pltpu.PrefetchScalarGridSpec(
        num_scalar_prefetch=1,
        grid=(pairs,),
        in_specs=[block] * 4 + [far_k_spec, far_v_spec]
        + [pl.BlockSpec(memory_space=pl.ANY)] * len(earlier),
        out_specs=[block] * 4 + [pl.BlockSpec((2, far_rows, head_dim), lambda p, s: (0, 0, p))],
    )
    return pl.pallas_call(
        functools.partial(fixed_kernel, scale=scale, unused=len(earlier)),
        grid_spec=grid_spec,
        out_shape=[jax.ShapeDtypeStruct(array.shape, array.dtype) for array in earlier]
        + [jax.ShapeDtypeStruct((2, far_rows, pairs * head_dim), jnp.bfloat16)],
        input_output_aliases=aliases,
        compiler_params=pltpu.CompilerParams(vmem_limit_bytes=48 * 1024 * 1024),
        cost_estimate=attention_cost(rows, rows + far_rows, head_dim, pairs),
    )(*operands)


def finalize_kernel(own_k_ref, own_v_ref, back_ref, digest_ref, select_ref, k_out, v_out):
    hd = back_ref.shape[2]
    pick = select_ref[0]
    for own_ref, side, out_ref in ((own_k_ref, 0, k_out), (own_v_ref, 1, v_out)):
        out_ref[:, :hd] = (own_ref[:, :hd] + back_ref[side].astype(jnp.float32)).astype(out_ref.dtype)
        summary = tn(pick, digest_ref[side])
        out_ref[:, hd:] = (own_ref[:, hd:] + summary).astype(out_ref.dtype)


def finalize(own_k, own_v, back_kv, digest, select, head_pairs, head_dim):
    rows = own_k.shape[0]
    digest_rows = digest.shape[1]
    wide = pl.BlockSpec((rows, 2 * head_dim), lambda p: (0, p))
    narrow = pl.BlockSpec((2, rows, head_dim), lambda p: (0, 0, p))
    return pl.pallas_call(
        finalize_kernel,
        grid=(head_pairs,),
        in_specs=[
            wide,
            wide,
            narrow,
            pl.BlockSpec((2, digest_rows, head_dim), lambda p: (0, 0, p)),
            pl.BlockSpec((1, digest_rows, rows), lambda p: (p, 0, 0)),
        ],
        out_specs=[wide, wide],
        out_shape=[jax.ShapeDtypeStruct(own_k.shape, jnp.bfloat16)] * 2,
        cost_estimate=pl.CostEstimate(
            flops=4 * rows * digest_rows * head_dim * head_pairs,
            transcendentals=0,
            bytes_accessed=rows * head_dim * head_pairs * 20,
        ),
    )(own_k, own_v, back_kv, digest, select)


def on_device(queries, keys, values, out_weight, cotangent, offsets):
    seq_rows = queries.shape[0]
    full_width = queries.shape[1]
    head_pairs = offsets.shape[0]
    head_dim = full_width // (2 * head_pairs)
    score_scale = head_dim ** (-0.5)
    assert seq_rows == WIN and seq_rows % BLOCK == 0
    seq_index = lax.axis_index("seq")
    split_k = keys.reshape(seq_rows, head_pairs, 2, head_dim)
    split_v = values.reshape(seq_rows, head_pairs, 2, head_dim)
    fixed_k = split_k[:, :, 1]
    fixed_v = split_v[:, :, 1]
    band_kv = jnp.stack([split_k[:, :, 0], split_v[:, :, 0]], 0).reshape(
        2, seq_rows, head_pairs * head_dim
    )
    prev_kv = passed_along(band_kv, "seq", 1)
    digest_count = seq_rows // BLOCK * SUMM
    offset_table = jnp.tile(offsets.T, (seq_rows // BLOCK, 1))
    digest_rows = (jnp.arange(digest_count, dtype=jnp.int32) // SUMM * BLOCK)[
        :, None
    ] + offset_table
    select = (
        digest_rows.T[:, :, None] == jnp.arange(seq_rows, dtype=jnp.int32)[None, None, :]
    ).astype(jnp.bfloat16)
    digest_k = jnp.einsum(
        "hjr,rhc->jhc", select, fixed_k, preferred_element_type=jnp.float32
    ).astype(jnp.bfloat16)
    digest_v = jnp.einsum(
        "hjr,rhc->jhc", select, fixed_v, preferred_element_type=jnp.float32
    ).astype(jnp.bfloat16)
    pair_width = head_pairs * head_dim
    far_kv = lax.all_gather(
        jnp.concatenate(
            [
                digest_k.reshape(digest_count, pair_width),
                digest_v.reshape(digest_count, pair_width),
            ],
            1,
        ),
        "seq",
        axis=0,
        tiled=True,
    )
    head_count = lax.axis_size("head")
    head_index = lax.axis_index("head")
    pieces = [cotangent] + [
        lax.ppermute(
            cotangent, "head", [(source, (source + shift) % head_count) for source in range(head_count)]
        )
        for shift in range(1, head_count)
    ]
    doubled = jnp.stack(pieces[::-1] + pieces[::-1], 0)
    gathered = lax.dynamic_slice_in_dim(doubled, head_count - 1 - head_index, head_count, 0)
    grad_out = lax.dot_general(
        gathered.reshape(seq_rows, cotangent.shape[1]),
        out_weight,
        (((1,), (1,)), ((), ())),
        preferred_element_type=jnp.float32,
    ).astype(jnp.bfloat16)
    seq_scalar = seq_index.reshape(1).astype(jnp.int32)
    attention, query_grad, own_dk, own_dv, back_kv = band_attention(
        seq_scalar, queries, keys, values, grad_out, prev_kv, head_pairs, head_dim, score_scale
    )
    chunks = 4 if head_pairs % 4 == 0 else (2 if head_pairs % 2 == 0 else 1)
    pairs = head_pairs // chunks
    outputs = (attention, query_grad, own_dk, own_dv)
    digests = []
    for chunk in range(chunks):
        *outputs, far_dkv = fixed_attention(
            seq_scalar,
            queries,
            keys,
            values,
            grad_out,
            far_kv,
            chunk * pairs,
            pairs,
            head_pairs,
            head_dim,
            score_scale,
            outputs,
        )
        digests.append(seq_reduce_scatter(far_dkv, 1, chunk))
    attention, query_grad, own_dk, own_dv = outputs
    back_kv = passed_along(back_kv, "seq", -1)
    digest_dkv = jnp.concatenate(digests, 2) if chunks > 1 else digests[0]
    key_grad, value_grad = finalize(
        own_dk, own_dv, back_kv, digest_dkv, select, head_pairs, head_dim
    )
    return attention, query_grad, key_grad, value_grad


def solution(mesh):
    in_specs = (
        P("seq", "head"),
        P("seq", "head"),
        P("seq", "head"),
        P("head", None),
        P(("seq", "head"), None),
        P("head", None),
    )
    out_specs = (P("seq", "head"), P("seq", "head"), P("seq", "head"), P("seq", "head"))
    return jax.shard_map(
        on_device, mesh=mesh, in_specs=in_specs, out_specs=out_specs, check_vma=False
    )
```

```python
import functools

import jax
import jax.numpy as jnp
from jax import lax
from jax.experimental import pallas as pl
from jax.experimental.pallas import tpu as pltpu
from jax.sharding import PartitionSpec as P

WIN = 256
BLOCK = 128
SUMM = 32


NEG = -1e30


def passed_along(value, axis, steps):
    count = lax.axis_size(axis)
    first, last = (max(0, -steps), min(count, count - steps))
    return lax.ppermute(value, axis, [(source, source + steps) for source in range(first, last)])


def seq_reduce_scatter(parts, axis, rotate=0):
    count = lax.axis_size("seq")
    if count & (count - 1):
        return lax.psum_scatter(
            parts.astype(jnp.bfloat16), "seq", scatter_dimension=axis, tiled=True
        )
    me = lax.axis_index("seq")
    bits = count.bit_length() - 1
    chunk = parts.shape[axis] // count
    held = parts.reshape(parts.shape[:axis] + (2,) * bits + (chunk,) + parts.shape[axis + 1 :])
    if bits > 2:
        order = [0] + sorted(range(1, bits - 1), key=lambda b: (b - 1 - rotate) % (bits - 2)) + [bits - 1]
    else:
        order = list(range(bits))
    gone = []
    for bit in order:
        where = axis + bits - 1 - bit - sum(1 for done in gone if done > bit)
        gone.append(bit)
        mine = (me >> bit) & 1
        keep = lax.dynamic_index_in_dim(held, mine, where, keepdims=False)
        send = lax.dynamic_index_in_dim(held, 1 - mine, where, keepdims=False)
        arrived = lax.ppermute(
            send.astype(jnp.bfloat16), "seq", [(source, source ^ (1 << bit)) for source in range(count)]
        )
        held = keep + arrived.astype(jnp.float32)
    return held.astype(jnp.bfloat16)


def nt(left, right):
    return lax.dot_general(left, right, (((1,), (1,)), ((), ())), preferred_element_type=jnp.float32)


def tn(left, right):
    return lax.dot_general(left, right, (((0,), (0,)), ((), ())), preferred_element_type=jnp.float32)


def nn(left, right):
    return lax.dot_general(left, right, (((1,), (0,)), ((), ())), preferred_element_type=jnp.float32)


def two_part_attention(q, g, first, second, scale):
    (k_a, v_a, mask_a), (k_b, v_b, mask_b) = first, second
    s_a = jnp.where(mask_a, nt(q, k_a) * scale, NEG)
    s_b = jnp.where(mask_b, nt(q, k_b) * scale, NEG)
    row_max = jnp.maximum(s_a.max(-1, keepdims=True), s_b.max(-1, keepdims=True))
    w_a = jnp.exp(s_a - row_max)
    w_b = jnp.exp(s_b - row_max)
    row_sum = w_a.sum(-1, keepdims=True) + w_b.sum(-1, keepdims=True)
    mixed = nn(w_a.astype(jnp.bfloat16), v_a) + nn(w_b.astype(jnp.bfloat16), v_b)
    out = (mixed / row_sum).astype(jnp.bfloat16)
    delta = jnp.sum(g.astype(jnp.float32) * out.astype(jnp.float32), -1, keepdims=True)
    inverse = 1.0 / row_sum
    p_a = w_a * inverse
    p_b = w_b * inverse
    gs_a = (p_a * (nt(g, v_a) - delta)).astype(jnp.bfloat16)
    gs_b = (p_b * (nt(g, v_b) - delta)).astype(jnp.bfloat16)
    dq = ((nn(gs_a, k_a) + nn(gs_b, k_b)) * scale).astype(jnp.bfloat16)
    dk_a = tn(gs_a, q) * scale
    dk_b = tn(gs_b, q) * scale
    dv_a = tn(p_a.astype(jnp.bfloat16), g)
    dv_b = tn(p_b.astype(jnp.bfloat16), g)
    return out, dq, (dk_a, dv_a), (dk_b, dv_b)


def band_kernel(seq_ref, q_ref, k_ref, v_ref, g_ref, kvp_ref, out_ref, dq_ref, dk_ref, dv_ref, dkvp_ref, *, scale):
    rows = q_ref.shape[0]
    qi = lax.broadcasted_iota(jnp.int32, (rows, rows), 0)
    kj = lax.broadcasted_iota(jnp.int32, (rows, rows), 1)
    prev_mask = (kj > qi) & (seq_ref[0] > 0)
    own_mask = (kj <= qi) & (qi - kj < WIN)
    out, dq, (dkp, dvp), (dko, dvo) = two_part_attention(
        q_ref[...],
        g_ref[...],
        (kvp_ref[0], kvp_ref[1], prev_mask),
        (k_ref[...], v_ref[...], own_mask),
        scale,
    )
    out_ref[...] = out
    dq_ref[...] = dq
    dk_ref[...] = dko
    dv_ref[...] = dvo
    dkvp_ref[0] = dkp.astype(dkvp_ref.dtype)
    dkvp_ref[1] = dvp.astype(dkvp_ref.dtype)


def fixed_kernel(seq_ref, q_ref, k_ref, v_ref, g_ref, kf_ref, vf_ref, *refs, scale, unused):
    out_ref, dq_ref, dk_ref, dv_ref, dkvf_ref = refs[unused:]
    rows = q_ref.shape[0]
    far_rows = kf_ref.shape[0]
    start = seq_ref[0] * rows
    qi = lax.broadcasted_iota(jnp.int32, (rows, rows), 0)
    kj = lax.broadcasted_iota(jnp.int32, (rows, rows), 1)
    own_mask = (kj <= qi) & ((qi // BLOCK) == (kj // BLOCK))
    fq = lax.broadcasted_iota(jnp.int32, (rows, far_rows), 0)
    fr = lax.broadcasted_iota(jnp.int32, (rows, far_rows), 1)
    far_mask = (fr // SUMM) < ((start + fq) // BLOCK)
    out, dq, (dko, dvo), (dkf, dvf) = two_part_attention(
        q_ref[...],
        g_ref[...],
        (k_ref[...], v_ref[...], own_mask),
        (kf_ref[...], vf_ref[...], far_mask),
        scale,
    )
    out_ref[...] = out
    dq_ref[...] = dq
    dk_ref[...] = dko
    dv_ref[...] = dvo
    dkvf_ref[0] = dkf.astype(dkvf_ref.dtype)
    dkvf_ref[1] = dvf.astype(dkvf_ref.dtype)


def attention_cost(rows, keys, head_dim, heads):
    return pl.CostEstimate(
        flops=2 * rows * keys * head_dim * 7 * heads,
        transcendentals=3 * rows * keys * heads,
        bytes_accessed=(rows * 16 + keys * 6) * head_dim * heads,
    )


def band_attention(seq_index, q, k, v, g, kv_prev, head_pairs, head_dim, scale):
    rows = q.shape[0]
    block = pl.BlockSpec((rows, head_dim), lambda p, s: (0, 2 * p))
    narrow = pl.BlockSpec((2, rows, head_dim), lambda p, s: (0, 0, p))
    width = 2 * head_pairs * head_dim
    grid_spec = pltpu.PrefetchScalarGridSpec(
        num_scalar_prefetch=1,
        grid=(head_pairs,),
        in_specs=[block] * 4 + [narrow],
        out_specs=[block] * 4 + [narrow],
    )
    return pl.pallas_call(
        functools.partial(band_kernel, scale=scale),
        grid_spec=grid_spec,
        out_shape=[
            jax.ShapeDtypeStruct((rows, width), jnp.bfloat16),
            jax.ShapeDtypeStruct((rows, width), jnp.bfloat16),
            jax.ShapeDtypeStruct((rows, width), jnp.float32),
            jax.ShapeDtypeStruct((rows, width), jnp.float32),
            jax.ShapeDtypeStruct((2, rows, head_pairs * head_dim), jnp.bfloat16),
        ],
        compiler_params=pltpu.CompilerParams(vmem_limit_bytes=48 * 1024 * 1024),
        cost_estimate=attention_cost(rows, 2 * rows, head_dim, head_pairs),
    )(seq_index, q, k, v, g, kv_prev)


def fixed_attention(seq_index, q, k, v, g, far_kv, first_pair, pairs, head_pairs, head_dim, scale, earlier):
    rows = q.shape[0]
    far_rows = far_kv.shape[0]
    block = pl.BlockSpec((rows, head_dim), lambda p, s: (0, 2 * (first_pair + p) + 1))
    far_k_spec = pl.BlockSpec((far_rows, head_dim), lambda p, s: (0, first_pair + p))
    far_v_spec = pl.BlockSpec((far_rows, head_dim), lambda p, s: (0, head_pairs + first_pair + p))
    operands = [seq_index, q, k, v, g, far_kv, far_kv] + list(earlier)
    aliases = {7 + number: number for number in range(len(earlier))}
    grid_spec = pltpu.PrefetchScalarGridSpec(
        num_scalar_prefetch=1,
        grid=(pairs,),
        in_specs=[block] * 4 + [far_k_spec, far_v_spec]
        + [pl.BlockSpec(memory_space=pl.ANY)] * len(earlier),
        out_specs=[block] * 4 + [pl.BlockSpec((2, far_rows, head_dim), lambda p, s: (0, 0, p))],
    )
    return pl.pallas_call(
        functools.partial(fixed_kernel, scale=scale, unused=len(earlier)),
        grid_spec=grid_spec,
        out_shape=[jax.ShapeDtypeStruct(array.shape, array.dtype) for array in earlier]
        + [jax.ShapeDtypeStruct((2, far_rows, pairs * head_dim), jnp.bfloat16)],
        input_output_aliases=aliases,
        compiler_params=pltpu.CompilerParams(vmem_limit_bytes=48 * 1024 * 1024),
        cost_estimate=attention_cost(rows, rows + far_rows, head_dim, pairs),
    )(*operands)


def finalize_kernel(own_k_ref, own_v_ref, back_ref, digest_ref, select_ref, k_out, v_out):
    hd = back_ref.shape[2]
    pick = select_ref[0]
    for own_ref, side, out_ref in ((own_k_ref, 0, k_out), (own_v_ref, 1, v_out)):
        out_ref[:, :hd] = (own_ref[:, :hd] + back_ref[side].astype(jnp.float32)).astype(out_ref.dtype)
        summary = tn(pick, digest_ref[side])
        out_ref[:, hd:] = (own_ref[:, hd:] + summary).astype(out_ref.dtype)


def finalize(own_k, own_v, back_kv, digest, select, head_pairs, head_dim):
    rows = own_k.shape[0]
    digest_rows = digest.shape[1]
    wide = pl.BlockSpec((rows, 2 * head_dim), lambda p: (0, p))
    narrow = pl.BlockSpec((2, rows, head_dim), lambda p: (0, 0, p))
    return pl.pallas_call(
        finalize_kernel,
        grid=(head_pairs,),
        in_specs=[
            wide,
            wide,
            narrow,
            pl.BlockSpec((2, digest_rows, head_dim), lambda p: (0, 0, p)),
            pl.BlockSpec((1, digest_rows, rows), lambda p: (p, 0, 0)),
        ],
        out_specs=[wide, wide],
        out_shape=[jax.ShapeDtypeStruct(own_k.shape, jnp.bfloat16)] * 2,
        cost_estimate=pl.CostEstimate(
            flops=4 * rows * digest_rows * head_dim * head_pairs,
            transcendentals=0,
            bytes_accessed=rows * head_dim * head_pairs * 20,
        ),
    )(own_k, own_v, back_kv, digest, select)


def on_device(queries, keys, values, out_weight, cotangent, offsets):
    seq_rows = queries.shape[0]
    full_width = queries.shape[1]
    head_pairs = offsets.shape[0]
    head_dim = full_width // (2 * head_pairs)
    score_scale = head_dim ** (-0.5)
    assert seq_rows == WIN and seq_rows % BLOCK == 0
    seq_index = lax.axis_index("seq")
    split_k = keys.reshape(seq_rows, head_pairs, 2, head_dim)
    split_v = values.reshape(seq_rows, head_pairs, 2, head_dim)
    fixed_k = split_k[:, :, 1]
    fixed_v = split_v[:, :, 1]
    band_kv = jnp.stack([split_k[:, :, 0], split_v[:, :, 0]], 0).reshape(
        2, seq_rows, head_pairs * head_dim
    )
    prev_kv = passed_along(band_kv, "seq", 1)
    digest_count = seq_rows // BLOCK * SUMM
    offset_table = jnp.tile(offsets.T, (seq_rows // BLOCK, 1))
    digest_rows = (jnp.arange(digest_count, dtype=jnp.int32) // SUMM * BLOCK)[
        :, None
    ] + offset_table
    select = (
        digest_rows.T[:, :, None] == jnp.arange(seq_rows, dtype=jnp.int32)[None, None, :]
    ).astype(jnp.bfloat16)
    digest_k = jnp.einsum(
        "hjr,rhc->jhc", select, fixed_k, preferred_element_type=jnp.float32
    ).astype(jnp.bfloat16)
    digest_v = jnp.einsum(
        "hjr,rhc->jhc", select, fixed_v, preferred_element_type=jnp.float32
    ).astype(jnp.bfloat16)
    pair_width = head_pairs * head_dim
    far_kv = lax.all_gather(
        jnp.concatenate(
            [
                digest_k.reshape(digest_count, pair_width),
                digest_v.reshape(digest_count, pair_width),
            ],
            1,
        ),
        "seq",
        axis=0,
        tiled=True,
    )
    head_count = lax.axis_size("head")
    head_index = lax.axis_index("head")
    pieces = [cotangent] + [
        lax.ppermute(
            cotangent, "head", [(source, (source + shift) % head_count) for source in range(head_count)]
        )
        for shift in range(1, head_count)
    ]
    doubled = jnp.stack(pieces[::-1] + pieces[::-1], 0)
    gathered = lax.dynamic_slice_in_dim(doubled, head_count - 1 - head_index, head_count, 0)
    grad_out = lax.dot_general(
        gathered.reshape(seq_rows, cotangent.shape[1]),
        out_weight,
        (((1,), (1,)), ((), ())),
        preferred_element_type=jnp.float32,
    ).astype(jnp.bfloat16)
    seq_scalar = seq_index.reshape(1).astype(jnp.int32)
    attention, query_grad, own_dk, own_dv, back_kv = band_attention(
        seq_scalar, queries, keys, values, grad_out, prev_kv, head_pairs, head_dim, score_scale
    )
    chunks = 2 if head_pairs % 2 == 0 else 1
    pairs = head_pairs // chunks
    outputs = (attention, query_grad, own_dk, own_dv)
    digests = []
    for chunk in range(chunks):
        *outputs, far_dkv = fixed_attention(
            seq_scalar,
            queries,
            keys,
            values,
            grad_out,
            far_kv,
            chunk * pairs,
            pairs,
            head_pairs,
            head_dim,
            score_scale,
            outputs,
        )
        digests.append(seq_reduce_scatter(far_dkv, 1, chunk))
    attention, query_grad, own_dk, own_dv = outputs
    back_kv = passed_along(back_kv, "seq", -1)
    digest_dkv = jnp.concatenate(digests, 2) if chunks > 1 else digests[0]
    key_grad, value_grad = finalize(
        own_dk, own_dv, back_kv, digest_dkv, select, head_pairs, head_dim
    )
    return attention, query_grad, key_grad, value_grad


def solution(mesh):
    in_specs = (
        P("seq", "head"),
        P("seq", "head"),
        P("seq", "head"),
        P("head", None),
        P(("seq", "head"), None),
        P("head", None),
    )
    out_specs = (P("seq", "head"), P("seq", "head"), P("seq", "head"), P("seq", "head"))
    return jax.shard_map(
        on_device, mesh=mesh, in_specs=in_specs, out_specs=out_specs, check_vma=False
    )
```

```python
import functools

import jax
import jax.numpy as jnp
from jax import lax
from jax.experimental import pallas as pl
from jax.experimental.pallas import tpu as pltpu
from jax.sharding import PartitionSpec as P

WIN = 256
BLOCK = 128
SUMM = 32


NEG = -1e30


def passed_along(value, axis, steps):
    count = lax.axis_size(axis)
    first, last = (max(0, -steps), min(count, count - steps))
    return lax.ppermute(value, axis, [(source, source + steps) for source in range(first, last)])


def seq_reduce_scatter(parts, axis, rotate=0):
    count = lax.axis_size("seq")
    if count & (count - 1):
        return lax.psum_scatter(
            parts.astype(jnp.bfloat16), "seq", scatter_dimension=axis, tiled=True
        )
    me = lax.axis_index("seq")
    bits = count.bit_length() - 1
    chunk = parts.shape[axis] // count
    held = parts.reshape(parts.shape[:axis] + (2,) * bits + (chunk,) + parts.shape[axis + 1 :])
    if bits > 2:
        order = [0] + sorted(range(1, bits - 1), key=lambda b: (b - 1 - rotate) % (bits - 2)) + [bits - 1]
    else:
        order = list(range(bits))
    gone = []
    for bit in order:
        where = axis + bits - 1 - bit - sum(1 for done in gone if done > bit)
        gone.append(bit)
        mine = (me >> bit) & 1
        keep = lax.dynamic_index_in_dim(held, mine, where, keepdims=False)
        send = lax.dynamic_index_in_dim(held, 1 - mine, where, keepdims=False)
        arrived = lax.ppermute(
            send.astype(jnp.bfloat16), "seq", [(source, source ^ (1 << bit)) for source in range(count)]
        )
        held = keep + arrived.astype(jnp.float32)
    return held.astype(jnp.bfloat16)


def nt(left, right):
    return lax.dot_general(left, right, (((1,), (1,)), ((), ())), preferred_element_type=jnp.float32)


def tn(left, right):
    return lax.dot_general(left, right, (((0,), (0,)), ((), ())), preferred_element_type=jnp.float32)


def nn(left, right):
    return lax.dot_general(left, right, (((1,), (0,)), ((), ())), preferred_element_type=jnp.float32)


def two_part_attention(q, g, first, second, scale):
    (k_a, v_a, mask_a), (k_b, v_b, mask_b) = first, second
    s_a = jnp.where(mask_a, nt(q, k_a) * scale, NEG)
    s_b = jnp.where(mask_b, nt(q, k_b) * scale, NEG)
    row_max = jnp.maximum(s_a.max(-1, keepdims=True), s_b.max(-1, keepdims=True))
    w_a = jnp.exp(s_a - row_max)
    w_b = jnp.exp(s_b - row_max)
    row_sum = w_a.sum(-1, keepdims=True) + w_b.sum(-1, keepdims=True)
    mixed = nn(w_a.astype(jnp.bfloat16), v_a) + nn(w_b.astype(jnp.bfloat16), v_b)
    out = (mixed / row_sum).astype(jnp.bfloat16)
    delta = jnp.sum(g.astype(jnp.float32) * out.astype(jnp.float32), -1, keepdims=True)
    inverse = 1.0 / row_sum
    p_a = w_a * inverse
    p_b = w_b * inverse
    gs_a = (p_a * (nt(g, v_a) - delta)).astype(jnp.bfloat16)
    gs_b = (p_b * (nt(g, v_b) - delta)).astype(jnp.bfloat16)
    dq = ((nn(gs_a, k_a) + nn(gs_b, k_b)) * scale).astype(jnp.bfloat16)
    dk_a = tn(gs_a, q) * scale
    dk_b = tn(gs_b, q) * scale
    dv_a = tn(p_a.astype(jnp.bfloat16), g)
    dv_b = tn(p_b.astype(jnp.bfloat16), g)
    return out, dq, (dk_a, dv_a), (dk_b, dv_b)


def band_kernel(seq_ref, q_ref, k_ref, v_ref, g_ref, kvp_ref, out_ref, dq_ref, dk_ref, dv_ref, dkvp_ref, *, scale):
    rows = q_ref.shape[0]
    qi = lax.broadcasted_iota(jnp.int32, (rows, rows), 0)
    kj = lax.broadcasted_iota(jnp.int32, (rows, rows), 1)
    prev_mask = (kj > qi) & (seq_ref[0] > 0)
    own_mask = (kj <= qi) & (qi - kj < WIN)
    out, dq, (dkp, dvp), (dko, dvo) = two_part_attention(
        q_ref[...],
        g_ref[...],
        (kvp_ref[0], kvp_ref[1], prev_mask),
        (k_ref[...], v_ref[...], own_mask),
        scale,
    )
    out_ref[...] = out
    dq_ref[...] = dq
    dk_ref[...] = dko
    dv_ref[...] = dvo
    dkvp_ref[0] = dkp.astype(dkvp_ref.dtype)
    dkvp_ref[1] = dvp.astype(dkvp_ref.dtype)


def fixed_kernel(seq_ref, q_ref, k_ref, v_ref, g_ref, kf_ref, vf_ref, *refs, scale, unused):
    out_ref, dq_ref, dk_ref, dv_ref, dkvf_ref = refs[unused:]
    rows = q_ref.shape[0]
    far_rows = kf_ref.shape[0]
    start = seq_ref[0] * rows
    qi = lax.broadcasted_iota(jnp.int32, (rows, rows), 0)
    kj = lax.broadcasted_iota(jnp.int32, (rows, rows), 1)
    own_mask = (kj <= qi) & ((qi // BLOCK) == (kj // BLOCK))
    fq = lax.broadcasted_iota(jnp.int32, (rows, far_rows), 0)
    fr = lax.broadcasted_iota(jnp.int32, (rows, far_rows), 1)
    far_mask = (fr // SUMM) < ((start + fq) // BLOCK)
    out, dq, (dko, dvo), (dkf, dvf) = two_part_attention(
        q_ref[...],
        g_ref[...],
        (k_ref[...], v_ref[...], own_mask),
        (kf_ref[...], vf_ref[...], far_mask),
        scale,
    )
    out_ref[...] = out
    dq_ref[...] = dq
    dk_ref[...] = dko
    dv_ref[...] = dvo
    dkvf_ref[0] = dkf.astype(dkvf_ref.dtype)
    dkvf_ref[1] = dvf.astype(dkvf_ref.dtype)


def attention_cost(rows, keys, head_dim, heads):
    return pl.CostEstimate(
        flops=2 * rows * keys * head_dim * 7 * heads,
        transcendentals=3 * rows * keys * heads,
        bytes_accessed=(rows * 16 + keys * 6) * head_dim * heads,
    )


def band_attention(seq_index, q, k, v, g, kv_prev, head_pairs, head_dim, scale):
    rows = q.shape[0]
    block = pl.BlockSpec((rows, head_dim), lambda p, s: (0, 2 * p))
    narrow = pl.BlockSpec((2, rows, head_dim), lambda p, s: (0, 0, p))
    width = 2 * head_pairs * head_dim
    grid_spec = pltpu.PrefetchScalarGridSpec(
        num_scalar_prefetch=1,
        grid=(head_pairs,),
        in_specs=[block] * 4 + [narrow],
        out_specs=[block] * 4 + [narrow],
    )
    return pl.pallas_call(
        functools.partial(band_kernel, scale=scale),
        grid_spec=grid_spec,
        out_shape=[
            jax.ShapeDtypeStruct((rows, width), jnp.bfloat16),
            jax.ShapeDtypeStruct((rows, width), jnp.bfloat16),
            jax.ShapeDtypeStruct((rows, width), jnp.float32),
            jax.ShapeDtypeStruct((rows, width), jnp.float32),
            jax.ShapeDtypeStruct((2, rows, head_pairs * head_dim), jnp.bfloat16),
        ],
        compiler_params=pltpu.CompilerParams(vmem_limit_bytes=48 * 1024 * 1024),
        cost_estimate=attention_cost(rows, 2 * rows, head_dim, head_pairs),
    )(seq_index, q, k, v, g, kv_prev)


def fixed_attention(seq_index, q, k, v, g, far_kv, first_pair, pairs, head_pairs, head_dim, scale, earlier):
    rows = q.shape[0]
    far_rows = far_kv.shape[0]
    block = pl.BlockSpec((rows, head_dim), lambda p, s: (0, 2 * (first_pair + p) + 1))
    far_k_spec = pl.BlockSpec((far_rows, head_dim), lambda p, s: (0, first_pair + p))
    far_v_spec = pl.BlockSpec((far_rows, head_dim), lambda p, s: (0, head_pairs + first_pair + p))
    operands = [seq_index, q, k, v, g, far_kv, far_kv] + list(earlier)
    aliases = {7 + number: number for number in range(len(earlier))}
    grid_spec = pltpu.PrefetchScalarGridSpec(
        num_scalar_prefetch=1,
        grid=(pairs,),
        in_specs=[block] * 4 + [far_k_spec, far_v_spec]
        + [pl.BlockSpec(memory_space=pl.ANY)] * len(earlier),
        out_specs=[block] * 4 + [pl.BlockSpec((2, far_rows, head_dim), lambda p, s: (0, 0, p))],
    )
    return pl.pallas_call(
        functools.partial(fixed_kernel, scale=scale, unused=len(earlier)),
        grid_spec=grid_spec,
        out_shape=[jax.ShapeDtypeStruct(array.shape, array.dtype) for array in earlier]
        + [jax.ShapeDtypeStruct((2, far_rows, pairs * head_dim), jnp.bfloat16)],
        input_output_aliases=aliases,
        compiler_params=pltpu.CompilerParams(vmem_limit_bytes=48 * 1024 * 1024),
        cost_estimate=attention_cost(rows, rows + far_rows, head_dim, pairs),
    )(*operands)


def finalize_kernel(own_k_ref, own_v_ref, back_ref, digest_ref, select_ref, k_out, v_out):
    hd = back_ref.shape[2]
    pick = select_ref[0]
    for own_ref, side, out_ref in ((own_k_ref, 0, k_out), (own_v_ref, 1, v_out)):
        out_ref[:, :hd] = (own_ref[:, :hd] + back_ref[side].astype(jnp.float32)).astype(out_ref.dtype)
        summary = tn(pick, digest_ref[side])
        out_ref[:, hd:] = (own_ref[:, hd:] + summary).astype(out_ref.dtype)


def finalize(own_k, own_v, back_kv, digest, select, head_pairs, head_dim):
    rows = own_k.shape[0]
    digest_rows = digest.shape[1]
    wide = pl.BlockSpec((rows, 2 * head_dim), lambda p: (0, p))
    narrow = pl.BlockSpec((2, rows, head_dim), lambda p: (0, 0, p))
    return pl.pallas_call(
        finalize_kernel,
        grid=(head_pairs,),
        in_specs=[
            wide,
            wide,
            narrow,
            pl.BlockSpec((2, digest_rows, head_dim), lambda p: (0, 0, p)),
            pl.BlockSpec((1, digest_rows, rows), lambda p: (p, 0, 0)),
        ],
        out_specs=[wide, wide],
        out_shape=[jax.ShapeDtypeStruct(own_k.shape, jnp.bfloat16)] * 2,
        cost_estimate=pl.CostEstimate(
            flops=4 * rows * digest_rows * head_dim * head_pairs,
            transcendentals=0,
            bytes_accessed=rows * head_dim * head_pairs * 20,
        ),
    )(own_k, own_v, back_kv, digest, select)


def on_device(queries, keys, values, out_weight, cotangent, offsets):
    seq_rows = queries.shape[0]
    full_width = queries.shape[1]
    head_pairs = offsets.shape[0]
    head_dim = full_width // (2 * head_pairs)
    score_scale = head_dim ** (-0.5)
    assert seq_rows == WIN and seq_rows % BLOCK == 0
    seq_index = lax.axis_index("seq")
    split_k = keys.reshape(seq_rows, head_pairs, 2, head_dim)
    split_v = values.reshape(seq_rows, head_pairs, 2, head_dim)
    fixed_k = split_k[:, :, 1]
    fixed_v = split_v[:, :, 1]
    band_kv = jnp.stack([split_k[:, :, 0], split_v[:, :, 0]], 0).reshape(
        2, seq_rows, head_pairs * head_dim
    )
    prev_kv = passed_along(band_kv, "seq", 1)
    digest_count = seq_rows // BLOCK * SUMM
    offset_table = jnp.tile(offsets.T, (seq_rows // BLOCK, 1))
    digest_rows = (jnp.arange(digest_count, dtype=jnp.int32) // SUMM * BLOCK)[
        :, None
    ] + offset_table
    select = (
        digest_rows.T[:, :, None] == jnp.arange(seq_rows, dtype=jnp.int32)[None, None, :]
    ).astype(jnp.bfloat16)
    digest_k = jnp.einsum(
        "hjr,rhc->jhc", select, fixed_k, preferred_element_type=jnp.float32
    ).astype(jnp.bfloat16)
    digest_v = jnp.einsum(
        "hjr,rhc->jhc", select, fixed_v, preferred_element_type=jnp.float32
    ).astype(jnp.bfloat16)
    pair_width = head_pairs * head_dim
    far_kv = lax.all_gather(
        jnp.concatenate(
            [
                digest_k.reshape(digest_count, pair_width),
                digest_v.reshape(digest_count, pair_width),
            ],
            1,
        ),
        "seq",
        axis=0,
        tiled=True,
    )
    head_count = lax.axis_size("head")
    head_index = lax.axis_index("head")
    pieces = [cotangent] + [
        lax.ppermute(
            cotangent, "head", [(source, (source + shift) % head_count) for source in range(head_count)]
        )
        for shift in range(1, head_count)
    ]
    doubled = jnp.stack(pieces[::-1] + pieces[::-1], 0)
    gathered = lax.dynamic_slice_in_dim(doubled, head_count - 1 - head_index, head_count, 0)
    grad_out = lax.dot_general(
        gathered.reshape(seq_rows, cotangent.shape[1]),
        out_weight,
        (((1,), (1,)), ((), ())),
        preferred_element_type=jnp.float32,
    ).astype(jnp.bfloat16)
    seq_scalar = seq_index.reshape(1).astype(jnp.int32)
    attention, query_grad, own_dk, own_dv, back_kv = band_attention(
        seq_scalar, queries, keys, values, grad_out, prev_kv, head_pairs, head_dim, score_scale
    )
    chunks = 8 if head_pairs % 8 == 0 else (4 if head_pairs % 4 == 0 else (2 if head_pairs % 2 == 0 else 1))
    pairs = head_pairs // chunks
    outputs = (attention, query_grad, own_dk, own_dv)
    digests = []
    for chunk in range(chunks):
        *outputs, far_dkv = fixed_attention(
            seq_scalar,
            queries,
            keys,
            values,
            grad_out,
            far_kv,
            chunk * pairs,
            pairs,
            head_pairs,
            head_dim,
            score_scale,
            outputs,
        )
        digests.append(seq_reduce_scatter(far_dkv, 1, chunk))
    attention, query_grad, own_dk, own_dv = outputs
    back_kv = passed_along(back_kv, "seq", -1)
    digest_dkv = jnp.concatenate(digests, 2) if chunks > 1 else digests[0]
    key_grad, value_grad = finalize(
        own_dk, own_dv, back_kv, digest_dkv, select, head_pairs, head_dim
    )
    return attention, query_grad, key_grad, value_grad


def solution(mesh):
    in_specs = (
        P("seq", "head"),
        P("seq", "head"),
        P("seq", "head"),
        P("head", None),
        P(("seq", "head"), None),
        P("head", None),
    )
    out_specs = (P("seq", "head"), P("seq", "head"), P("seq", "head"), P("seq", "head"))
    return jax.shard_map(
        on_device, mesh=mesh, in_specs=in_specs, out_specs=out_specs, check_vma=False
    )
```

```python
import functools

import jax
import jax.numpy as jnp
from jax import lax
from jax.experimental import pallas as pl
from jax.experimental.pallas import tpu as pltpu
from jax.sharding import PartitionSpec as P

WIN = 256
BLOCK = 128
SUMM = 32


NEG = -1e30


def passed_along(value, axis, steps):
    count = lax.axis_size(axis)
    first, last = (max(0, -steps), min(count, count - steps))
    return lax.ppermute(value, axis, [(source, source + steps) for source in range(first, last)])


def seq_reduce_scatter(parts, axis, rotate=0):
    count = lax.axis_size("seq")
    if count & (count - 1):
        return lax.psum_scatter(
            parts.astype(jnp.bfloat16), "seq", scatter_dimension=axis, tiled=True
        )
    me = lax.axis_index("seq")
    bits = count.bit_length() - 1
    chunk = parts.shape[axis] // count
    held = parts.reshape(parts.shape[:axis] + (2,) * bits + (chunk,) + parts.shape[axis + 1 :])
    if bits > 2:
        order = [0] + sorted(range(1, bits - 1), key=lambda b: (b - 1 - rotate) % (bits - 2)) + [bits - 1]
    else:
        order = list(range(bits))
    gone = []
    for bit in order:
        where = axis + bits - 1 - bit - sum(1 for done in gone if done > bit)
        gone.append(bit)
        mine = (me >> bit) & 1
        keep = lax.dynamic_index_in_dim(held, mine, where, keepdims=False)
        send = lax.dynamic_index_in_dim(held, 1 - mine, where, keepdims=False)
        arrived = lax.ppermute(
            send.astype(jnp.bfloat16), "seq", [(source, source ^ (1 << bit)) for source in range(count)]
        )
        held = keep + arrived.astype(jnp.float32)
    return held.astype(jnp.bfloat16)


def nt(left, right):
    return lax.dot_general(left, right, (((1,), (1,)), ((), ())), preferred_element_type=jnp.float32)


def tn(left, right):
    return lax.dot_general(left, right, (((0,), (0,)), ((), ())), preferred_element_type=jnp.float32)


def nn(left, right):
    return lax.dot_general(left, right, (((1,), (0,)), ((), ())), preferred_element_type=jnp.float32)


def two_part_attention(q, g, first, second, scale):
    (k_a, v_a, mask_a), (k_b, v_b, mask_b) = first, second
    s_a = jnp.where(mask_a, nt(q, k_a) * scale, NEG)
    s_b = jnp.where(mask_b, nt(q, k_b) * scale, NEG)
    row_max = jnp.maximum(s_a.max(-1, keepdims=True), s_b.max(-1, keepdims=True))
    w_a = jnp.exp(s_a - row_max)
    w_b = jnp.exp(s_b - row_max)
    row_sum = w_a.sum(-1, keepdims=True) + w_b.sum(-1, keepdims=True)
    mixed = nn(w_a.astype(jnp.bfloat16), v_a) + nn(w_b.astype(jnp.bfloat16), v_b)
    out = (mixed / row_sum).astype(jnp.bfloat16)
    delta = jnp.sum(g.astype(jnp.float32) * out.astype(jnp.float32), -1, keepdims=True)
    inverse = 1.0 / row_sum
    p_a = w_a * inverse
    p_b = w_b * inverse
    gs_a = (p_a * (nt(g, v_a) - delta)).astype(jnp.bfloat16)
    gs_b = (p_b * (nt(g, v_b) - delta)).astype(jnp.bfloat16)
    dq = ((nn(gs_a, k_a) + nn(gs_b, k_b)) * scale).astype(jnp.bfloat16)
    dk_a = tn(gs_a, q) * scale
    dk_b = tn(gs_b, q) * scale
    dv_a = tn(p_a.astype(jnp.bfloat16), g)
    dv_b = tn(p_b.astype(jnp.bfloat16), g)
    return out, dq, (dk_a, dv_a), (dk_b, dv_b)


def band_kernel(seq_ref, q_ref, k_ref, v_ref, g_ref, kvp_ref, out_ref, dq_ref, dk_ref, dv_ref, dkvp_ref, *, scale):
    rows = q_ref.shape[0]
    qi = lax.broadcasted_iota(jnp.int32, (rows, rows), 0)
    kj = lax.broadcasted_iota(jnp.int32, (rows, rows), 1)
    prev_mask = (kj > qi) & (seq_ref[0] > 0)
    own_mask = (kj <= qi) & (qi - kj < WIN)
    out, dq, (dkp, dvp), (dko, dvo) = two_part_attention(
        q_ref[...],
        g_ref[...],
        (kvp_ref[0], kvp_ref[1], prev_mask),
        (k_ref[...], v_ref[...], own_mask),
        scale,
    )
    out_ref[...] = out
    dq_ref[...] = dq
    dk_ref[...] = dko
    dv_ref[...] = dvo
    dkvp_ref[0] = dkp.astype(dkvp_ref.dtype)
    dkvp_ref[1] = dvp.astype(dkvp_ref.dtype)


def fixed_kernel(seq_ref, q_ref, k_ref, v_ref, g_ref, kf_ref, vf_ref, *refs, scale, unused):
    out_ref, dq_ref, dk_ref, dv_ref, dkvf_ref = refs[unused:]
    rows = q_ref.shape[0]
    far_rows = kf_ref.shape[0]
    start = seq_ref[0] * rows
    qi = lax.broadcasted_iota(jnp.int32, (rows, rows), 0)
    kj = lax.broadcasted_iota(jnp.int32, (rows, rows), 1)
    own_mask = (kj <= qi) & ((qi // BLOCK) == (kj // BLOCK))
    fq = lax.broadcasted_iota(jnp.int32, (rows, far_rows), 0)
    fr = lax.broadcasted_iota(jnp.int32, (rows, far_rows), 1)
    far_mask = (fr // SUMM) < ((start + fq) // BLOCK)
    out, dq, (dko, dvo), (dkf, dvf) = two_part_attention(
        q_ref[...],
        g_ref[...],
        (k_ref[...], v_ref[...], own_mask),
        (kf_ref[...], vf_ref[...], far_mask),
        scale,
    )
    out_ref[...] = out
    dq_ref[...] = dq
    dk_ref[...] = dko
    dv_ref[...] = dvo
    dkvf_ref[0] = dkf.astype(dkvf_ref.dtype)
    dkvf_ref[1] = dvf.astype(dkvf_ref.dtype)


def attention_cost(rows, keys, head_dim, heads):
    return pl.CostEstimate(
        flops=2 * rows * keys * head_dim * 7 * heads,
        transcendentals=3 * rows * keys * heads,
        bytes_accessed=(rows * 16 + keys * 6) * head_dim * heads,
    )


def band_attention(seq_index, q, k, v, g, kv_prev, head_pairs, head_dim, scale):
    rows = q.shape[0]
    block = pl.BlockSpec((rows, head_dim), lambda p, s: (0, 2 * p))
    narrow = pl.BlockSpec((2, rows, head_dim), lambda p, s: (0, 0, p))
    width = 2 * head_pairs * head_dim
    grid_spec = pltpu.PrefetchScalarGridSpec(
        num_scalar_prefetch=1,
        grid=(head_pairs,),
        in_specs=[block] * 4 + [narrow],
        out_specs=[block] * 4 + [narrow],
    )
    return pl.pallas_call(
        functools.partial(band_kernel, scale=scale),
        grid_spec=grid_spec,
        out_shape=[
            jax.ShapeDtypeStruct((rows, width), jnp.bfloat16),
            jax.ShapeDtypeStruct((rows, width), jnp.bfloat16),
            jax.ShapeDtypeStruct((rows, width), jnp.float32),
            jax.ShapeDtypeStruct((rows, width), jnp.float32),
            jax.ShapeDtypeStruct((2, rows, head_pairs * head_dim), jnp.bfloat16),
        ],
        compiler_params=pltpu.CompilerParams(vmem_limit_bytes=48 * 1024 * 1024),
        cost_estimate=attention_cost(rows, 2 * rows, head_dim, head_pairs),
    )(seq_index, q, k, v, g, kv_prev)


def fixed_attention(seq_index, q, k, v, g, far_kv, first_pair, pairs, head_pairs, head_dim, scale, earlier):
    rows = q.shape[0]
    far_rows = far_kv.shape[0]
    block = pl.BlockSpec((rows, head_dim), lambda p, s: (0, 2 * (first_pair + p) + 1))
    far_k_spec = pl.BlockSpec((far_rows, head_dim), lambda p, s: (0, first_pair + p))
    far_v_spec = pl.BlockSpec((far_rows, head_dim), lambda p, s: (0, head_pairs + first_pair + p))
    operands = [seq_index, q, k, v, g, far_kv, far_kv] + list(earlier)
    aliases = {7 + number: number for number in range(len(earlier))}
    grid_spec = pltpu.PrefetchScalarGridSpec(
        num_scalar_prefetch=1,
        grid=(pairs,),
        in_specs=[block] * 4 + [far_k_spec, far_v_spec]
        + [pl.BlockSpec(memory_space=pl.ANY)] * len(earlier),
        out_specs=[block] * 4 + [pl.BlockSpec((2, far_rows, head_dim), lambda p, s: (0, 0, p))],
    )
    return pl.pallas_call(
        functools.partial(fixed_kernel, scale=scale, unused=len(earlier)),
        grid_spec=grid_spec,
        out_shape=[jax.ShapeDtypeStruct(array.shape, array.dtype) for array in earlier]
        + [jax.ShapeDtypeStruct((2, far_rows, pairs * head_dim), jnp.bfloat16)],
        input_output_aliases=aliases,
        compiler_params=pltpu.CompilerParams(vmem_limit_bytes=48 * 1024 * 1024),
        cost_estimate=attention_cost(rows, rows + far_rows, head_dim, pairs),
    )(*operands)


def finalize_kernel(own_k_ref, own_v_ref, back_ref, digest_ref, select_ref, k_out, v_out):
    hd = back_ref.shape[2]
    pick = select_ref[0]
    for own_ref, side, out_ref in ((own_k_ref, 0, k_out), (own_v_ref, 1, v_out)):
        out_ref[:, :hd] = (own_ref[:, :hd] + back_ref[side].astype(jnp.float32)).astype(out_ref.dtype)
        summary = tn(pick, digest_ref[side])
        out_ref[:, hd:] = (own_ref[:, hd:] + summary).astype(out_ref.dtype)


def finalize(own_k, own_v, back_kv, digest, select, head_pairs, head_dim):
    rows = own_k.shape[0]
    digest_rows = digest.shape[1]
    wide = pl.BlockSpec((rows, 2 * head_dim), lambda p: (0, p))
    narrow = pl.BlockSpec((2, rows, head_dim), lambda p: (0, 0, p))
    return pl.pallas_call(
        finalize_kernel,
        grid=(head_pairs,),
        in_specs=[
            wide,
            wide,
            narrow,
            pl.BlockSpec((2, digest_rows, head_dim), lambda p: (0, 0, p)),
            pl.BlockSpec((1, digest_rows, rows), lambda p: (p, 0, 0)),
        ],
        out_specs=[wide, wide],
        out_shape=[jax.ShapeDtypeStruct(own_k.shape, jnp.bfloat16)] * 2,
        cost_estimate=pl.CostEstimate(
            flops=4 * rows * digest_rows * head_dim * head_pairs,
            transcendentals=0,
            bytes_accessed=rows * head_dim * head_pairs * 20,
        ),
    )(own_k, own_v, back_kv, digest, select)


def on_device(queries, keys, values, out_weight, cotangent, offsets):
    seq_rows = queries.shape[0]
    full_width = queries.shape[1]
    head_pairs = offsets.shape[0]
    head_dim = full_width // (2 * head_pairs)
    score_scale = head_dim ** (-0.5)
    assert seq_rows == WIN and seq_rows % BLOCK == 0
    seq_index = lax.axis_index("seq")
    split_k = keys.reshape(seq_rows, head_pairs, 2, head_dim)
    split_v = values.reshape(seq_rows, head_pairs, 2, head_dim)
    fixed_k = split_k[:, :, 1]
    fixed_v = split_v[:, :, 1]
    band_kv = jnp.stack([split_k[:, :, 0], split_v[:, :, 0]], 0).reshape(
        2, seq_rows, head_pairs * head_dim
    )
    prev_kv = passed_along(band_kv, "seq", 1)
    digest_count = seq_rows // BLOCK * SUMM
    offset_table = jnp.tile(offsets.T, (seq_rows // BLOCK, 1))
    digest_rows = (jnp.arange(digest_count, dtype=jnp.int32) // SUMM * BLOCK)[
        :, None
    ] + offset_table
    select = (
        digest_rows.T[:, :, None] == jnp.arange(seq_rows, dtype=jnp.int32)[None, None, :]
    ).astype(jnp.bfloat16)
    fixed_kv = jnp.stack([fixed_k, fixed_v], 1)
    digest_kv = jnp.einsum(
        "hjr,rthc->jthc", select, fixed_kv, preferred_element_type=jnp.float32
    ).astype(jnp.bfloat16)
    far_kv = lax.all_gather(
        digest_kv.reshape(digest_count, 2 * head_pairs * head_dim), "seq", axis=0, tiled=True
    )
    head_count = lax.axis_size("head")
    head_index = lax.axis_index("head")
    pieces = [cotangent] + [
        lax.ppermute(
            cotangent, "head", [(source, (source + shift) % head_count) for source in range(head_count)]
        )
        for shift in range(1, head_count)
    ]
    doubled = jnp.stack(pieces[::-1] + pieces[::-1], 0)
    gathered = lax.dynamic_slice_in_dim(doubled, head_count - 1 - head_index, head_count, 0)
    grad_out = lax.dot_general(
        gathered.reshape(seq_rows, cotangent.shape[1]),
        out_weight,
        (((1,), (1,)), ((), ())),
        preferred_element_type=jnp.float32,
    ).astype(jnp.bfloat16)
    seq_scalar = seq_index.reshape(1).astype(jnp.int32)
    attention, query_grad, own_dk, own_dv, back_kv = band_attention(
        seq_scalar, queries, keys, values, grad_out, prev_kv, head_pairs, head_dim, score_scale
    )
    chunks = 4 if head_pairs % 4 == 0 else (2 if head_pairs % 2 == 0 else 1)
    pairs = head_pairs // chunks
    outputs = (attention, query_grad, own_dk, own_dv)
    digests = []
    for chunk in range(chunks):
        *outputs, far_dkv = fixed_attention(
            seq_scalar,
            queries,
            keys,
            values,
            grad_out,
            far_kv,
            chunk * pairs,
            pairs,
            head_pairs,
            head_dim,
            score_scale,
            outputs,
        )
        digests.append(seq_reduce_scatter(far_dkv, 1, chunk))
    attention, query_grad, own_dk, own_dv = outputs
    back_kv = passed_along(back_kv, "seq", -1)
    digest_dkv = jnp.concatenate(digests, 2) if chunks > 1 else digests[0]
    key_grad, value_grad = finalize(
        own_dk, own_dv, back_kv, digest_dkv, select, head_pairs, head_dim
    )
    return attention, query_grad, key_grad, value_grad


def solution(mesh):
    in_specs = (
        P("seq", "head"),
        P("seq", "head"),
        P("seq", "head"),
        P("head", None),
        P(("seq", "head"), None),
        P("head", None),
    )
    out_specs = (P("seq", "head"), P("seq", "head"), P("seq", "head"), P("seq", "head"))
    return jax.shard_map(
        on_device, mesh=mesh, in_specs=in_specs, out_specs=out_specs, check_vma=False
    )
```
